32 devices in a mesh: seq: 4 (over z), tp: 4 (over y, x), dp: 2 (over core).
Axes of the slice: x: 2, y: 2, z: 4, core: 2. Of those that a mesh axis runs over, the one named last changes fastest.
Arguments:
- hidden_states: bfloat16 [2048, 7168], P(('dp', 'seq'), 'tp'), parts along dimension 0, may hold values from -120 to 120
- input_gain: float32 [7168], P('tp'), may hold values from 0.1 to 1.9
- query_down: bfloat16 [7168, 1536], P('tp', 'seq'), may hold values from -0.0625 to 0.0625
- memory_down: bfloat16 [7168, 576], P('tp', 'seq'), may hold values from -0.0625 to 0.0625
- query_gain: float32 [1536], replicated, may hold values from 0.1 to 1.9
- memory_gain: float32 [512], replicated, may hold values from 0.1 to 1.9
- query_up: bfloat16 [1536, 12288], P('seq', 'tp'), may hold values from -16 to 16
- key_up: bfloat16 [512, 8192], P('seq', 'tp'), may hold values from -0.25 to 0.25
- value_up: bfloat16 [512, 8192], P('seq', 'tp'), may hold values from -0.25 to 0.25
- segment_ids: int32 [2048], P(('dp', 'seq')), parts along dimension 0, may hold values from 0 to 11, never falling along the last dimension, each value on 1 to 256 neighbouring positions
Outputs:
- attended: bfloat16 [2048, 8192], P(('dp', 'seq'), 'tp'), parts along dimension 0
The draws below stay inside these ranges and needn't reach their ends.
There are 2 independent parts, one for each index of `dp`. The reference program is written for one: setup_inputs(seed, part) draws one part's arguments, and reference() takes and returns one part's arrays. A program takes and returns all parts, laid end to end along the dimension named above; an argument that names none is the same for every part. Nothing has to cross between parts.
Inputs may be any that keep to these rules, and one draw needn't show every extreme that they name: `segment_ids`: ids never fall along the group; each of the 12 documents has 1 to 256 tokens and one has exactly 256.
All inputs are finite; a program needn't handle non-finite values.
Results may differ from the reference program's by a relative error of at most 0.0065.
The reference program's roundings to bfloat16 on the way (of `normed`, `query` and `weights`) count: a program that leaves them out, or rounds other values in their place, can miss the bound.
Values may be sent and summed in bfloat16 or wider, within the bound.
No kernel may reach another device: no remote copies, remote signals or barrier semaphores. Data moves between devices by JAX's collectives and lax.ppermute only.
A program may use at most 128 MiB of HBM per device.

```python
import math
import jax
import jax.numpy as jnp
import numpy as np
from jax import lax

D = 7168
HEADS = 64
QRANK = 1536
KVRANK = 512
NOPE = 128
ROPE = 64
VDIM = 128
DOCS = 12
TOKENS = 1024
DOC_MOST = 256


def draw_hidden_states(key, part):
    row_key, column_key, base_key = jax.random.split(key, 3)
    row_scale = jnp.exp(jax.random.uniform(row_key, (TOKENS, 1), dtype=jnp.float32) * jnp.log(10.0))
    column_scale = jnp.exp(jax.random.uniform(column_key, (1, D), dtype=jnp.float32, minval=-1.0, maxval=1.0) * jnp.log(3.0))
    base = jnp.clip(jax.random.normal(base_key, (TOKENS, D), dtype=jnp.float32), -4.0, 4.0)
    return (base * row_scale * column_scale).astype(jnp.bfloat16)


def draw_query_up(key, part):
    scale_key, base_key = jax.random.split(key, 2)
    head_scale = jnp.exp(jax.random.uniform(scale_key, (HEADS, 1), dtype=jnp.float32) * jnp.log(4.0))
    base = jnp.clip(jax.random.normal(base_key, (QRANK, HEADS * (NOPE + ROPE)), dtype=jnp.float32), -4.0, 4.0)
    column_scale = jnp.broadcast_to(head_scale, (HEADS, NOPE + ROPE)).reshape(1, HEADS * (NOPE + ROPE))
    return (base * column_scale / jnp.sqrt(jnp.float32(QRANK))).astype(jnp.bfloat16)


def levels(stream_key, extent, pieces, low, high):
    gain, own = 1.0, jax.random.fold_in(stream_key, 6)
    for dim, blocks in pieces:
        draws = jnp.exp(jax.random.uniform(jax.random.fold_in(own, dim), (blocks,), jnp.float32, low / len(pieces), high / len(pieces)))
        gain = gain * jnp.repeat(draws, extent[dim] // blocks).reshape([-1 if axis == dim else 1 for axis in range(len(extent))])
    return gain


def profile(number_of, total, limit, skew):
    weights = [(1 << 20) // math.isqrt(grade ** skew) + 1 for grade in range(2, number_of + 1)]
    surplus, counts = total - limit - (number_of - 1), [1] * (number_of - 1)
    while surplus > 0:
        movable = [i for i in range(number_of - 1) if counts[i] < limit]
        mass, budget = sum([weights[i] for i in movable]), surplus
        for i in movable:
            extra = min(limit - counts[i], max(1, budget * weights[i] // mass), surplus)
            counts[i] = counts[i] + extra
            surplus = surplus - extra
    return np.array([limit] + counts)


def uneven_parts(stream_key, count, total, limit, skew):
    if count == 2:
        one = jax.random.randint(stream_key, (), max(1, total - limit), min(limit, total - 1) + 1)
        return jnp.stack([one, total - one])
    tallies = jnp.asarray(profile(count, total, limit, skew), jnp.int32)
    couples = (count - 1) // 2
    giver, receiver = tallies[1:1 + 2 * couples:2], tallies[2:2 + 2 * couples:2]
    slack = jnp.minimum(giver - 1, limit - receiver)
    passed = jax.random.randint(jax.random.fold_in(stream_key, 1), (couples,), 0, 1 << 20) % (slack + 1)
    tallies = tallies.at[1:1 + 2 * couples:2].set(giver - passed).at[2:2 + 2 * couples:2].set(receiver + passed)
    return tallies[jax.random.permutation(jax.random.fold_in(stream_key, 2), count)]


def centred(stream_key, dims, scale, most, cuts=(), held_as=jnp.bfloat16):
    values = scale * jax.random.normal(stream_key, dims, jnp.float32)
    if cuts:
        values = values * levels(stream_key, dims, cuts, -0.22, 0.18)
    return jnp.clip(values, -most, most).astype(held_as)


def setup_inputs(seed: int = 0, part: int = 0) -> dict:
    seeds = jax.random.split(jax.random.key(seed), 11)
    part_keys = jax.random.split(jax.random.fold_in(seeds[10], part), 11)
    hidden_states = draw_hidden_states(jax.random.fold_in(jax.random.fold_in(seeds[10], part), 71), part)
    input_gain = jnp.clip(1.0 + 0.18 * jax.random.normal(seeds[1], (D,), jnp.float32), 0.1, 1.9)
    query_down = centred(seeds[2], (D, QRANK), D ** -0.5, 0.0625, ((0, 4), (1, 4)))
    memory_down = centred(seeds[3], (D, KVRANK + ROPE), D ** -0.5, 0.0625, ((0, 4), (1, 4)))
    query_gain = jnp.clip(1.0 + 0.18 * jax.random.normal(seeds[4], (QRANK,), jnp.float32), 0.1, 1.9)
    memory_gain = jnp.clip(1.0 + 0.18 * jax.random.normal(seeds[5], (KVRANK,), jnp.float32), 0.1, 1.9)
    query_up = draw_query_up(jax.random.fold_in(seeds[10], 71), part)
    key_up = centred(seeds[7], (KVRANK, HEADS * NOPE), KVRANK ** -0.5, 0.25, ((0, 4), (1, 4)))
    value_up = centred(seeds[8], (KVRANK, HEADS * VDIM), KVRANK ** -0.5, 0.25, ((0, 4), (1, 4)))
    segment_ids = jnp.searchsorted(jnp.cumsum(uneven_parts(part_keys[9], DOCS, TOKENS, DOC_MOST, 2)), jnp.arange(TOKENS), side="right").astype(jnp.int32)
    return dict(hidden_states=hidden_states, input_gain=input_gain, query_down=query_down, memory_down=memory_down, query_gain=query_gain, memory_gain=memory_gain, query_up=query_up, key_up=key_up, value_up=value_up, segment_ids=segment_ids)


epsilon = 1e-06

def rms_scale(entries, gain_vector):
    return entries * lax.rsqrt(lax.optimization_barrier(jnp.mean(entries * entries, -1, keepdims=True)) + epsilon) * gain_vector.astype(jnp.float32)

def rotate(entries, position):
    half_width = entries.shape[-1] // 2
    frequency = jnp.power(10000.0, -2.0 * jnp.arange(half_width, dtype=jnp.float32) / ROPE)
    angles = position.astype(jnp.float32)[..., None] * frequency
    cosine = jnp.cos(angles)
    sine_part = jnp.sin(angles)
    first_half = entries[..., :half_width]
    second_half = entries[..., half_width:]
    return jnp.concatenate([first_half * cosine - second_half * sine_part, second_half * cosine + first_half * sine_part], -1)

def reference(hidden_states, input_gain, query_down, memory_down, query_gain, memory_gain, query_up, key_up, value_up, segment_ids):
    inputs = hidden_states.astype(jnp.float32)
    normed = rms_scale(inputs, input_gain).astype(jnp.bfloat16)
    query_latent = jnp.dot(normed, query_down, preferred_element_type=jnp.float32)
    memory_latent = jnp.dot(normed, memory_down, preferred_element_type=jnp.float32)
    token_index = jnp.arange(TOKENS, dtype=jnp.int32)
    onehot = segment_ids[:, None] == jnp.arange(DOCS, dtype=jnp.int32)[None, :]
    starts = lax.optimization_barrier(jnp.min(jnp.where(onehot, token_index[:, None], TOKENS), 0)).astype(jnp.int32)
    position = (token_index - lax.optimization_barrier(jnp.sum(jnp.where(onehot, starts[None, :], 0), 1))).astype(jnp.int32)
    compressed_query = rms_scale(query_latent, query_gain).astype(jnp.bfloat16)
    compressed_memory = rms_scale(memory_latent[:, :KVRANK], memory_gain).astype(jnp.bfloat16)
    key_rope = rotate(memory_latent[:, KVRANK:], position).astype(jnp.bfloat16)
    query_full = jnp.dot(compressed_query, query_up, preferred_element_type=jnp.float32).reshape(TOKENS, HEADS, NOPE + ROPE)
    query = jnp.concatenate([query_full[..., :NOPE], rotate(query_full[..., NOPE:], position[:, None])], -1).astype(jnp.bfloat16)
    key_nope = jnp.dot(compressed_memory, key_up, preferred_element_type=jnp.float32).astype(jnp.bfloat16).reshape(TOKENS, HEADS, NOPE)
    value = jnp.dot(compressed_memory, value_up, preferred_element_type=jnp.float32).astype(jnp.bfloat16).reshape(TOKENS, HEADS, VDIM)
    allowed = (segment_ids[:, None] == segment_ids[None, :]) & (token_index[:, None] >= token_index[None, :])
    score_scale = (NOPE + ROPE) ** (-0.5)

    def one_head(operands):
        query_head, key_head, value_head = operands
        keys_full = jnp.concatenate([key_head, key_rope], -1)
        scores = jnp.dot(query_head, keys_full.T, preferred_element_type=jnp.float32) * score_scale
        scores = jnp.where(allowed, scores, -jnp.inf)
        row_max = lax.optimization_barrier(jnp.max(scores, -1, keepdims=True))
        probs_full = jnp.exp(scores - row_max)
        denominator = lax.optimization_barrier(jnp.sum(probs_full, -1, keepdims=True))
        weights = probs_full.astype(jnp.bfloat16)
        return jnp.dot(weights, value_head, preferred_element_type=jnp.float32) / denominator
    heads_out = lax.map(one_head, (jnp.transpose(query, (1, 0, 2)), jnp.transpose(key_nope, (1, 0, 2)), jnp.transpose(value, (1, 0, 2))))
    return jnp.transpose(heads_out, (1, 0, 2)).reshape(TOKENS, HEADS * VDIM).astype(jnp.bfloat16)
```

```python
import jax
import jax.numpy as jnp
from jax import lax
from jax.sharding import PartitionSpec as P

KVRANK = 512
NOPE = 128
ROPE = 64
VDIM = 128
DOCS = 12


epsilon = 1e-06


def rms_scale(entries, gain_vector):
    return (
        entries * lax.rsqrt(jnp.mean(entries * entries, -1, keepdims=True) + epsilon) * gain_vector
    )


def rotate(entries, position):
    half_width = entries.shape[-1] // 2
    frequency = jnp.power(10000.0, -2.0 * jnp.arange(half_width, dtype=jnp.float32) / ROPE)
    angles = position.astype(jnp.float32)[..., None] * frequency
    cosine = jnp.cos(angles)
    sine_part = jnp.sin(angles)
    first_half = entries[..., :half_width]
    second_half = entries[..., half_width:]
    return jnp.concatenate(
        [
            first_half * cosine - second_half * sine_part,
            second_half * cosine + first_half * sine_part,
        ],
        -1,
    )


def heads_attention(query_all, key_all, value_all, group_ids, score_scale, doc_most):
    total_rows = query_all.shape[0]
    block_rows = min(512, total_rows)
    key_index = jnp.arange(total_rows, dtype=jnp.int32)
    results = []
    for block in range(total_rows // block_rows):
        lower = block * block_rows
        upper = lower + block_rows
        key_low = max(0, lower - doc_most)
        scores = (
            jnp.einsum(
                "qhd,khd->hqk",
                query_all[lower:upper],
                key_all[key_low:upper],
                preferred_element_type=jnp.float32,
            )
            * score_scale
        )
        allowed = (group_ids[lower:upper, None] == group_ids[None, key_low:upper]) & (
            key_index[lower:upper, None] >= key_index[None, key_low:upper]
        )
        scores = jnp.where(allowed[None], scores, -jnp.inf)
        row_max = jnp.max(scores, -1, keepdims=True)
        probs_full = jnp.exp(scores - row_max)
        denominator = jnp.sum(probs_full, -1)
        weights = probs_full.astype(jnp.bfloat16)
        weighted = jnp.einsum(
            "hqk,khd->qhd", weights, value_all[key_low:upper], preferred_element_type=jnp.float32
        )
        results.append((weighted / jnp.transpose(denominator)[:, :, None]).astype(jnp.bfloat16))
    return jnp.concatenate(results, 0)


def body(
    hidden_states,
    input_gain,
    query_down,
    memory_down,
    query_gain,
    memory_gain,
    query_up,
    key_up,
    value_up,
    segment_ids,
):
    tok_count = hidden_states.shape[0]
    seq_count = lax.axis_size("seq")
    tp_count = lax.axis_size("tp")
    seq_index = lax.axis_index("seq")
    tp_index = lax.axis_index("tp")
    width = hidden_states.shape[1] * tp_count
    total_rows = tok_count * seq_count
    doc_most = total_rows // 4
    qrank_piece = query_down.shape[1]
    memory_piece = memory_down.shape[1]
    qrank = qrank_piece * seq_count
    memory_cols = memory_piece * seq_count

    group_ids = lax.all_gather(segment_ids, "seq", axis=0, tiled=True)
    token_index = jnp.arange(total_rows, dtype=jnp.int32)
    onehot = group_ids[:, None] == jnp.arange(DOCS, dtype=jnp.int32)[None, :]
    starts = jnp.min(jnp.where(onehot, token_index[:, None], total_rows), 0)
    position = token_index - jnp.sum(jnp.where(onehot, starts[None, :], 0), 1)

    inputs = hidden_states.astype(jnp.float32)
    square_sums = lax.psum(jnp.sum(inputs * inputs, 1), "tp")
    normed = (inputs * lax.rsqrt(square_sums / width + epsilon)[:, None] * input_gain).astype(
        jnp.bfloat16
    )

    down_piece = jnp.concatenate([query_down, memory_down], 1)
    down_all = lax.all_gather(down_piece, "seq", axis=1, tiled=True)
    partial = jnp.dot(normed, down_all, preferred_element_type=jnp.float32)
    latent_rows = lax.psum_scatter(partial, "tp", scatter_dimension=0, tiled=True)
    chunk = latent_rows.shape[0]
    latent_rows = latent_rows.reshape(chunk, seq_count, qrank_piece + memory_piece)
    query_sums = latent_rows[:, :, :qrank_piece].reshape(chunk, qrank)
    memory_sums = latent_rows[:, :, qrank_piece:].reshape(chunk, memory_cols)
    chunk_position = lax.dynamic_slice(
        position, (seq_index * tok_count + tp_index * chunk,), (chunk,)
    )
    compressed_query = rms_scale(query_sums, query_gain).astype(jnp.bfloat16)
    compressed_memory = rms_scale(memory_sums[:, :KVRANK], memory_gain).astype(jnp.bfloat16)
    key_rope = rotate(memory_sums[:, KVRANK:], chunk_position).astype(jnp.bfloat16)
    packed = jnp.concatenate([compressed_query, compressed_memory, key_rope], 1)
    packed = lax.all_gather(packed, "seq", axis=0, tiled=False)
    packed = lax.all_gather(packed, "tp", axis=0, tiled=False)
    latent = jnp.transpose(packed, (1, 0, 2, 3)).reshape(total_rows, packed.shape[-1])
    cq_all = latent[:, :qrank]
    cm_all = latent[:, qrank : qrank + KVRANK]
    rope_all = latent[:, qrank + KVRANK :]

    local_heads = query_up.shape[1] // (NOPE + ROPE)
    heads = local_heads // seq_count
    query_w = lax.all_to_all(
        query_up.reshape(query_up.shape[0], seq_count, heads * (NOPE + ROPE)),
        "seq",
        split_axis=1,
        concat_axis=0,
        tiled=True,
    ).reshape(qrank, heads * (NOPE + ROPE))
    key_w = lax.all_to_all(
        key_up.reshape(key_up.shape[0], seq_count, heads * NOPE),
        "seq",
        split_axis=1,
        concat_axis=0,
        tiled=True,
    ).reshape(KVRANK, heads * NOPE)
    value_w = lax.all_to_all(
        value_up.reshape(value_up.shape[0], seq_count, heads * VDIM),
        "seq",
        split_axis=1,
        concat_axis=0,
        tiled=True,
    ).reshape(KVRANK, heads * VDIM)

    query_full = jnp.dot(cq_all, query_w, preferred_element_type=jnp.float32).reshape(
        total_rows, heads, NOPE + ROPE
    )
    query = jnp.concatenate(
        [query_full[..., :NOPE], rotate(query_full[..., NOPE:], position[:, None])], -1
    ).astype(jnp.bfloat16)
    key_nope = (
        jnp.dot(cm_all, key_w, preferred_element_type=jnp.float32)
        .astype(jnp.bfloat16)
        .reshape(total_rows, heads, NOPE)
    )
    value = (
        jnp.dot(cm_all, value_w, preferred_element_type=jnp.float32)
        .astype(jnp.bfloat16)
        .reshape(total_rows, heads, VDIM)
    )
    key_all = jnp.concatenate(
        [key_nope, jnp.broadcast_to(rope_all[:, None, :], (total_rows, heads, ROPE))], -1
    )
    score_scale = (NOPE + ROPE) ** (-0.5)
    head_output = heads_attention(query, key_all, value, group_ids, score_scale, doc_most)
    attended = lax.all_to_all(head_output, "seq", split_axis=0, concat_axis=1, tiled=True)
    return attended.reshape(tok_count, local_heads * VDIM)


def solution(mesh):
    in_specs = (
        P(("dp", "seq"), "tp"),
        P("tp"),
        P("tp", "seq"),
        P("tp", "seq"),
        P(),
        P(),
        P("seq", "tp"),
        P("seq", "tp"),
        P("seq", "tp"),
        P(("dp", "seq")),
    )
    out_specs = P(("dp", "seq"), "tp")
    return jax.shard_map(body, mesh=mesh, in_specs=in_specs, out_specs=out_specs, check_vma=False)
```

```python
import jax
import jax.numpy as jnp
from jax import lax
from jax.sharding import PartitionSpec as P

KVRANK = 512
NOPE = 128
ROPE = 64
VDIM = 128
DOCS = 12


epsilon = 1e-06


def rms_scale(entries, gain_vector):
    return (
        entries * lax.rsqrt(jnp.mean(entries * entries, -1, keepdims=True) + epsilon) * gain_vector
    )


def rotate(entries, position):
    half_width = entries.shape[-1] // 2
    frequency = jnp.power(10000.0, -2.0 * jnp.arange(half_width, dtype=jnp.float32) / ROPE)
    angles = position.astype(jnp.float32)[..., None] * frequency
    cosine = jnp.cos(angles)
    sine_part = jnp.sin(angles)
    first_half = entries[..., :half_width]
    second_half = entries[..., half_width:]
    return jnp.concatenate(
        [
            first_half * cosine - second_half * sine_part,
            second_half * cosine + first_half * sine_part,
        ],
        -1,
    )


def heads_attention(query_all, key_all, value_all, group_ids, score_scale, doc_most):
    total_rows = query_all.shape[0]
    block_rows = min(512, total_rows)
    key_index = jnp.arange(total_rows, dtype=jnp.int32)
    results = []
    for block in range(total_rows // block_rows):
        lower = block * block_rows
        upper = lower + block_rows
        key_low = max(0, lower - doc_most)
        scores = (
            jnp.einsum(
                "qhd,khd->hqk",
                query_all[lower:upper],
                key_all[key_low:upper],
                preferred_element_type=jnp.float32,
            )
            * score_scale
        )
        allowed = (group_ids[lower:upper, None] == group_ids[None, key_low:upper]) & (
            key_index[lower:upper, None] >= key_index[None, key_low:upper]
        )
        scores = jnp.where(allowed[None], scores, -jnp.inf)
        row_max = jnp.max(scores, -1, keepdims=True)
        probs_full = jnp.exp(scores - row_max)
        denominator = jnp.sum(probs_full, -1)
        weights = probs_full.astype(jnp.bfloat16)
        weighted = jnp.einsum(
            "hqk,khd->qhd", weights, value_all[key_low:upper], preferred_element_type=jnp.float32
        )
        results.append((weighted / jnp.transpose(denominator)[:, :, None]).astype(jnp.bfloat16))
    return jnp.concatenate(results, 0)


def body(
    hidden_states,
    input_gain,
    query_down,
    memory_down,
    query_gain,
    memory_gain,
    query_up,
    key_up,
    value_up,
    segment_ids,
):
    tok_count = hidden_states.shape[0]
    seq_count = lax.axis_size("seq")
    tp_count = lax.axis_size("tp")
    seq_index = lax.axis_index("seq")
    tp_index = lax.axis_index("tp")
    width = hidden_states.shape[1] * tp_count
    total_rows = tok_count * seq_count
    doc_most = total_rows // 4
    qrank_piece = query_down.shape[1]
    memory_piece = memory_down.shape[1]
    qrank = qrank_piece * seq_count
    memory_cols = memory_piece * seq_count

    group_ids = lax.all_gather(segment_ids, "seq", axis=0, tiled=True)
    token_index = jnp.arange(total_rows, dtype=jnp.int32)
    onehot = group_ids[:, None] == jnp.arange(DOCS, dtype=jnp.int32)[None, :]
    starts = jnp.min(jnp.where(onehot, token_index[:, None], total_rows), 0)
    position = token_index - jnp.sum(jnp.where(onehot, starts[None, :], 0), 1)

    inputs = hidden_states.astype(jnp.float32)
    square_sums = lax.psum(jnp.sum(inputs * inputs, 1), "tp")
    normed = (inputs * lax.rsqrt(square_sums / width + epsilon)[:, None] * input_gain).astype(
        jnp.bfloat16
    )

    dp_index = lax.axis_index("dp")
    dp_count = lax.axis_size("dp")
    down_piece = jnp.concatenate([query_down, memory_down], 1)
    half_rows = down_piece.shape[0] // dp_count
    own_rows = lax.dynamic_slice_in_dim(down_piece, dp_index * half_rows, half_rows, 0)
    own_all = lax.all_gather(own_rows, "seq", axis=1, tiled=True)
    partial = jnp.dot(
        lax.dynamic_slice_in_dim(normed, dp_index * half_rows, half_rows, 1),
        own_all,
        preferred_element_type=jnp.float32,
    )
    for shift in range(1, dp_count):
        peer = (dp_index + dp_count - shift) % dp_count
        peer_all = lax.ppermute(
            own_all, "dp", perm=[(i, (i + shift) % dp_count) for i in range(dp_count)]
        )
        partial = partial + jnp.dot(
            lax.dynamic_slice_in_dim(normed, peer * half_rows, half_rows, 1),
            peer_all,
            preferred_element_type=jnp.float32,
        )
    latent_rows = lax.psum_scatter(partial, "tp", scatter_dimension=0, tiled=True)
    chunk = latent_rows.shape[0]
    latent_rows = latent_rows.reshape(chunk, seq_count, qrank_piece + memory_piece)
    query_sums = latent_rows[:, :, :qrank_piece].reshape(chunk, qrank)
    memory_sums = latent_rows[:, :, qrank_piece:].reshape(chunk, memory_cols)
    chunk_position = lax.dynamic_slice(
        position, (seq_index * tok_count + tp_index * chunk,), (chunk,)
    )
    compressed_query = rms_scale(query_sums, query_gain).astype(jnp.bfloat16)
    compressed_memory = rms_scale(memory_sums[:, :KVRANK], memory_gain).astype(jnp.bfloat16)
    key_rope = rotate(memory_sums[:, KVRANK:], chunk_position).astype(jnp.bfloat16)
    packed = jnp.concatenate([compressed_query, compressed_memory, key_rope], 1)
    latent = lax.all_gather(packed, ("seq", "tp"), axis=0, tiled=True)
    cq_all = latent[:, :qrank]
    cm_all = latent[:, qrank : qrank + KVRANK]
    rope_all = latent[:, qrank + KVRANK :]

    local_heads = query_up.shape[1] // (NOPE + ROPE)
    heads = local_heads // seq_count

    def head_columns(weight, head_width):
        rows = weight.shape[0]
        cols = heads * head_width // dp_count
        own = lax.dynamic_slice_in_dim(
            weight.reshape(rows, seq_count, heads * head_width), dp_index * cols, cols, 2
        )
        own = lax.all_to_all(own, "seq", split_axis=1, concat_axis=0, tiled=True)
        own = own.reshape(rows * seq_count, cols)
        pieces = [own]
        for shift in range(1, dp_count):
            pieces.append(
                lax.ppermute(
                    own, "dp", perm=[(i, (i + shift) % dp_count) for i in range(dp_count)]
                )
            )
        ordered = []
        for core in range(dp_count):
            pick = pieces[0]
            for k in range(1, dp_count):
                pick = jnp.where((dp_index + dp_count - k) % dp_count == core, pieces[k], pick)
            ordered.append(pick)
        return jnp.concatenate(ordered, 1)

    query_w = head_columns(query_up, NOPE + ROPE)
    key_w = head_columns(key_up, NOPE)
    value_w = head_columns(value_up, VDIM)

    query_full = jnp.dot(cq_all, query_w, preferred_element_type=jnp.float32).reshape(
        total_rows, heads, NOPE + ROPE
    )
    query = jnp.concatenate(
        [query_full[..., :NOPE], rotate(query_full[..., NOPE:], position[:, None])], -1
    ).astype(jnp.bfloat16)
    key_nope = (
        jnp.dot(cm_all, key_w, preferred_element_type=jnp.float32)
        .astype(jnp.bfloat16)
        .reshape(total_rows, heads, NOPE)
    )
    value = (
        jnp.dot(cm_all, value_w, preferred_element_type=jnp.float32)
        .astype(jnp.bfloat16)
        .reshape(total_rows, heads, VDIM)
    )
    key_all = jnp.concatenate(
        [key_nope, jnp.broadcast_to(rope_all[:, None, :], (total_rows, heads, ROPE))], -1
    )
    score_scale = (NOPE + ROPE) ** (-0.5)
    head_output = heads_attention(query, key_all, value, group_ids, score_scale, doc_most)
    attended = lax.all_to_all(head_output, "seq", split_axis=0, concat_axis=1, tiled=True)
    return attended.reshape(tok_count, local_heads * VDIM)


def solution(mesh):
    in_specs = (
        P(("dp", "seq"), "tp"),
        P("tp"),
        P("tp", "seq"),
        P("tp", "seq"),
        P(),
        P(),
        P("seq", "tp"),
        P("seq", "tp"),
        P("seq", "tp"),
        P(("dp", "seq")),
    )
    out_specs = P(("dp", "seq"), "tp")
    return jax.shard_map(body, mesh=mesh, in_specs=in_specs, out_specs=out_specs, check_vma=False)
```

```python
import jax
import jax.numpy as jnp
from jax import lax
from jax.sharding import PartitionSpec as P

KVRANK = 512
NOPE = 128
ROPE = 64
VDIM = 128
DOCS = 12


epsilon = 1e-06


def rms_scale(entries, gain_vector):
    return (
        entries * lax.rsqrt(jnp.mean(entries * entries, -1, keepdims=True) + epsilon) * gain_vector
    )


def rotate(entries, position):
    half_width = entries.shape[-1] // 2
    frequency = jnp.power(10000.0, -2.0 * jnp.arange(half_width, dtype=jnp.float32) / ROPE)
    angles = position.astype(jnp.float32)[..., None] * frequency
    cosine = jnp.cos(angles)
    sine_part = jnp.sin(angles)
    first_half = entries[..., :half_width]
    second_half = entries[..., half_width:]
    return jnp.concatenate(
        [
            first_half * cosine - second_half * sine_part,
            second_half * cosine + first_half * sine_part,
        ],
        -1,
    )


def heads_attention(query_all, key_all, value_all, group_ids, score_scale, doc_most):
    total_rows = query_all.shape[0]
    block_rows = min(512, total_rows)
    key_index = jnp.arange(total_rows, dtype=jnp.int32)
    results = []
    for block in range(total_rows // block_rows):
        lower = block * block_rows
        upper = lower + block_rows
        key_low = max(0, lower - doc_most)
        scores = (
            jnp.einsum(
                "qhd,khd->hqk",
                query_all[lower:upper],
                key_all[key_low:upper],
                preferred_element_type=jnp.float32,
            )
            * score_scale
        )
        allowed = (group_ids[lower:upper, None] == group_ids[None, key_low:upper]) & (
            key_index[lower:upper, None] >= key_index[None, key_low:upper]
        )
        scores = jnp.where(allowed[None], scores, -jnp.inf)
        row_max = jnp.max(scores, -1, keepdims=True)
        probs_full = jnp.exp(scores - row_max)
        denominator = jnp.sum(probs_full, -1)
        weights = probs_full.astype(jnp.bfloat16)
        weighted = jnp.einsum(
            "hqk,khd->qhd", weights, value_all[key_low:upper], preferred_element_type=jnp.float32
        )
        results.append((weighted / jnp.transpose(denominator)[:, :, None]).astype(jnp.bfloat16))
    return jnp.concatenate(results, 0)


def body(
    hidden_states,
    input_gain,
    query_down,
    memory_down,
    query_gain,
    memory_gain,
    query_up,
    key_up,
    value_up,
    segment_ids,
):
    tok_count = hidden_states.shape[0]
    seq_count = lax.axis_size("seq")
    tp_count = lax.axis_size("tp")
    seq_index = lax.axis_index("seq")
    tp_index = lax.axis_index("tp")
    width = hidden_states.shape[1] * tp_count
    total_rows = tok_count * seq_count
    doc_most = total_rows // 4
    qrank_piece = query_down.shape[1]
    memory_piece = memory_down.shape[1]
    qrank = qrank_piece * seq_count
    memory_cols = memory_piece * seq_count

    group_ids = lax.all_gather(segment_ids, "seq", axis=0, tiled=True)

    inputs = hidden_states.astype(jnp.float32)
    square_sums = lax.psum(jnp.sum(inputs * inputs, 1), "tp")
    normed = (inputs * lax.rsqrt(square_sums / width + epsilon)[:, None] * input_gain).astype(
        jnp.bfloat16
    )

    dp_index = lax.axis_index("dp")
    dp_count = lax.axis_size("dp")
    down_piece = jnp.concatenate([query_down, memory_down], 1)
    half_rows = down_piece.shape[0] // dp_count
    own_rows = lax.dynamic_slice_in_dim(down_piece, dp_index * half_rows, half_rows, 0)
    own_all = lax.all_gather(own_rows, "seq", axis=1, tiled=True)
    own_all, normed, group_ids = lax.optimization_barrier((own_all, normed, group_ids))
    partial = jnp.dot(
        lax.dynamic_slice_in_dim(normed, dp_index * half_rows, half_rows, 1),
        own_all,
        preferred_element_type=jnp.float32,
    )
    for shift in range(1, dp_count):
        peer = (dp_index + dp_count - shift) % dp_count
        peer_all = lax.ppermute(
            own_all, "dp", perm=[(i, (i + shift) % dp_count) for i in range(dp_count)]
        )
        partial = partial + jnp.dot(
            lax.dynamic_slice_in_dim(normed, peer * half_rows, half_rows, 1),
            peer_all,
            preferred_element_type=jnp.float32,
        )
    latent_rows = lax.psum_scatter(partial, "tp", scatter_dimension=0, tiled=True)

    token_index = jnp.arange(total_rows, dtype=jnp.int32)
    onehot = group_ids[:, None] == jnp.arange(DOCS, dtype=jnp.int32)[None, :]
    starts = jnp.min(jnp.where(onehot, token_index[:, None], total_rows), 0)
    position = token_index - jnp.sum(jnp.where(onehot, starts[None, :], 0), 1)
    chunk = latent_rows.shape[0]
    latent_rows = latent_rows.reshape(chunk, seq_count, qrank_piece + memory_piece)
    query_sums = latent_rows[:, :, :qrank_piece].reshape(chunk, qrank)
    memory_sums = latent_rows[:, :, qrank_piece:].reshape(chunk, memory_cols)
    chunk_position = lax.dynamic_slice(
        position, (seq_index * tok_count + tp_index * chunk,), (chunk,)
    )
    compressed_query = rms_scale(query_sums, query_gain).astype(jnp.bfloat16)
    compressed_memory = rms_scale(memory_sums[:, :KVRANK], memory_gain).astype(jnp.bfloat16)
    key_rope = rotate(memory_sums[:, KVRANK:], chunk_position).astype(jnp.bfloat16)
    packed = jnp.concatenate([compressed_query, compressed_memory, key_rope], 1)
    packed = lax.all_gather(packed, "seq", axis=0, tiled=False)
    packed = lax.all_gather(packed, "tp", axis=0, tiled=False)
    latent = jnp.transpose(packed, (1, 0, 2, 3)).reshape(total_rows, packed.shape[-1])
    cq_all = latent[:, :qrank]
    cm_all = latent[:, qrank : qrank + KVRANK]
    rope_all = latent[:, qrank + KVRANK :]

    local_heads = query_up.shape[1] // (NOPE + ROPE)
    heads = local_heads // seq_count

    def head_columns(weight, head_width):
        rows = weight.shape[0]
        cols = heads * head_width // dp_count
        own = lax.dynamic_slice_in_dim(
            weight.reshape(rows, seq_count, heads * head_width), dp_index * cols, cols, 2
        )
        own = lax.all_to_all(own, "seq", split_axis=1, concat_axis=0, tiled=True)
        own = own.reshape(rows * seq_count, cols)
        pieces = [own]
        for shift in range(1, dp_count):
            pieces.append(
                lax.ppermute(
                    own, "dp", perm=[(i, (i + shift) % dp_count) for i in range(dp_count)]
                )
            )
        ordered = []
        for core in range(dp_count):
            pick = pieces[0]
            for k in range(1, dp_count):
                pick = jnp.where((dp_index + dp_count - k) % dp_count == core, pieces[k], pick)
            ordered.append(pick)
        return jnp.concatenate(ordered, 1)

    query_w = head_columns(query_up, NOPE + ROPE)
    key_w = head_columns(key_up, NOPE)
    value_w = head_columns(value_up, VDIM)

    query_full = jnp.dot(cq_all, query_w, preferred_element_type=jnp.float32).reshape(
        total_rows, heads, NOPE + ROPE
    )
    query = jnp.concatenate(
        [query_full[..., :NOPE], rotate(query_full[..., NOPE:], position[:, None])], -1
    ).astype(jnp.bfloat16)
    key_nope = (
        jnp.dot(cm_all, key_w, preferred_element_type=jnp.float32)
        .astype(jnp.bfloat16)
        .reshape(total_rows, heads, NOPE)
    )
    value = (
        jnp.dot(cm_all, value_w, preferred_element_type=jnp.float32)
        .astype(jnp.bfloat16)
        .reshape(total_rows, heads, VDIM)
    )
    key_all = jnp.concatenate(
        [key_nope, jnp.broadcast_to(rope_all[:, None, :], (total_rows, heads, ROPE))], -1
    )
    score_scale = (NOPE + ROPE) ** (-0.5)
    groups = 2 if heads % 2 == 0 else 1
    per_group = heads // groups
    attended = []
    for group in range(groups):
        picked = slice(group * per_group, (group + 1) * per_group)
        head_output = heads_attention(
            query[:, picked], key_all[:, picked], value[:, picked], group_ids, score_scale, doc_most
        )
        attended.append(
            lax.all_to_all(head_output, "seq", split_axis=0, concat_axis=1, tiled=True).reshape(
                tok_count, seq_count, per_group, VDIM
            )
        )
    attended = jnp.concatenate(attended, 2)
    return attended.reshape(tok_count, local_heads * VDIM)


def solution(mesh):
    in_specs = (
        P(("dp", "seq"), "tp"),
        P("tp"),
        P("tp", "seq"),
        P("tp", "seq"),
        P(),
        P(),
        P("seq", "tp"),
        P("seq", "tp"),
        P("seq", "tp"),
        P(("dp", "seq")),
    )
    out_specs = P(("dp", "seq"), "tp")
    return jax.shard_map(body, mesh=mesh, in_specs=in_specs, out_specs=out_specs, check_vma=False)
```

```python
import jax
import jax.numpy as jnp
from jax import lax
from jax.sharding import PartitionSpec as P

KVRANK = 512
NOPE = 128
ROPE = 64
VDIM = 128
DOCS = 12


epsilon = 1e-06


def rms_scale(entries, gain_vector):
    return (
        entries * lax.rsqrt(jnp.mean(entries * entries, -1, keepdims=True) + epsilon) * gain_vector
    )


def rotate(entries, position):
    half_width = entries.shape[-1] // 2
    frequency = jnp.power(10000.0, -2.0 * jnp.arange(half_width, dtype=jnp.float32) / ROPE)
    angles = position.astype(jnp.float32)[..., None] * frequency
    cosine = jnp.cos(angles)
    sine_part = jnp.sin(angles)
    first_half = entries[..., :half_width]
    second_half = entries[..., half_width:]
    return jnp.concatenate(
        [
            first_half * cosine - second_half * sine_part,
            second_half * cosine + first_half * sine_part,
        ],
        -1,
    )


def heads_attention(query_all, key_all, value_all, group_ids, score_scale, doc_most):
    total_rows = query_all.shape[0]
    block_rows = min(512, total_rows)
    key_index = jnp.arange(total_rows, dtype=jnp.int32)
    results = []
    for block in range(total_rows // block_rows):
        lower = block * block_rows
        upper = lower + block_rows
        key_low = max(0, lower - doc_most)
        scores = (
            jnp.einsum(
                "qhd,khd->hqk",
                query_all[lower:upper],
                key_all[key_low:upper],
                preferred_element_type=jnp.float32,
            )
            * score_scale
        )
        allowed = (group_ids[lower:upper, None] == group_ids[None, key_low:upper]) & (
            key_index[lower:upper, None] >= key_index[None, key_low:upper]
        )
        scores = jnp.where(allowed[None], scores, -jnp.inf)
        row_max = jnp.max(scores, -1, keepdims=True)
        probs_full = jnp.exp(scores - row_max)
        denominator = jnp.sum(probs_full, -1)
        weights = probs_full.astype(jnp.bfloat16)
        weighted = jnp.einsum(
            "hqk,khd->qhd", weights, value_all[key_low:upper], preferred_element_type=jnp.float32
        )
        results.append((weighted / jnp.transpose(denominator)[:, :, None]).astype(jnp.bfloat16))
    return jnp.concatenate(results, 0)


def shifted(values, axis_name, count, shift):
    return lax.ppermute(values, axis_name, perm=[(i, (i + shift) % count) for i in range(count)])


def gather_chunks(chunk, seq_index, seq_count, tp_index, tp_count):
    from_seq = [chunk] + [shifted(chunk, "seq", seq_count, k) for k in range(1, seq_count)]
    plane = jnp.stack(from_seq)
    grid = [plane] + [shifted(plane, "tp", tp_count, k) for k in range(1, tp_count)]
    grid = jnp.stack(grid, 1)
    seq_order = (seq_index - jnp.arange(seq_count)) % seq_count
    tp_order = (tp_index - jnp.arange(tp_count)) % tp_count
    grid = jnp.take(grid, seq_order, axis=0)
    grid = jnp.take(grid, tp_order, axis=1)
    return grid.reshape(seq_count * tp_count * chunk.shape[0], chunk.shape[1])


def body(
    hidden_states,
    input_gain,
    query_down,
    memory_down,
    query_gain,
    memory_gain,
    query_up,
    key_up,
    value_up,
    segment_ids,
):
    tok_count = hidden_states.shape[0]
    seq_count = lax.axis_size("seq")
    tp_count = lax.axis_size("tp")
    seq_index = lax.axis_index("seq")
    tp_index = lax.axis_index("tp")
    width = hidden_states.shape[1] * tp_count
    total_rows = tok_count * seq_count
    doc_most = total_rows // 4
    qrank_piece = query_down.shape[1]
    memory_piece = memory_down.shape[1]
    qrank = qrank_piece * seq_count
    memory_cols = memory_piece * seq_count

    group_ids = lax.all_gather(segment_ids, "seq", axis=0, tiled=True)

    inputs = hidden_states.astype(jnp.float32)
    square_sums = lax.psum(jnp.sum(inputs * inputs, 1), "tp")
    normed = (inputs * lax.rsqrt(square_sums / width + epsilon)[:, None] * input_gain).astype(
        jnp.bfloat16
    )

    dp_index = lax.axis_index("dp")
    dp_count = lax.axis_size("dp")
    down_piece = jnp.concatenate([query_down, memory_down], 1)
    half_rows = down_piece.shape[0] // dp_count
    own_rows = lax.dynamic_slice_in_dim(down_piece, dp_index * half_rows, half_rows, 0)
    own_all = lax.all_gather(own_rows, "seq", axis=1, tiled=True)
    own_all, normed, group_ids = lax.optimization_barrier((own_all, normed, group_ids))
    partial = jnp.dot(
        lax.dynamic_slice_in_dim(normed, dp_index * half_rows, half_rows, 1),
        own_all,
        preferred_element_type=jnp.float32,
    )
    for shift in range(1, dp_count):
        peer = (dp_index + dp_count - shift) % dp_count
        peer_all = lax.ppermute(
            own_all, "dp", perm=[(i, (i + shift) % dp_count) for i in range(dp_count)]
        )
        partial = partial + jnp.dot(
            lax.dynamic_slice_in_dim(normed, peer * half_rows, half_rows, 1),
            peer_all,
            preferred_element_type=jnp.float32,
        )
    latent_rows = lax.psum_scatter(partial, "tp", scatter_dimension=0, tiled=True)

    token_index = jnp.arange(total_rows, dtype=jnp.int32)
    onehot = group_ids[:, None] == jnp.arange(DOCS, dtype=jnp.int32)[None, :]
    starts = jnp.min(jnp.where(onehot, token_index[:, None], total_rows), 0)
    position = token_index - jnp.sum(jnp.where(onehot, starts[None, :], 0), 1)
    chunk = latent_rows.shape[0]
    latent_rows = latent_rows.reshape(chunk, seq_count, qrank_piece + memory_piece)
    query_sums = latent_rows[:, :, :qrank_piece].reshape(chunk, qrank)
    memory_sums = latent_rows[:, :, qrank_piece:].reshape(chunk, memory_cols)
    chunk_position = lax.dynamic_slice(
        position, (seq_index * tok_count + tp_index * chunk,), (chunk,)
    )
    compressed_query = rms_scale(query_sums, query_gain).astype(jnp.bfloat16)
    compressed_memory = rms_scale(memory_sums[:, :KVRANK], memory_gain).astype(jnp.bfloat16)
    key_rope = rotate(memory_sums[:, KVRANK:], chunk_position).astype(jnp.bfloat16)
    packed = jnp.concatenate([compressed_query, compressed_memory, key_rope], 1)
    latent = gather_chunks(packed, seq_index, seq_count, tp_index, tp_count)
    cq_all = latent[:, :qrank]
    cm_all = latent[:, qrank : qrank + KVRANK]
    rope_all = latent[:, qrank + KVRANK :]

    local_heads = query_up.shape[1] // (NOPE + ROPE)
    heads = local_heads // seq_count

    def head_columns(weight, head_width):
        rows = weight.shape[0]
        cols = heads * head_width // dp_count
        own = lax.dynamic_slice_in_dim(
            weight.reshape(rows, seq_count, heads * head_width), dp_index * cols, cols, 2
        )
        own = lax.all_to_all(own, "seq", split_axis=1, concat_axis=0, tiled=True)
        own = own.reshape(rows * seq_count, cols)
        pieces = [own]
        for shift in range(1, dp_count):
            pieces.append(
                lax.ppermute(
                    own, "dp", perm=[(i, (i + shift) % dp_count) for i in range(dp_count)]
                )
            )
        ordered = []
        for core in range(dp_count):
            pick = pieces[0]
            for k in range(1, dp_count):
                pick = jnp.where((dp_index + dp_count - k) % dp_count == core, pieces[k], pick)
            ordered.append(pick)
        return jnp.concatenate(ordered, 1)

    query_w = head_columns(query_up, NOPE + ROPE)
    key_w = head_columns(key_up, NOPE)
    value_w = head_columns(value_up, VDIM)

    query_full = jnp.dot(cq_all, query_w, preferred_element_type=jnp.float32).reshape(
        total_rows, heads, NOPE + ROPE
    )
    query = jnp.concatenate(
        [query_full[..., :NOPE], rotate(query_full[..., NOPE:], position[:, None])], -1
    ).astype(jnp.bfloat16)
    key_nope = (
        jnp.dot(cm_all, key_w, preferred_element_type=jnp.float32)
        .astype(jnp.bfloat16)
        .reshape(total_rows, heads, NOPE)
    )
    value = (
        jnp.dot(cm_all, value_w, preferred_element_type=jnp.float32)
        .astype(jnp.bfloat16)
        .reshape(total_rows, heads, VDIM)
    )
    key_all = jnp.concatenate(
        [key_nope, jnp.broadcast_to(rope_all[:, None, :], (total_rows, heads, ROPE))], -1
    )
    score_scale = (NOPE + ROPE) ** (-0.5)
    groups = 2 if heads % 2 == 0 else 1
    per_group = heads // groups
    attended = []
    for group in range(groups):
        picked = slice(group * per_group, (group + 1) * per_group)
        head_output = heads_attention(
            query[:, picked], key_all[:, picked], value[:, picked], group_ids, score_scale, doc_most
        )
        attended.append(
            lax.all_to_all(head_output, "seq", split_axis=0, concat_axis=1, tiled=True).reshape(
                tok_count, seq_count, per_group, VDIM
            )
        )
    attended = jnp.concatenate(attended, 2)
    return attended.reshape(tok_count, local_heads * VDIM)


def solution(mesh):
    in_specs = (
        P(("dp", "seq"), "tp"),
        P("tp"),
        P("tp", "seq"),
        P("tp", "seq"),
        P(),
        P(),
        P("seq", "tp"),
        P("seq", "tp"),
        P("seq", "tp"),
        P(("dp", "seq")),
    )
    out_specs = P(("dp", "seq"), "tp")
    return jax.shard_map(body, mesh=mesh, in_specs=in_specs, out_specs=out_specs, check_vma=False)
```

```python
import jax
import jax.numpy as jnp
from jax import lax
from jax.sharding import PartitionSpec as P

KVRANK = 512
NOPE = 128
ROPE = 64
VDIM = 128
DOCS = 12


epsilon = 1e-06


def rms_scale(entries, gain_vector):
    return (
        entries * lax.rsqrt(jnp.mean(entries * entries, -1, keepdims=True) + epsilon) * gain_vector
    )


def rotate(entries, position):
    half_width = entries.shape[-1] // 2
    frequency = jnp.power(10000.0, -2.0 * jnp.arange(half_width, dtype=jnp.float32) / ROPE)
    angles = position.astype(jnp.float32)[..., None] * frequency
    cosine = jnp.cos(angles)
    sine_part = jnp.sin(angles)
    first_half = entries[..., :half_width]
    second_half = entries[..., half_width:]
    return jnp.concatenate(
        [
            first_half * cosine - second_half * sine_part,
            second_half * cosine + first_half * sine_part,
        ],
        -1,
    )


def heads_attention(query_all, key_all, value_all, group_ids, score_scale, doc_most):
    total_rows = query_all.shape[0]
    block_rows = min(512, total_rows)
    key_index = jnp.arange(total_rows, dtype=jnp.int32)
    results = []
    for block in range(total_rows // block_rows):
        lower = block * block_rows
        upper = lower + block_rows
        key_low = max(0, lower - doc_most)
        scores = (
            jnp.einsum(
                "qhd,khd->hqk",
                query_all[lower:upper],
                key_all[key_low:upper],
                preferred_element_type=jnp.float32,
            )
            * score_scale
        )
        allowed = (group_ids[lower:upper, None] == group_ids[None, key_low:upper]) & (
            key_index[lower:upper, None] >= key_index[None, key_low:upper]
        )
        scores = jnp.where(allowed[None], scores, -jnp.inf)
        row_max = jnp.max(scores, -1, keepdims=True)
        probs_full = jnp.exp(scores - row_max)
        denominator = jnp.sum(probs_full, -1)
        weights = probs_full.astype(jnp.bfloat16)
        weighted = jnp.einsum(
            "hqk,khd->qhd", weights, value_all[key_low:upper], preferred_element_type=jnp.float32
        )
        results.append((weighted / jnp.transpose(denominator)[:, :, None]).astype(jnp.bfloat16))
    return jnp.concatenate(results, 0)


def shifted(values, axis_name, count, shift):
    return lax.ppermute(values, axis_name, perm=[(i, (i + shift) % count) for i in range(count)])


def gather_chunks(chunk, seq_index, seq_count, tp_index, tp_count):
    from_seq = [chunk] + [shifted(chunk, "seq", seq_count, k) for k in range(1, seq_count)]
    plane = jnp.stack(from_seq)
    grid = [plane] + [shifted(plane, "tp", tp_count, k) for k in range(1, tp_count)]
    grid = jnp.stack(grid, 1).reshape(seq_count * tp_count, chunk.shape[0], chunk.shape[1])
    source = jnp.arange(seq_count * tp_count)
    order = ((seq_index - source // tp_count) % seq_count) * tp_count + (
        tp_index - source % tp_count
    ) % tp_count
    grid = jnp.take(grid, order, axis=0)
    return grid.reshape(seq_count * tp_count * chunk.shape[0], chunk.shape[1])


def body(
    hidden_states,
    input_gain,
    query_down,
    memory_down,
    query_gain,
    memory_gain,
    query_up,
    key_up,
    value_up,
    segment_ids,
):
    tok_count = hidden_states.shape[0]
    seq_count = lax.axis_size("seq")
    tp_count = lax.axis_size("tp")
    seq_index = lax.axis_index("seq")
    tp_index = lax.axis_index("tp")
    width = hidden_states.shape[1] * tp_count
    total_rows = tok_count * seq_count
    doc_most = total_rows // 4
    qrank_piece = query_down.shape[1]
    memory_piece = memory_down.shape[1]
    qrank = qrank_piece * seq_count
    memory_cols = memory_piece * seq_count

    group_ids = lax.all_gather(segment_ids, "seq", axis=0, tiled=True)

    inputs = hidden_states.astype(jnp.float32)
    square_sums = lax.psum(jnp.sum(inputs * inputs, 1), "tp")
    normed = (inputs * lax.rsqrt(square_sums / width + epsilon)[:, None] * input_gain).astype(
        jnp.bfloat16
    )

    dp_index = lax.axis_index("dp")
    dp_count = lax.axis_size("dp")
    down_piece = jnp.concatenate([query_down, memory_down], 1)
    half_rows = down_piece.shape[0] // dp_count
    own_rows = lax.dynamic_slice_in_dim(down_piece, dp_index * half_rows, half_rows, 0)
    own_all = lax.all_gather(own_rows, "seq", axis=1, tiled=True)
    own_all, normed, group_ids = lax.optimization_barrier((own_all, normed, group_ids))
    partial = jnp.dot(
        lax.dynamic_slice_in_dim(normed, dp_index * half_rows, half_rows, 1),
        own_all,
        preferred_element_type=jnp.float32,
    )
    for shift in range(1, dp_count):
        peer = (dp_index + dp_count - shift) % dp_count
        peer_all = lax.ppermute(
            own_all, "dp", perm=[(i, (i + shift) % dp_count) for i in range(dp_count)]
        )
        partial = partial + jnp.dot(
            lax.dynamic_slice_in_dim(normed, peer * half_rows, half_rows, 1),
            peer_all,
            preferred_element_type=jnp.float32,
        )

    token_index = jnp.arange(total_rows, dtype=jnp.int32)
    onehot = group_ids[:, None] == jnp.arange(DOCS, dtype=jnp.int32)[None, :]
    starts = jnp.min(jnp.where(onehot, token_index[:, None], total_rows), 0)
    position = token_index - jnp.sum(jnp.where(onehot, starts[None, :], 0), 1)

    partial = partial.reshape(tok_count, seq_count, qrank_piece + memory_piece)
    query_partial = partial[:, :, :qrank_piece].reshape(tok_count, qrank)
    memory_partial = partial[:, :, qrank_piece:].reshape(tok_count, memory_cols)
    chunk = tok_count // tp_count
    chunk_position = lax.dynamic_slice(
        position, (seq_index * tok_count + tp_index * chunk,), (chunk,)
    )

    query_sums = lax.psum_scatter(query_partial, "tp", scatter_dimension=0, tiled=True)
    compressed_query = rms_scale(query_sums, query_gain).astype(jnp.bfloat16)
    cq_all = lax.all_gather(compressed_query, "seq", axis=0, tiled=False)
    cq_all = lax.all_gather(cq_all, "tp", axis=0, tiled=False)
    cq_all = jnp.transpose(cq_all, (1, 0, 2, 3)).reshape(total_rows, qrank)

    blocks = memory_partial.reshape(tp_count, chunk, memory_cols)
    memory_sums = lax.dynamic_index_in_dim(blocks, tp_index, 0, keepdims=False)
    for k in range(1, tp_count):
        sent = lax.dynamic_index_in_dim(blocks, (tp_index + k) % tp_count, 0, keepdims=False)
        memory_sums = memory_sums + shifted(sent, "tp", tp_count, k)
    compressed_memory = rms_scale(memory_sums[:, :KVRANK], memory_gain).astype(jnp.bfloat16)
    key_rope = rotate(memory_sums[:, KVRANK:], chunk_position).astype(jnp.bfloat16)
    memory_all = gather_chunks(
        jnp.concatenate([compressed_memory, key_rope], 1), seq_index, seq_count, tp_index, tp_count
    )
    cm_all = memory_all[:, :KVRANK]
    rope_all = memory_all[:, KVRANK:]

    local_heads = query_up.shape[1] // (NOPE + ROPE)
    heads = local_heads // seq_count

    def head_columns(weight, head_width):
        rows = weight.shape[0]
        cols = heads * head_width // dp_count
        own = lax.dynamic_slice_in_dim(
            weight.reshape(rows, seq_count, heads * head_width), dp_index * cols, cols, 2
        )
        own = lax.all_to_all(own, "seq", split_axis=1, concat_axis=0, tiled=True)
        own = own.reshape(rows * seq_count, cols)
        pieces = [own]
        for shift in range(1, dp_count):
            pieces.append(
                lax.ppermute(
                    own, "dp", perm=[(i, (i + shift) % dp_count) for i in range(dp_count)]
                )
            )
        ordered = []
        for core in range(dp_count):
            pick = pieces[0]
            for k in range(1, dp_count):
                pick = jnp.where((dp_index + dp_count - k) % dp_count == core, pieces[k], pick)
            ordered.append(pick)
        return jnp.concatenate(ordered, 1)

    query_w = head_columns(query_up, NOPE + ROPE)
    key_w = head_columns(key_up, NOPE)
    value_w = head_columns(value_up, VDIM)

    query_full = jnp.dot(cq_all, query_w, preferred_element_type=jnp.float32).reshape(
        total_rows, heads, NOPE + ROPE
    )
    query = jnp.concatenate(
        [query_full[..., :NOPE], rotate(query_full[..., NOPE:], position[:, None])], -1
    ).astype(jnp.bfloat16)
    key_nope = (
        jnp.dot(cm_all, key_w, preferred_element_type=jnp.float32)
        .astype(jnp.bfloat16)
        .reshape(total_rows, heads, NOPE)
    )
    value = (
        jnp.dot(cm_all, value_w, preferred_element_type=jnp.float32)
        .astype(jnp.bfloat16)
        .reshape(total_rows, heads, VDIM)
    )
    key_all = jnp.concatenate(
        [key_nope, jnp.broadcast_to(rope_all[:, None, :], (total_rows, heads, ROPE))], -1
    )
    score_scale = (NOPE + ROPE) ** (-0.5)
    groups = 2 if heads % 2 == 0 else 1
    per_group = heads // groups
    attended = []
    for group in range(groups):
        picked = slice(group * per_group, (group + 1) * per_group)
        head_output = heads_attention(
            query[:, picked], key_all[:, picked], value[:, picked], group_ids, score_scale, doc_most
        )
        attended.append(
            lax.all_to_all(head_output, "seq", split_axis=0, concat_axis=1, tiled=True).reshape(
                tok_count, seq_count, per_group, VDIM
            )
        )
    attended = jnp.concatenate(attended, 2)
    return attended.reshape(tok_count, local_heads * VDIM)


def solution(mesh):
    in_specs = (
        P(("dp", "seq"), "tp"),
        P("tp"),
        P("tp", "seq"),
        P("tp", "seq"),
        P(),
        P(),
        P("seq", "tp"),
        P("seq", "tp"),
        P("seq", "tp"),
        P(("dp", "seq")),
    )
    out_specs = P(("dp", "seq"), "tp")
    return jax.shard_map(body, mesh=mesh, in_specs=in_specs, out_specs=out_specs, check_vma=False)
```

```python
import jax
import jax.numpy as jnp
from jax import lax
from jax.sharding import PartitionSpec as P

KVRANK = 512
NOPE = 128
ROPE = 64
VDIM = 128
DOCS = 12


epsilon = 1e-06


def rms_scale(entries, gain_vector):
    return (
        entries * lax.rsqrt(jnp.mean(entries * entries, -1, keepdims=True) + epsilon) * gain_vector
    )


def rotate(entries, position):
    half_width = entries.shape[-1] // 2
    frequency = jnp.power(10000.0, -2.0 * jnp.arange(half_width, dtype=jnp.float32) / ROPE)
    angles = position.astype(jnp.float32)[..., None] * frequency
    cosine = jnp.cos(angles)
    sine_part = jnp.sin(angles)
    first_half = entries[..., :half_width]
    second_half = entries[..., half_width:]
    return jnp.concatenate(
        [
            first_half * cosine - second_half * sine_part,
            second_half * cosine + first_half * sine_part,
        ],
        -1,
    )


def heads_attention(query_all, key_all, value_all, group_ids, score_scale, doc_most):
    total_rows = query_all.shape[0]
    block_rows = min(512, total_rows)
    key_index = jnp.arange(total_rows, dtype=jnp.int32)
    results = []
    for block in range(total_rows // block_rows):
        lower = block * block_rows
        upper = lower + block_rows
        key_low = max(0, lower - doc_most)
        scores = (
            jnp.einsum(
                "qhd,khd->hqk",
                query_all[lower:upper],
                key_all[key_low:upper],
                preferred_element_type=jnp.float32,
            )
            * score_scale
        )
        allowed = (group_ids[lower:upper, None] == group_ids[None, key_low:upper]) & (
            key_index[lower:upper, None] >= key_index[None, key_low:upper]
        )
        scores = jnp.where(allowed[None], scores, -jnp.inf)
        row_max = jnp.max(scores, -1, keepdims=True)
        probs_full = jnp.exp(scores - row_max)
        denominator = jnp.sum(probs_full, -1)
        weights = probs_full.astype(jnp.bfloat16)
        weighted = jnp.einsum(
            "hqk,khd->qhd", weights, value_all[key_low:upper], preferred_element_type=jnp.float32
        )
        results.append((weighted / jnp.transpose(denominator)[:, :, None]).astype(jnp.bfloat16))
    return jnp.concatenate(results, 0)


def body(
    hidden_states,
    input_gain,
    query_down,
    memory_down,
    query_gain,
    memory_gain,
    query_up,
    key_up,
    value_up,
    segment_ids,
):
    tok_count = hidden_states.shape[0]
    seq_count = lax.axis_size("seq")
    tp_count = lax.axis_size("tp")
    seq_index = lax.axis_index("seq")
    tp_index = lax.axis_index("tp")
    width = hidden_states.shape[1] * tp_count
    total_rows = tok_count * seq_count
    doc_most = total_rows // 4
    qrank_piece = query_down.shape[1]
    memory_piece = memory_down.shape[1]
    qrank = qrank_piece * seq_count
    memory_cols = memory_piece * seq_count

    group_ids = lax.all_gather(segment_ids, "seq", axis=0, tiled=True)

    inputs = hidden_states.astype(jnp.float32)
    square_sums = lax.psum(jnp.sum(inputs * inputs, 1), "tp")
    normed = (inputs * lax.rsqrt(square_sums / width + epsilon)[:, None] * input_gain).astype(
        jnp.bfloat16
    )

    dp_index = lax.axis_index("dp")
    dp_count = lax.axis_size("dp")
    down_piece = jnp.concatenate([query_down, memory_down], 1)
    half_rows = down_piece.shape[0] // dp_count
    own_rows = lax.dynamic_slice_in_dim(down_piece, dp_index * half_rows, half_rows, 0)
    own_all = lax.all_gather(own_rows, "seq", axis=1, tiled=True)
    local_heads = query_up.shape[1] // (NOPE + ROPE)
    heads = local_heads // seq_count

    def head_columns(weight, head_width):
        rows = weight.shape[0]
        cols = heads * head_width // dp_count
        own = lax.dynamic_slice_in_dim(
            weight.reshape(rows, seq_count, heads * head_width), dp_index * cols, cols, 2
        )
        own = lax.all_to_all(own, "seq", split_axis=1, concat_axis=0, tiled=True)
        own = own.reshape(rows * seq_count, cols)
        pieces = [own]
        for shift in range(1, dp_count):
            pieces.append(
                lax.ppermute(
                    own, "dp", perm=[(i, (i + shift) % dp_count) for i in range(dp_count)]
                )
            )
        ordered = []
        for core in range(dp_count):
            pick = pieces[0]
            for k in range(1, dp_count):
                pick = jnp.where((dp_index + dp_count - k) % dp_count == core, pieces[k], pick)
            ordered.append(pick)
        return jnp.concatenate(ordered, 1)

    query_w = head_columns(query_up, NOPE + ROPE)
    key_w = head_columns(key_up, NOPE)
    value_w = head_columns(value_up, VDIM)

    own_all, normed, group_ids, query_w, key_w, value_w = lax.optimization_barrier(
        (own_all, normed, group_ids, query_w, key_w, value_w)
    )
    partial = jnp.dot(
        lax.dynamic_slice_in_dim(normed, dp_index * half_rows, half_rows, 1),
        own_all,
        preferred_element_type=jnp.float32,
    )
    for shift in range(1, dp_count):
        peer = (dp_index + dp_count - shift) % dp_count
        peer_all = lax.ppermute(
            own_all, "dp", perm=[(i, (i + shift) % dp_count) for i in range(dp_count)]
        )
        partial = partial + jnp.dot(
            lax.dynamic_slice_in_dim(normed, peer * half_rows, half_rows, 1),
            peer_all,
            preferred_element_type=jnp.float32,
        )
    latent_rows = lax.psum_scatter(partial, "tp", scatter_dimension=0, tiled=True)

    token_index = jnp.arange(total_rows, dtype=jnp.int32)
    onehot = group_ids[:, None] == jnp.arange(DOCS, dtype=jnp.int32)[None, :]
    starts = jnp.min(jnp.where(onehot, token_index[:, None], total_rows), 0)
    position = token_index - jnp.sum(jnp.where(onehot, starts[None, :], 0), 1)
    chunk = latent_rows.shape[0]
    latent_rows = latent_rows.reshape(chunk, seq_count, qrank_piece + memory_piece)
    query_sums = latent_rows[:, :, :qrank_piece].reshape(chunk, qrank)
    memory_sums = latent_rows[:, :, qrank_piece:].reshape(chunk, memory_cols)
    chunk_position = lax.dynamic_slice(
        position, (seq_index * tok_count + tp_index * chunk,), (chunk,)
    )
    compressed_query = rms_scale(query_sums, query_gain).astype(jnp.bfloat16)
    compressed_memory = rms_scale(memory_sums[:, :KVRANK], memory_gain).astype(jnp.bfloat16)
    key_rope = rotate(memory_sums[:, KVRANK:], chunk_position).astype(jnp.bfloat16)
    packed = jnp.concatenate([compressed_query, compressed_memory, key_rope], 1)
    packed = lax.all_gather(packed, "seq", axis=0, tiled=False)
    packed = lax.all_gather(packed, "tp", axis=0, tiled=False)
    latent = jnp.transpose(packed, (1, 0, 2, 3)).reshape(total_rows, packed.shape[-1])
    cq_all = latent[:, :qrank]
    cm_all = latent[:, qrank : qrank + KVRANK]
    rope_all = latent[:, qrank + KVRANK :]

    query_full = jnp.dot(cq_all, query_w, preferred_element_type=jnp.float32).reshape(
        total_rows, heads, NOPE + ROPE
    )
    query = jnp.concatenate(
        [query_full[..., :NOPE], rotate(query_full[..., NOPE:], position[:, None])], -1
    ).astype(jnp.bfloat16)
    key_nope = (
        jnp.dot(cm_all, key_w, preferred_element_type=jnp.float32)
        .astype(jnp.bfloat16)
        .reshape(total_rows, heads, NOPE)
    )
    value = (
        jnp.dot(cm_all, value_w, preferred_element_type=jnp.float32)
        .astype(jnp.bfloat16)
        .reshape(total_rows, heads, VDIM)
    )
    key_all = jnp.concatenate(
        [key_nope, jnp.broadcast_to(rope_all[:, None, :], (total_rows, heads, ROPE))], -1
    )
    score_scale = (NOPE + ROPE) ** (-0.5)
    groups = 2 if heads % 2 == 0 else 1
    per_group = heads // groups
    attended = []
    for group in range(groups):
        picked = slice(group * per_group, (group + 1) * per_group)
        head_output = heads_attention(
            query[:, picked], key_all[:, picked], value[:, picked], group_ids, score_scale, doc_most
        )
        attended.append(
            lax.all_to_all(head_output, "seq", split_axis=0, concat_axis=1, tiled=True).reshape(
                tok_count, seq_count, per_group, VDIM
            )
        )
    attended = jnp.concatenate(attended, 2)
    return attended.reshape(tok_count, local_heads * VDIM)


def solution(mesh):
    in_specs = (
        P(("dp", "seq"), "tp"),
        P("tp"),
        P("tp", "seq"),
        P("tp", "seq"),
        P(),
        P(),
        P("seq", "tp"),
        P("seq", "tp"),
        P("seq", "tp"),
        P(("dp", "seq")),
    )
    out_specs = P(("dp", "seq"), "tp")
    return jax.shard_map(body, mesh=mesh, in_specs=in_specs, out_specs=out_specs, check_vma=False)
```

```python
import functools

import jax
import jax.numpy as jnp
from jax import lax
from jax.experimental import pallas as pl
from jax.experimental.pallas import tpu as pltpu
from jax.sharding import PartitionSpec as P

KVRANK = 512
NOPE = 128
ROPE = 64
VDIM = 128
DOCS = 12


epsilon = 1e-06


def rms_scale(entries, gain_vector):
    return (
        entries * lax.rsqrt(jnp.mean(entries * entries, -1, keepdims=True) + epsilon) * gain_vector
    )


def rotate(entries, position):
    half_width = entries.shape[-1] // 2
    frequency = jnp.power(10000.0, -2.0 * jnp.arange(half_width, dtype=jnp.float32) / ROPE)
    angles = position.astype(jnp.float32)[..., None] * frequency
    cosine = jnp.cos(angles)
    sine_part = jnp.sin(angles)
    first_half = entries[..., :half_width]
    second_half = entries[..., half_width:]
    return jnp.concatenate(
        [
            first_half * cosine - second_half * sine_part,
            second_half * cosine + first_half * sine_part,
        ],
        -1,
    )


def heads_attention(query_all, key_all, value_all, group_ids, score_scale, doc_most):
    total_rows = query_all.shape[0]
    block_rows = min(512, total_rows)
    key_index = jnp.arange(total_rows, dtype=jnp.int32)
    results = []
    for block in range(total_rows // block_rows):
        lower = block * block_rows
        upper = lower + block_rows
        key_low = max(0, lower - doc_most)
        scores = (
            jnp.einsum(
                "qhd,khd->hqk",
                query_all[lower:upper],
                key_all[key_low:upper],
                preferred_element_type=jnp.float32,
            )
            * score_scale
        )
        allowed = (group_ids[lower:upper, None] == group_ids[None, key_low:upper]) & (
            key_index[lower:upper, None] >= key_index[None, key_low:upper]
        )
        scores = jnp.where(allowed[None], scores, -jnp.inf)
        row_max = jnp.max(scores, -1, keepdims=True)
        probs_full = jnp.exp(scores - row_max)
        denominator = jnp.sum(probs_full, -1)
        weights = probs_full.astype(jnp.bfloat16)
        weighted = jnp.einsum(
            "hqk,khd->qhd", weights, value_all[key_low:upper], preferred_element_type=jnp.float32
        )
        results.append((weighted / jnp.transpose(denominator)[:, :, None]).astype(jnp.bfloat16))
    return jnp.concatenate(results, 0)


def attention_kernel(
    query_ref, key_ref, rope_ref, value_ref, ids_col_ref, ids_row_ref, out_ref, *, block, window, doc_most, scale
):
    lower = pl.program_id(1) * block
    start = pl.multiple_of(jnp.maximum(lower - doc_most, 0), block)
    query = query_ref[0]
    keys = key_ref[0, pl.ds(start, window), :]
    rope = rope_ref[pl.ds(start, window), :]
    values = value_ref[0, pl.ds(start, window), :]
    dims = (((1,), (1,)), ((), ()))
    scores = lax.dot_general(query[:, :NOPE], keys, dims, preferred_element_type=jnp.float32)
    scores = scores + lax.dot_general(
        query[:, NOPE:], rope, dims, preferred_element_type=jnp.float32
    )
    scores = scores * scale
    query_index = lower + lax.broadcasted_iota(jnp.int32, (block, window), 0)
    key_index = start + lax.broadcasted_iota(jnp.int32, (block, window), 1)
    allowed = (ids_col_ref[...] == ids_row_ref[:, pl.ds(start, window)]) & (
        query_index >= key_index
    )
    scores = jnp.where(allowed, scores, -jnp.inf)
    row_max = jnp.max(scores, -1, keepdims=True)
    probs = jnp.exp(scores - row_max)
    denominator = jnp.sum(probs, -1, keepdims=True)
    weighted = jnp.dot(probs.astype(jnp.bfloat16), values, preferred_element_type=jnp.float32)
    out_ref[0] = (weighted / denominator).astype(out_ref.dtype)


def heads_attention_kernel(query, key_nope, key_rope, value, group_ids, score_scale, doc_most):
    heads, total_rows, _ = query.shape
    block = min(256, total_rows)
    window = min(total_rows, doc_most + block)
    kernel = functools.partial(
        attention_kernel, block=block, window=window, doc_most=doc_most, scale=score_scale
    )
    flops = 2 * heads * total_rows * window * (NOPE + ROPE + VDIM)
    return pl.pallas_call(
        kernel,
        grid=(heads, total_rows // block),
        in_specs=[
            pl.BlockSpec((1, block, NOPE + ROPE), lambda h, i: (h, i, 0)),
            pl.BlockSpec((1, total_rows, NOPE), lambda h, i: (h, 0, 0)),
            pl.BlockSpec((total_rows, ROPE), lambda h, i: (0, 0)),
            pl.BlockSpec((1, total_rows, VDIM), lambda h, i: (h, 0, 0)),
            pl.BlockSpec((block, 1), lambda h, i: (i, 0)),
            pl.BlockSpec((1, total_rows), lambda h, i: (0, 0)),
        ],
        out_specs=pl.BlockSpec((1, block, VDIM), lambda h, i: (h, i, 0)),
        out_shape=jax.ShapeDtypeStruct((heads, total_rows, VDIM), jnp.bfloat16),
        cost_estimate=pl.CostEstimate(
            flops=flops,
            transcendentals=heads * total_rows * window,
            bytes_accessed=2 * heads * total_rows * (NOPE + ROPE + NOPE + VDIM + VDIM),
        ),
    )(
        query,
        key_nope,
        key_rope,
        value,
        group_ids.reshape(total_rows, 1),
        group_ids.reshape(1, total_rows),
    )


def body(
    hidden_states,
    input_gain,
    query_down,
    memory_down,
    query_gain,
    memory_gain,
    query_up,
    key_up,
    value_up,
    segment_ids,
):
    tok_count = hidden_states.shape[0]
    seq_count = lax.axis_size("seq")
    tp_count = lax.axis_size("tp")
    seq_index = lax.axis_index("seq")
    tp_index = lax.axis_index("tp")
    width = hidden_states.shape[1] * tp_count
    total_rows = tok_count * seq_count
    doc_most = total_rows // 4
    qrank_piece = query_down.shape[1]
    memory_piece = memory_down.shape[1]
    qrank = qrank_piece * seq_count
    memory_cols = memory_piece * seq_count

    group_ids = lax.all_gather(segment_ids, "seq", axis=0, tiled=True)

    inputs = hidden_states.astype(jnp.float32)
    square_sums = lax.psum(jnp.sum(inputs * inputs, 1), "tp")
    normed = (inputs * lax.rsqrt(square_sums / width + epsilon)[:, None] * input_gain).astype(
        jnp.bfloat16
    )

    dp_index = lax.axis_index("dp")
    dp_count = lax.axis_size("dp")
    down_piece = jnp.concatenate([query_down, memory_down], 1)
    half_rows = down_piece.shape[0] // dp_count
    own_rows = lax.dynamic_slice_in_dim(down_piece, dp_index * half_rows, half_rows, 0)
    own_all = lax.all_gather(own_rows, "seq", axis=1, tiled=True)
    own_all, normed, group_ids = lax.optimization_barrier((own_all, normed, group_ids))
    partial = jnp.dot(
        lax.dynamic_slice_in_dim(normed, dp_index * half_rows, half_rows, 1),
        own_all,
        preferred_element_type=jnp.float32,
    )
    for shift in range(1, dp_count):
        peer = (dp_index + dp_count - shift) % dp_count
        peer_all = lax.ppermute(
            own_all, "dp", perm=[(i, (i + shift) % dp_count) for i in range(dp_count)]
        )
        partial = partial + jnp.dot(
            lax.dynamic_slice_in_dim(normed, peer * half_rows, half_rows, 1),
            peer_all,
            preferred_element_type=jnp.float32,
        )
    latent_rows = lax.psum_scatter(partial, "tp", scatter_dimension=0, tiled=True)

    token_index = jnp.arange(total_rows, dtype=jnp.int32)
    onehot = group_ids[:, None] == jnp.arange(DOCS, dtype=jnp.int32)[None, :]
    starts = jnp.min(jnp.where(onehot, token_index[:, None], total_rows), 0)
    position = token_index - jnp.sum(jnp.where(onehot, starts[None, :], 0), 1)
    chunk = latent_rows.shape[0]
    latent_rows = latent_rows.reshape(chunk, seq_count, qrank_piece + memory_piece)
    query_sums = latent_rows[:, :, :qrank_piece].reshape(chunk, qrank)
    memory_sums = latent_rows[:, :, qrank_piece:].reshape(chunk, memory_cols)
    chunk_position = lax.dynamic_slice(
        position, (seq_index * tok_count + tp_index * chunk,), (chunk,)
    )
    compressed_query = rms_scale(query_sums, query_gain).astype(jnp.bfloat16)
    compressed_memory = rms_scale(memory_sums[:, :KVRANK], memory_gain).astype(jnp.bfloat16)
    key_rope = rotate(memory_sums[:, KVRANK:], chunk_position).astype(jnp.bfloat16)
    packed = jnp.concatenate([compressed_query, compressed_memory, key_rope], 1)
    packed = lax.all_gather(packed, "seq", axis=0, tiled=False)
    packed = lax.all_gather(packed, "tp", axis=0, tiled=False)
    latent = jnp.transpose(packed, (1, 0, 2, 3)).reshape(total_rows, packed.shape[-1])
    cq_all = latent[:, :qrank]
    cm_all = latent[:, qrank : qrank + KVRANK]
    rope_all = latent[:, qrank + KVRANK :]

    local_heads = query_up.shape[1] // (NOPE + ROPE)
    heads = local_heads // seq_count

    def head_columns(weight, head_width):
        rows = weight.shape[0]
        cols = heads * head_width // dp_count
        own = lax.dynamic_slice_in_dim(
            weight.reshape(rows, seq_count, heads * head_width), dp_index * cols, cols, 2
        )
        own = lax.all_to_all(own, "seq", split_axis=1, concat_axis=0, tiled=True)
        own = own.reshape(rows * seq_count, cols)
        pieces = [own]
        for shift in range(1, dp_count):
            pieces.append(
                lax.ppermute(
                    own, "dp", perm=[(i, (i + shift) % dp_count) for i in range(dp_count)]
                )
            )
        ordered = []
        for core in range(dp_count):
            pick = pieces[0]
            for k in range(1, dp_count):
                pick = jnp.where((dp_index + dp_count - k) % dp_count == core, pieces[k], pick)
            ordered.append(pick)
        return jnp.concatenate(ordered, 1)

    query_w = head_columns(query_up, NOPE + ROPE)
    key_w = head_columns(key_up, NOPE)
    value_w = head_columns(value_up, VDIM)

    query_full = jnp.einsum(
        "td,dhe->hte",
        cq_all,
        query_w.reshape(qrank, heads, NOPE + ROPE),
        preferred_element_type=jnp.float32,
    )
    query = jnp.concatenate(
        [query_full[..., :NOPE], rotate(query_full[..., NOPE:], position[None, :])], -1
    ).astype(jnp.bfloat16)
    key_nope = jnp.einsum(
        "td,dhe->hte", cm_all, key_w.reshape(KVRANK, heads, NOPE), preferred_element_type=jnp.float32
    ).astype(jnp.bfloat16)
    value = jnp.einsum(
        "td,dhe->hte", cm_all, value_w.reshape(KVRANK, heads, VDIM), preferred_element_type=jnp.float32
    ).astype(jnp.bfloat16)
    score_scale = (NOPE + ROPE) ** (-0.5)
    head_output = heads_attention_kernel(
        query, key_nope, rope_all, value, group_ids, score_scale, doc_most
    )
    attended = lax.all_to_all(head_output, "seq", split_axis=1, concat_axis=0, tiled=True)
    attended = jnp.transpose(attended, (1, 0, 2))
    return attended.reshape(tok_count, local_heads * VDIM)


def solution(mesh):
    in_specs = (
        P(("dp", "seq"), "tp"),
        P("tp"),
        P("tp", "seq"),
        P("tp", "seq"),
        P(),
        P(),
        P("seq", "tp"),
        P("seq", "tp"),
        P("seq", "tp"),
        P(("dp", "seq")),
    )
    out_specs = P(("dp", "seq"), "tp")
    return jax.shard_map(body, mesh=mesh, in_specs=in_specs, out_specs=out_specs, check_vma=False)
```

```python
import functools

import jax
import jax.numpy as jnp
from jax import lax
from jax.experimental import pallas as pl
from jax.experimental.pallas import tpu as pltpu
from jax.sharding import PartitionSpec as P

KVRANK = 512
NOPE = 128
ROPE = 64
VDIM = 128
DOCS = 12


epsilon = 1e-06


def rms_scale(entries, gain_vector):
    return (
        entries * lax.rsqrt(jnp.mean(entries * entries, -1, keepdims=True) + epsilon) * gain_vector
    )


def rotate(entries, position):
    half_width = entries.shape[-1] // 2
    frequency = jnp.power(10000.0, -2.0 * jnp.arange(half_width, dtype=jnp.float32) / ROPE)
    angles = position.astype(jnp.float32)[..., None] * frequency
    cosine = jnp.cos(angles)
    sine_part = jnp.sin(angles)
    first_half = entries[..., :half_width]
    second_half = entries[..., half_width:]
    return jnp.concatenate(
        [
            first_half * cosine - second_half * sine_part,
            second_half * cosine + first_half * sine_part,
        ],
        -1,
    )


def heads_attention(query_all, key_all, value_all, group_ids, score_scale, doc_most):
    total_rows = query_all.shape[0]
    block_rows = min(512, total_rows)
    key_index = jnp.arange(total_rows, dtype=jnp.int32)
    results = []
    for block in range(total_rows // block_rows):
        lower = block * block_rows
        upper = lower + block_rows
        key_low = max(0, lower - doc_most)
        scores = (
            jnp.einsum(
                "qhd,khd->hqk",
                query_all[lower:upper],
                key_all[key_low:upper],
                preferred_element_type=jnp.float32,
            )
            * score_scale
        )
        allowed = (group_ids[lower:upper, None] == group_ids[None, key_low:upper]) & (
            key_index[lower:upper, None] >= key_index[None, key_low:upper]
        )
        scores = jnp.where(allowed[None], scores, -jnp.inf)
        row_max = jnp.max(scores, -1, keepdims=True)
        probs_full = jnp.exp(scores - row_max)
        denominator = jnp.sum(probs_full, -1)
        weights = probs_full.astype(jnp.bfloat16)
        weighted = jnp.einsum(
            "hqk,khd->qhd", weights, value_all[key_low:upper], preferred_element_type=jnp.float32
        )
        results.append((weighted / jnp.transpose(denominator)[:, :, None]).astype(jnp.bfloat16))
    return jnp.concatenate(results, 0)


def attention_kernel(
    query_ref, key_ref, rope_ref, value_ref, ids_col_ref, ids_row_ref, out_ref, *, block, window, doc_most, scale
):
    lower = pl.program_id(1) * block
    start = pl.multiple_of(jnp.maximum(lower - doc_most, 0), block)
    query = query_ref[0]
    keys = key_ref[0, pl.ds(start, window), :]
    rope = rope_ref[pl.ds(start, window), :]
    values = value_ref[0, pl.ds(start, window), :]
    dims = (((1,), (1,)), ((), ()))
    scores = lax.dot_general(query[:, :NOPE], keys, dims, preferred_element_type=jnp.float32)
    scores = scores + lax.dot_general(
        query[:, NOPE:], rope, dims, preferred_element_type=jnp.float32
    )
    scores = scores * scale
    query_index = lower + lax.broadcasted_iota(jnp.int32, (block, window), 0)
    key_index = start + lax.broadcasted_iota(jnp.int32, (block, window), 1)
    allowed = (ids_col_ref[...] == ids_row_ref[:, pl.ds(start, window)]) & (
        query_index >= key_index
    )
    scores = jnp.where(allowed, scores, -jnp.inf)
    row_max = jnp.max(scores, -1, keepdims=True)
    probs = jnp.exp(scores - row_max)
    denominator = jnp.sum(probs, -1, keepdims=True)
    weighted = jnp.dot(probs.astype(jnp.bfloat16), values, preferred_element_type=jnp.float32)
    out_ref[0] = (weighted / denominator).astype(out_ref.dtype)


def heads_attention_kernel(query, key_nope, key_rope, value, group_ids, score_scale, doc_most):
    heads, total_rows, _ = query.shape
    block = min(256, total_rows)
    window = min(total_rows, doc_most + block)
    kernel = functools.partial(
        attention_kernel, block=block, window=window, doc_most=doc_most, scale=score_scale
    )
    flops = 2 * heads * total_rows * window * (NOPE + ROPE + VDIM)
    return pl.pallas_call(
        kernel,
        grid=(heads, total_rows // block),
        in_specs=[
            pl.BlockSpec((1, block, NOPE + ROPE), lambda h, i: (h, i, 0)),
            pl.BlockSpec((1, total_rows, NOPE), lambda h, i: (h, 0, 0)),
            pl.BlockSpec((total_rows, ROPE), lambda h, i: (0, 0)),
            pl.BlockSpec((1, total_rows, VDIM), lambda h, i: (h, 0, 0)),
            pl.BlockSpec((block, 1), lambda h, i: (i, 0)),
            pl.BlockSpec((1, total_rows), lambda h, i: (0, 0)),
        ],
        out_specs=pl.BlockSpec((1, block, VDIM), lambda h, i: (h, i, 0)),
        out_shape=jax.ShapeDtypeStruct((heads, total_rows, VDIM), jnp.bfloat16),
        cost_estimate=pl.CostEstimate(
            flops=flops,
            transcendentals=heads * total_rows * window,
            bytes_accessed=2 * heads * total_rows * (NOPE + ROPE + NOPE + VDIM + VDIM),
        ),
    )(
        query,
        key_nope,
        key_rope,
        value,
        group_ids.reshape(total_rows, 1),
        group_ids.reshape(1, total_rows),
    )


def body(
    hidden_states,
    input_gain,
    query_down,
    memory_down,
    query_gain,
    memory_gain,
    query_up,
    key_up,
    value_up,
    segment_ids,
):
    tok_count = hidden_states.shape[0]
    seq_count = lax.axis_size("seq")
    tp_count = lax.axis_size("tp")
    seq_index = lax.axis_index("seq")
    tp_index = lax.axis_index("tp")
    width = hidden_states.shape[1] * tp_count
    total_rows = tok_count * seq_count
    doc_most = total_rows // 4
    qrank_piece = query_down.shape[1]
    memory_piece = memory_down.shape[1]
    qrank = qrank_piece * seq_count
    memory_cols = memory_piece * seq_count

    group_ids = lax.all_gather(segment_ids, "seq", axis=0, tiled=True)

    inputs = hidden_states.astype(jnp.float32)
    square_sums = lax.psum(jnp.sum(inputs * inputs, 1), "tp")
    normed = (inputs * lax.rsqrt(square_sums / width + epsilon)[:, None] * input_gain).astype(
        jnp.bfloat16
    )

    dp_index = lax.axis_index("dp")
    dp_count = lax.axis_size("dp")
    down_piece = jnp.concatenate([query_down, memory_down], 1)
    half_rows = down_piece.shape[0] // dp_count
    own_rows = lax.dynamic_slice_in_dim(down_piece, dp_index * half_rows, half_rows, 0)
    own_all = lax.all_gather(own_rows, "seq", axis=1, tiled=True)
    own_all, normed, group_ids = lax.optimization_barrier((own_all, normed, group_ids))
    partial = jnp.dot(
        lax.dynamic_slice_in_dim(normed, dp_index * half_rows, half_rows, 1),
        own_all,
        preferred_element_type=jnp.float32,
    )
    for shift in range(1, dp_count):
        peer = (dp_index + dp_count - shift) % dp_count
        peer_all = lax.ppermute(
            own_all, "dp", perm=[(i, (i + shift) % dp_count) for i in range(dp_count)]
        )
        partial = partial + jnp.dot(
            lax.dynamic_slice_in_dim(normed, peer * half_rows, half_rows, 1),
            peer_all,
            preferred_element_type=jnp.float32,
        )
    latent_rows = lax.psum_scatter(partial, "tp", scatter_dimension=0, tiled=True)

    token_index = jnp.arange(total_rows, dtype=jnp.int32)
    onehot = group_ids[:, None] == jnp.arange(DOCS, dtype=jnp.int32)[None, :]
    starts = jnp.min(jnp.where(onehot, token_index[:, None], total_rows), 0)
    position = token_index - jnp.sum(jnp.where(onehot, starts[None, :], 0), 1)
    chunk = latent_rows.shape[0]
    latent_rows = latent_rows.reshape(chunk, seq_count, qrank_piece + memory_piece)
    query_sums = latent_rows[:, :, :qrank_piece].reshape(chunk, qrank)
    memory_sums = latent_rows[:, :, qrank_piece:].reshape(chunk, memory_cols)
    chunk_position = lax.dynamic_slice(
        position, (seq_index * tok_count + tp_index * chunk,), (chunk,)
    )
    compressed_query = rms_scale(query_sums, query_gain).astype(jnp.bfloat16)
    compressed_memory = rms_scale(memory_sums[:, :KVRANK], memory_gain).astype(jnp.bfloat16)
    key_rope = rotate(memory_sums[:, KVRANK:], chunk_position).astype(jnp.bfloat16)
    def gather_rows(rows):
        rows = lax.all_gather(rows, "seq", axis=0, tiled=False)
        rows = lax.all_gather(rows, "tp", axis=0, tiled=False)
        return jnp.transpose(rows, (1, 0, 2, 3)).reshape(total_rows, rows.shape[-1])

    memory_all = gather_rows(jnp.concatenate([compressed_memory, key_rope], 1))
    cm_all = memory_all[:, :KVRANK]
    rope_all = memory_all[:, KVRANK:]
    cq_all = gather_rows(compressed_query)

    local_heads = query_up.shape[1] // (NOPE + ROPE)
    heads = local_heads // seq_count

    def head_columns(weight, head_width):
        rows = weight.shape[0]
        cols = heads * head_width // dp_count
        own = lax.dynamic_slice_in_dim(
            weight.reshape(rows, seq_count, heads * head_width), dp_index * cols, cols, 2
        )
        own = lax.all_to_all(own, "seq", split_axis=1, concat_axis=0, tiled=True)
        own = own.reshape(rows * seq_count, cols)
        pieces = [own]
        for shift in range(1, dp_count):
            pieces.append(
                lax.ppermute(
                    own, "dp", perm=[(i, (i + shift) % dp_count) for i in range(dp_count)]
                )
            )
        ordered = []
        for core in range(dp_count):
            pick = pieces[0]
            for k in range(1, dp_count):
                pick = jnp.where((dp_index + dp_count - k) % dp_count == core, pieces[k], pick)
            ordered.append(pick)
        return jnp.concatenate(ordered, 1)

    query_w = head_columns(query_up, NOPE + ROPE)
    key_w = head_columns(key_up, NOPE)
    value_w = head_columns(value_up, VDIM)

    query_full = jnp.einsum(
        "td,dhe->hte",
        cq_all,
        query_w.reshape(qrank, heads, NOPE + ROPE),
        preferred_element_type=jnp.float32,
    )
    query = jnp.concatenate(
        [query_full[..., :NOPE], rotate(query_full[..., NOPE:], position[None, :])], -1
    ).astype(jnp.bfloat16)
    key_nope = jnp.einsum(
        "td,dhe->hte", cm_all, key_w.reshape(KVRANK, heads, NOPE), preferred_element_type=jnp.float32
    ).astype(jnp.bfloat16)
    value = jnp.einsum(
        "td,dhe->hte", cm_all, value_w.reshape(KVRANK, heads, VDIM), preferred_element_type=jnp.float32
    ).astype(jnp.bfloat16)
    score_scale = (NOPE + ROPE) ** (-0.5)
    groups = 2 if heads % 2 == 0 else 1
    per_group = heads // groups
    attended = []
    for group in range(groups):
        picked = slice(group * per_group, (group + 1) * per_group)
        head_output = heads_attention_kernel(
            query[picked], key_nope[picked], rope_all, value[picked], group_ids, score_scale, doc_most
        )
        head_output = lax.all_to_all(head_output, "seq", split_axis=1, concat_axis=0, tiled=True)
        attended.append(head_output.reshape(seq_count, per_group, tok_count, VDIM))
    attended = jnp.stack(attended, 1)
    attended = jnp.transpose(attended, (3, 0, 1, 2, 4))
    return attended.reshape(tok_count, local_heads * VDIM)


def solution(mesh):
    in_specs = (
        P(("dp", "seq"), "tp"),
        P("tp"),
        P("tp", "seq"),
        P("tp", "seq"),
        P(),
        P(),
        P("seq", "tp"),
        P("seq", "tp"),
        P("seq", "tp"),
        P(("dp", "seq")),
    )
    out_specs = P(("dp", "seq"), "tp")
    return jax.shard_map(body, mesh=mesh, in_specs=in_specs, out_specs=out_specs, check_vma=False)
```

```python
import functools

import jax
import jax.numpy as jnp
from jax import lax
from jax.experimental import pallas as pl
from jax.experimental.pallas import tpu as pltpu
from jax.sharding import PartitionSpec as P

KVRANK = 512
NOPE = 128
ROPE = 64
VDIM = 128
DOCS = 12


epsilon = 1e-06


def rms_scale(entries, gain_vector):
    return (
        entries * lax.rsqrt(jnp.mean(entries * entries, -1, keepdims=True) + epsilon) * gain_vector
    )


def rotate(entries, position):
    half_width = entries.shape[-1] // 2
    frequency = jnp.power(10000.0, -2.0 * jnp.arange(half_width, dtype=jnp.float32) / ROPE)
    angles = position.astype(jnp.float32)[..., None] * frequency
    cosine = jnp.cos(angles)
    sine_part = jnp.sin(angles)
    first_half = entries[..., :half_width]
    second_half = entries[..., half_width:]
    return jnp.concatenate(
        [
            first_half * cosine - second_half * sine_part,
            second_half * cosine + first_half * sine_part,
        ],
        -1,
    )


def heads_attention(query_all, key_all, value_all, group_ids, score_scale, doc_most):
    total_rows = query_all.shape[0]
    block_rows = min(512, total_rows)
    key_index = jnp.arange(total_rows, dtype=jnp.int32)
    results = []
    for block in range(total_rows // block_rows):
        lower = block * block_rows
        upper = lower + block_rows
        key_low = max(0, lower - doc_most)
        scores = (
            jnp.einsum(
                "qhd,khd->hqk",
                query_all[lower:upper],
                key_all[key_low:upper],
                preferred_element_type=jnp.float32,
            )
            * score_scale
        )
        allowed = (group_ids[lower:upper, None] == group_ids[None, key_low:upper]) & (
            key_index[lower:upper, None] >= key_index[None, key_low:upper]
        )
        scores = jnp.where(allowed[None], scores, -jnp.inf)
        row_max = jnp.max(scores, -1, keepdims=True)
        probs_full = jnp.exp(scores - row_max)
        denominator = jnp.sum(probs_full, -1)
        weights = probs_full.astype(jnp.bfloat16)
        weighted = jnp.einsum(
            "hqk,khd->qhd", weights, value_all[key_low:upper], preferred_element_type=jnp.float32
        )
        results.append((weighted / jnp.transpose(denominator)[:, :, None]).astype(jnp.bfloat16))
    return jnp.concatenate(results, 0)


def attention_kernel(
    query_ref, key_ref, rope_ref, value_ref, ids_col_ref, ids_row_ref, out_ref, *, block, window, doc_most, scale
):
    lower = pl.program_id(1) * block
    start = pl.multiple_of(jnp.maximum(lower - doc_most, 0), block)
    query = query_ref[0]
    keys = key_ref[0, pl.ds(start, window), :]
    rope = rope_ref[pl.ds(start, window), :]
    values = value_ref[0, pl.ds(start, window), :]
    dims = (((1,), (1,)), ((), ()))
    scores = lax.dot_general(query[:, :NOPE], keys, dims, preferred_element_type=jnp.float32)
    scores = scores + lax.dot_general(
        query[:, NOPE:], rope, dims, preferred_element_type=jnp.float32
    )
    scores = scores * scale
    query_index = lower + lax.broadcasted_iota(jnp.int32, (block, window), 0)
    key_index = start + lax.broadcasted_iota(jnp.int32, (block, window), 1)
    allowed = (ids_col_ref[...] == ids_row_ref[:, pl.ds(start, window)]) & (
        query_index >= key_index
    )
    scores = jnp.where(allowed, scores, -jnp.inf)
    row_max = jnp.max(scores, -1, keepdims=True)
    probs = jnp.exp(scores - row_max)
    denominator = jnp.sum(probs, -1, keepdims=True)
    weighted = jnp.dot(probs.astype(jnp.bfloat16), values, preferred_element_type=jnp.float32)
    out_ref[0] = (weighted / denominator).astype(out_ref.dtype)


def heads_attention_kernel(query, key_nope, key_rope, value, group_ids, score_scale, doc_most):
    heads, total_rows, _ = query.shape
    block = min(256, total_rows)
    window = min(total_rows, doc_most + block)
    kernel = functools.partial(
        attention_kernel, block=block, window=window, doc_most=doc_most, scale=score_scale
    )
    flops = 2 * heads * total_rows * window * (NOPE + ROPE + VDIM)
    return pl.pallas_call(
        kernel,
        grid=(heads, total_rows // block),
        in_specs=[
            pl.BlockSpec((1, block, NOPE + ROPE), lambda h, i: (h, i, 0)),
            pl.BlockSpec((1, total_rows, NOPE), lambda h, i: (h, 0, 0)),
            pl.BlockSpec((total_rows, ROPE), lambda h, i: (0, 0)),
            pl.BlockSpec((1, total_rows, VDIM), lambda h, i: (h, 0, 0)),
            pl.BlockSpec((block, 1), lambda h, i: (i, 0)),
            pl.BlockSpec((1, total_rows), lambda h, i: (0, 0)),
        ],
        out_specs=pl.BlockSpec((1, block, VDIM), lambda h, i: (h, i, 0)),
        out_shape=jax.ShapeDtypeStruct((heads, total_rows, VDIM), jnp.bfloat16),
        cost_estimate=pl.CostEstimate(
            flops=flops,
            transcendentals=heads * total_rows * window,
            bytes_accessed=2 * heads * total_rows * (NOPE + ROPE + NOPE + VDIM + VDIM),
        ),
    )(
        query,
        key_nope,
        key_rope,
        value,
        group_ids.reshape(total_rows, 1),
        group_ids.reshape(1, total_rows),
    )


def body(
    hidden_states,
    input_gain,
    query_down,
    memory_down,
    query_gain,
    memory_gain,
    query_up,
    key_up,
    value_up,
    segment_ids,
):
    tok_count = hidden_states.shape[0]
    seq_count = lax.axis_size("seq")
    tp_count = lax.axis_size("tp")
    seq_index = lax.axis_index("seq")
    tp_index = lax.axis_index("tp")
    width = hidden_states.shape[1] * tp_count
    total_rows = tok_count * seq_count
    doc_most = total_rows // 4
    qrank_piece = query_down.shape[1]
    memory_piece = memory_down.shape[1]
    qrank = qrank_piece * seq_count
    memory_cols = memory_piece * seq_count

    group_ids = lax.all_gather(segment_ids, "seq", axis=0, tiled=True)

    inputs = hidden_states.astype(jnp.float32)
    square_sums = lax.psum(jnp.sum(inputs * inputs, 1), "tp")
    normed = (inputs * lax.rsqrt(square_sums / width + epsilon)[:, None] * input_gain).astype(
        jnp.bfloat16
    )

    dp_index = lax.axis_index("dp")
    dp_count = lax.axis_size("dp")
    down_piece = jnp.concatenate([query_down, memory_down], 1)
    half_rows = down_piece.shape[0] // dp_count
    own_rows = lax.dynamic_slice_in_dim(down_piece, dp_index * half_rows, half_rows, 0)
    own_all = lax.all_gather(own_rows, "seq", axis=1, tiled=True)
    own_all, normed, group_ids = lax.optimization_barrier((own_all, normed, group_ids))
    partial = jnp.dot(
        lax.dynamic_slice_in_dim(normed, dp_index * half_rows, half_rows, 1),
        own_all,
        preferred_element_type=jnp.float32,
    )
    for shift in range(1, dp_count):
        peer = (dp_index + dp_count - shift) % dp_count
        peer_all = lax.ppermute(
            own_all, "dp", perm=[(i, (i + shift) % dp_count) for i in range(dp_count)]
        )
        partial = partial + jnp.dot(
            lax.dynamic_slice_in_dim(normed, peer * half_rows, half_rows, 1),
            peer_all,
            preferred_element_type=jnp.float32,
        )
    latent_rows = lax.psum_scatter(partial, "tp", scatter_dimension=0, tiled=True)

    token_index = jnp.arange(total_rows, dtype=jnp.int32)
    onehot = group_ids[:, None] == jnp.arange(DOCS, dtype=jnp.int32)[None, :]
    starts = jnp.min(jnp.where(onehot, token_index[:, None], total_rows), 0)
    position = token_index - jnp.sum(jnp.where(onehot, starts[None, :], 0), 1)
    chunk = latent_rows.shape[0]
    latent_rows = latent_rows.reshape(chunk, seq_count, qrank_piece + memory_piece)
    query_sums = latent_rows[:, :, :qrank_piece].reshape(chunk, qrank)
    memory_sums = latent_rows[:, :, qrank_piece:].reshape(chunk, memory_cols)
    chunk_position = lax.dynamic_slice(
        position, (seq_index * tok_count + tp_index * chunk,), (chunk,)
    )
    compressed_query = rms_scale(query_sums, query_gain).astype(jnp.bfloat16)
    compressed_memory = rms_scale(memory_sums[:, :KVRANK], memory_gain).astype(jnp.bfloat16)
    key_rope = rotate(memory_sums[:, KVRANK:], chunk_position).astype(jnp.bfloat16)
    packed = jnp.concatenate([compressed_query, compressed_memory, key_rope], 1)
    from_seq = [packed] + [
        lax.ppermute(packed, "seq", perm=[(i, (i + k) % seq_count) for i in range(seq_count)])
        for k in range(1, seq_count)
    ]
    packed = jnp.take(jnp.stack(from_seq), (seq_index - jnp.arange(seq_count)) % seq_count, axis=0)
    packed, query_up, key_up, value_up = lax.optimization_barrier(
        (packed, query_up, key_up, value_up)
    )
    packed = lax.all_gather(packed, "tp", axis=0, tiled=False)
    latent = jnp.transpose(packed, (1, 0, 2, 3)).reshape(total_rows, packed.shape[-1])
    cq_all = latent[:, :qrank]
    cm_all = latent[:, qrank : qrank + KVRANK]
    rope_all = latent[:, qrank + KVRANK :]

    local_heads = query_up.shape[1] // (NOPE + ROPE)
    heads = local_heads // seq_count

    def head_columns(weight, head_width):
        rows = weight.shape[0]
        cols = heads * head_width // dp_count
        own = lax.dynamic_slice_in_dim(
            weight.reshape(rows, seq_count, heads * head_width), dp_index * cols, cols, 2
        )
        own = lax.all_to_all(own, "seq", split_axis=1, concat_axis=0, tiled=True)
        own = own.reshape(rows * seq_count, cols)
        pieces = [own]
        for shift in range(1, dp_count):
            pieces.append(
                lax.ppermute(
                    own, "dp", perm=[(i, (i + shift) % dp_count) for i in range(dp_count)]
                )
            )
        ordered = []
        for core in range(dp_count):
            pick = pieces[0]
            for k in range(1, dp_count):
                pick = jnp.where((dp_index + dp_count - k) % dp_count == core, pieces[k], pick)
            ordered.append(pick)
        return jnp.concatenate(ordered, 1)

    query_w = head_columns(query_up, NOPE + ROPE)
    key_w = head_columns(key_up, NOPE)
    value_w = head_columns(value_up, VDIM)

    query_full = jnp.einsum(
        "td,dhe->hte",
        cq_all,
        query_w.reshape(qrank, heads, NOPE + ROPE),
        preferred_element_type=jnp.float32,
    )
    query = jnp.concatenate(
        [query_full[..., :NOPE], rotate(query_full[..., NOPE:], position[None, :])], -1
    ).astype(jnp.bfloat16)
    key_nope = jnp.einsum(
        "td,dhe->hte", cm_all, key_w.reshape(KVRANK, heads, NOPE), preferred_element_type=jnp.float32
    ).astype(jnp.bfloat16)
    value = jnp.einsum(
        "td,dhe->hte", cm_all, value_w.reshape(KVRANK, heads, VDIM), preferred_element_type=jnp.float32
    ).astype(jnp.bfloat16)
    score_scale = (NOPE + ROPE) ** (-0.5)
    head_output = heads_attention_kernel(
        query, key_nope, rope_all, value, group_ids, score_scale, doc_most
    )
    attended = lax.all_to_all(head_output, "seq", split_axis=1, concat_axis=0, tiled=True)
    attended = jnp.transpose(attended, (1, 0, 2))
    return attended.reshape(tok_count, local_heads * VDIM)


def solution(mesh):
    in_specs = (
        P(("dp", "seq"), "tp"),
        P("tp"),
        P("tp", "seq"),
        P("tp", "seq"),
        P(),
        P(),
        P("seq", "tp"),
        P("seq", "tp"),
        P("seq", "tp"),
        P(("dp", "seq")),
    )
    out_specs = P(("dp", "seq"), "tp")
    return jax.shard_map(body, mesh=mesh, in_specs=in_specs, out_specs=out_specs, check_vma=False)
```

```python
import functools

import jax
import jax.numpy as jnp
from jax import lax
from jax.experimental import pallas as pl
from jax.experimental.pallas import tpu as pltpu
from jax.sharding import PartitionSpec as P

KVRANK = 512
NOPE = 128
ROPE = 64
VDIM = 128
DOCS = 12


epsilon = 1e-06


def rms_scale(entries, gain_vector):
    return (
        entries * lax.rsqrt(jnp.mean(entries * entries, -1, keepdims=True) + epsilon) * gain_vector
    )


def rotate(entries, position):
    half_width = entries.shape[-1] // 2
    frequency = jnp.power(10000.0, -2.0 * jnp.arange(half_width, dtype=jnp.float32) / ROPE)
    angles = position.astype(jnp.float32)[..., None] * frequency
    cosine = jnp.cos(angles)
    sine_part = jnp.sin(angles)
    first_half = entries[..., :half_width]
    second_half = entries[..., half_width:]
    return jnp.concatenate(
        [
            first_half * cosine - second_half * sine_part,
            second_half * cosine + first_half * sine_part,
        ],
        -1,
    )


def heads_attention(query_all, key_all, value_all, group_ids, score_scale, doc_most):
    total_rows = query_all.shape[0]
    block_rows = min(512, total_rows)
    key_index = jnp.arange(total_rows, dtype=jnp.int32)
    results = []
    for block in range(total_rows // block_rows):
        lower = block * block_rows
        upper = lower + block_rows
        key_low = max(0, lower - doc_most)
        scores = (
            jnp.einsum(
                "qhd,khd->hqk",
                query_all[lower:upper],
                key_all[key_low:upper],
                preferred_element_type=jnp.float32,
            )
            * score_scale
        )
        allowed = (group_ids[lower:upper, None] == group_ids[None, key_low:upper]) & (
            key_index[lower:upper, None] >= key_index[None, key_low:upper]
        )
        scores = jnp.where(allowed[None], scores, -jnp.inf)
        row_max = jnp.max(scores, -1, keepdims=True)
        probs_full = jnp.exp(scores - row_max)
        denominator = jnp.sum(probs_full, -1)
        weights = probs_full.astype(jnp.bfloat16)
        weighted = jnp.einsum(
            "hqk,khd->qhd", weights, value_all[key_low:upper], preferred_element_type=jnp.float32
        )
        results.append((weighted / jnp.transpose(denominator)[:, :, None]).astype(jnp.bfloat16))
    return jnp.concatenate(results, 0)


def attention_kernel(
    block_ref, query_ref, key_ref, rope_ref, value_ref, ids_col_ref, ids_row_ref, out_ref, *, block, window, doc_most, scale
):
    lower = block_ref[0] * block
    start = pl.multiple_of(jnp.maximum(lower - doc_most, 0), block)
    query = query_ref[0]
    keys = key_ref[0, pl.ds(start, window), :]
    rope = rope_ref[pl.ds(start, window), :]
    values = value_ref[0, pl.ds(start, window), :]
    dims = (((1,), (1,)), ((), ()))
    scores = lax.dot_general(query[:, :NOPE], keys, dims, preferred_element_type=jnp.float32)
    scores = scores + lax.dot_general(
        query[:, NOPE:], rope, dims, preferred_element_type=jnp.float32
    )
    scores = scores * scale
    query_index = lower + lax.broadcasted_iota(jnp.int32, (block, window), 0)
    key_index = start + lax.broadcasted_iota(jnp.int32, (block, window), 1)
    allowed = (ids_col_ref[...] == ids_row_ref[:, pl.ds(start, window)]) & (
        query_index >= key_index
    )
    scores = jnp.where(allowed, scores, -jnp.inf)
    row_max = jnp.max(scores, -1, keepdims=True)
    probs = jnp.exp(scores - row_max)
    denominator = jnp.sum(probs, -1, keepdims=True)
    weighted = jnp.dot(probs.astype(jnp.bfloat16), values, preferred_element_type=jnp.float32)
    out_ref[0] = (weighted / denominator).astype(out_ref.dtype)


def block_attention(query, key_nope, key_rope, value, group_ids, score_scale, doc_most, block, index):
    heads, total_rows, _ = query.shape
    window = min(total_rows, doc_most + block)
    kernel = functools.partial(
        attention_kernel, block=block, window=window, doc_most=doc_most, scale=score_scale
    )
    flops = 2 * heads * block * window * (NOPE + ROPE + VDIM)
    return pl.pallas_call(
        kernel,
        grid_spec=pltpu.PrefetchScalarGridSpec(
            num_scalar_prefetch=1,
            grid=(heads,),
            in_specs=[
                pl.BlockSpec((1, block, NOPE + ROPE), lambda h, b: (h, b[0], 0)),
                pl.BlockSpec((1, total_rows, NOPE), lambda h, b: (h, 0, 0)),
                pl.BlockSpec((total_rows, ROPE), lambda h, b: (0, 0)),
                pl.BlockSpec((1, total_rows, VDIM), lambda h, b: (h, 0, 0)),
                pl.BlockSpec((block, 1), lambda h, b: (b[0], 0)),
                pl.BlockSpec((1, total_rows), lambda h, b: (0, 0)),
            ],
            out_specs=pl.BlockSpec((1, block, VDIM), lambda h, b: (h, 0, 0)),
        ),
        out_shape=jax.ShapeDtypeStruct((heads, block, VDIM), jnp.bfloat16),
        cost_estimate=pl.CostEstimate(
            flops=flops,
            transcendentals=heads * block * window,
            bytes_accessed=2 * heads * (block * (NOPE + ROPE + VDIM) + window * (NOPE + VDIM)),
        ),
    )(
        jnp.reshape(index, (1,)).astype(jnp.int32),
        query,
        key_nope,
        key_rope,
        value,
        group_ids.reshape(total_rows, 1),
        group_ids.reshape(1, total_rows),
    )


def body(
    hidden_states,
    input_gain,
    query_down,
    memory_down,
    query_gain,
    memory_gain,
    query_up,
    key_up,
    value_up,
    segment_ids,
):
    tok_count = hidden_states.shape[0]
    seq_count = lax.axis_size("seq")
    tp_count = lax.axis_size("tp")
    seq_index = lax.axis_index("seq")
    tp_index = lax.axis_index("tp")
    width = hidden_states.shape[1] * tp_count
    total_rows = tok_count * seq_count
    doc_most = total_rows // 4
    qrank_piece = query_down.shape[1]
    memory_piece = memory_down.shape[1]
    qrank = qrank_piece * seq_count
    memory_cols = memory_piece * seq_count

    group_ids = lax.all_gather(segment_ids, "seq", axis=0, tiled=True)

    inputs = hidden_states.astype(jnp.float32)
    square_sums = lax.psum(jnp.sum(inputs * inputs, 1), "tp")
    normed = (inputs * lax.rsqrt(square_sums / width + epsilon)[:, None] * input_gain).astype(
        jnp.bfloat16
    )

    dp_index = lax.axis_index("dp")
    dp_count = lax.axis_size("dp")
    down_piece = jnp.concatenate([query_down, memory_down], 1)
    half_rows = down_piece.shape[0] // dp_count
    own_rows = lax.dynamic_slice_in_dim(down_piece, dp_index * half_rows, half_rows, 0)
    own_all = lax.all_gather(own_rows, "seq", axis=1, tiled=True)
    own_all, normed, group_ids = lax.optimization_barrier((own_all, normed, group_ids))
    partial = jnp.dot(
        lax.dynamic_slice_in_dim(normed, dp_index * half_rows, half_rows, 1),
        own_all,
        preferred_element_type=jnp.float32,
    )
    for shift in range(1, dp_count):
        peer = (dp_index + dp_count - shift) % dp_count
        peer_all = lax.ppermute(
            own_all, "dp", perm=[(i, (i + shift) % dp_count) for i in range(dp_count)]
        )
        partial = partial + jnp.dot(
            lax.dynamic_slice_in_dim(normed, peer * half_rows, half_rows, 1),
            peer_all,
            preferred_element_type=jnp.float32,
        )
    latent_rows = lax.psum_scatter(partial, "tp", scatter_dimension=0, tiled=True)

    token_index = jnp.arange(total_rows, dtype=jnp.int32)
    onehot = group_ids[:, None] == jnp.arange(DOCS, dtype=jnp.int32)[None, :]
    starts = jnp.min(jnp.where(onehot, token_index[:, None], total_rows), 0)
    position = token_index - jnp.sum(jnp.where(onehot, starts[None, :], 0), 1)
    chunk = latent_rows.shape[0]
    latent_rows = latent_rows.reshape(chunk, seq_count, qrank_piece + memory_piece)
    query_sums = latent_rows[:, :, :qrank_piece].reshape(chunk, qrank)
    memory_sums = latent_rows[:, :, qrank_piece:].reshape(chunk, memory_cols)
    chunk_position = lax.dynamic_slice(
        position, (seq_index * tok_count + tp_index * chunk,), (chunk,)
    )
    compressed_query = rms_scale(query_sums, query_gain).astype(jnp.bfloat16)
    compressed_memory = rms_scale(memory_sums[:, :KVRANK], memory_gain).astype(jnp.bfloat16)
    key_rope = rotate(memory_sums[:, KVRANK:], chunk_position).astype(jnp.bfloat16)
    packed = jnp.concatenate([compressed_query, compressed_memory, key_rope], 1)
    from_seq = [packed] + [
        lax.ppermute(packed, "seq", perm=[(i, (i + k) % seq_count) for i in range(seq_count)])
        for k in range(1, seq_count)
    ]
    packed = jnp.take(jnp.stack(from_seq), (seq_index - jnp.arange(seq_count)) % seq_count, axis=0)
    packed, query_up, key_up, value_up = lax.optimization_barrier(
        (packed, query_up, key_up, value_up)
    )
    packed = lax.all_gather(packed, "tp", axis=0, tiled=False)
    latent = jnp.transpose(packed, (1, 0, 2, 3)).reshape(total_rows, packed.shape[-1])
    cq_all = latent[:, :qrank]
    cm_all = latent[:, qrank : qrank + KVRANK]
    rope_all = latent[:, qrank + KVRANK :]

    local_heads = query_up.shape[1] // (NOPE + ROPE)
    heads = local_heads // seq_count

    def head_columns(weight, head_width):
        rows = weight.shape[0]
        cols = heads * head_width // dp_count
        own = lax.dynamic_slice_in_dim(
            weight.reshape(rows, seq_count, heads * head_width), dp_index * cols, cols, 2
        )
        own = lax.all_to_all(own, "seq", split_axis=1, concat_axis=0, tiled=True)
        own = own.reshape(rows * seq_count, cols)
        pieces = [own]
        for shift in range(1, dp_count):
            pieces.append(
                lax.ppermute(
                    own, "dp", perm=[(i, (i + shift) % dp_count) for i in range(dp_count)]
                )
            )
        ordered = []
        for core in range(dp_count):
            pick = pieces[0]
            for k in range(1, dp_count):
                pick = jnp.where((dp_index + dp_count - k) % dp_count == core, pieces[k], pick)
            ordered.append(pick)
        return jnp.concatenate(ordered, 1)

    query_w = head_columns(query_up, NOPE + ROPE)
    key_w = head_columns(key_up, NOPE)
    value_w = head_columns(value_up, VDIM)

    query_full = jnp.einsum(
        "td,dhe->hte",
        cq_all,
        query_w.reshape(qrank, heads, NOPE + ROPE),
        preferred_element_type=jnp.float32,
    )
    query = jnp.concatenate(
        [query_full[..., :NOPE], rotate(query_full[..., NOPE:], position[None, :])], -1
    ).astype(jnp.bfloat16)
    key_nope = jnp.einsum(
        "td,dhe->hte", cm_all, key_w.reshape(KVRANK, heads, NOPE), preferred_element_type=jnp.float32
    ).astype(jnp.bfloat16)
    value = jnp.einsum(
        "td,dhe->hte", cm_all, value_w.reshape(KVRANK, heads, VDIM), preferred_element_type=jnp.float32
    ).astype(jnp.bfloat16)
    score_scale = (NOPE + ROPE) ** (-0.5)
    received = [None] * seq_count
    for k in list(range(1, seq_count)) + [0]:
        rows = block_attention(
            query, key_nope, rope_all, value, group_ids, score_scale, doc_most, tok_count,
            (seq_index + k) % seq_count,
        )
        if k:
            rows = lax.ppermute(
                rows, "seq", perm=[(i, (i + k) % seq_count) for i in range(seq_count)]
            )
        received[k] = rows
    attended = jnp.take(
        jnp.stack(received), (seq_index - jnp.arange(seq_count)) % seq_count, axis=0
    )
    attended = jnp.transpose(attended, (2, 0, 1, 3))
    return attended.reshape(tok_count, local_heads * VDIM)


def solution(mesh):
    in_specs = (
        P(("dp", "seq"), "tp"),
        P("tp"),
        P("tp", "seq"),
        P("tp", "seq"),
        P(),
        P(),
        P("seq", "tp"),
        P("seq", "tp"),
        P("seq", "tp"),
        P(("dp", "seq")),
    )
    out_specs = P(("dp", "seq"), "tp")
    return jax.shard_map(body, mesh=mesh, in_specs=in_specs, out_specs=out_specs, check_vma=False)
```

```python
import functools

import jax
import jax.numpy as jnp
from jax import lax
from jax.experimental import pallas as pl
from jax.experimental.pallas import tpu as pltpu
from jax.sharding import PartitionSpec as P

KVRANK = 512
NOPE = 128
ROPE = 64
VDIM = 128
DOCS = 12


epsilon = 1e-06


def rms_scale(entries, gain_vector):
    return (
        entries * lax.rsqrt(jnp.mean(entries * entries, -1, keepdims=True) + epsilon) * gain_vector
    )


def rotate(entries, position):
    half_width = entries.shape[-1] // 2
    frequency = jnp.power(10000.0, -2.0 * jnp.arange(half_width, dtype=jnp.float32) / ROPE)
    angles = position.astype(jnp.float32)[..., None] * frequency
    cosine = jnp.cos(angles)
    sine_part = jnp.sin(angles)
    first_half = entries[..., :half_width]
    second_half = entries[..., half_width:]
    return jnp.concatenate(
        [
            first_half * cosine - second_half * sine_part,
            second_half * cosine + first_half * sine_part,
        ],
        -1,
    )


def heads_attention(query_all, key_all, value_all, group_ids, score_scale, doc_most):
    total_rows = query_all.shape[0]
    block_rows = min(512, total_rows)
    key_index = jnp.arange(total_rows, dtype=jnp.int32)
    results = []
    for block in range(total_rows // block_rows):
        lower = block * block_rows
        upper = lower + block_rows
        key_low = max(0, lower - doc_most)
        scores = (
            jnp.einsum(
                "qhd,khd->hqk",
                query_all[lower:upper],
                key_all[key_low:upper],
                preferred_element_type=jnp.float32,
            )
            * score_scale
        )
        allowed = (group_ids[lower:upper, None] == group_ids[None, key_low:upper]) & (
            key_index[lower:upper, None] >= key_index[None, key_low:upper]
        )
        scores = jnp.where(allowed[None], scores, -jnp.inf)
        row_max = jnp.max(scores, -1, keepdims=True)
        probs_full = jnp.exp(scores - row_max)
        denominator = jnp.sum(probs_full, -1)
        weights = probs_full.astype(jnp.bfloat16)
        weighted = jnp.einsum(
            "hqk,khd->qhd", weights, value_all[key_low:upper], preferred_element_type=jnp.float32
        )
        results.append((weighted / jnp.transpose(denominator)[:, :, None]).astype(jnp.bfloat16))
    return jnp.concatenate(results, 0)


def attention_kernel(
    block_ref, query_ref, key_ref, rope_ref, value_ref, ids_col_ref, ids_row_ref, out_ref, bias_ref, *, block, window, doc_most, scale
):
    lower = block_ref[0] * block
    start = pl.multiple_of(jnp.maximum(lower - doc_most, 0), block)

    @pl.when(pl.program_id(0) == 0)
    def _():
        query_index = lower + lax.broadcasted_iota(jnp.int32, (block, window), 0)
        key_index = start + lax.broadcasted_iota(jnp.int32, (block, window), 1)
        allowed = (ids_col_ref[...] == ids_row_ref[:, pl.ds(start, window)]) & (
            query_index >= key_index
        )
        bias_ref[...] = jnp.where(allowed, 0.0, -jnp.inf).astype(jnp.float32)

    query = query_ref[0]
    keys = key_ref[0, pl.ds(start, window), :]
    rope = rope_ref[pl.ds(start, window), :]
    values = value_ref[0, pl.ds(start, window), :]
    dims = (((1,), (1,)), ((), ()))
    scores = lax.dot_general(query[:, :NOPE], keys, dims, preferred_element_type=jnp.float32)
    scores = scores + lax.dot_general(
        query[:, NOPE:], rope, dims, preferred_element_type=jnp.float32
    )
    scores = scores * scale + bias_ref[...]
    row_max = jnp.max(scores, -1, keepdims=True)
    probs = jnp.exp(scores - row_max)
    denominator = jnp.sum(probs, -1, keepdims=True)
    weighted = jnp.dot(probs.astype(jnp.bfloat16), values, preferred_element_type=jnp.float32)
    out_ref[0] = (weighted / denominator).astype(out_ref.dtype)


def block_attention(query, key_nope, key_rope, value, group_ids, score_scale, doc_most, block, index):
    heads, total_rows, _ = query.shape
    window = min(total_rows, doc_most + block)
    kernel = functools.partial(
        attention_kernel, block=block, window=window, doc_most=doc_most, scale=score_scale
    )
    flops = 2 * heads * block * window * (NOPE + ROPE + VDIM)
    return pl.pallas_call(
        kernel,
        grid_spec=pltpu.PrefetchScalarGridSpec(
            num_scalar_prefetch=1,
            grid=(heads,),
            in_specs=[
                pl.BlockSpec((1, block, NOPE + ROPE), lambda h, b: (h, b[0], 0)),
                pl.BlockSpec((1, total_rows, NOPE), lambda h, b: (h, 0, 0)),
                pl.BlockSpec((total_rows, ROPE), lambda h, b: (0, 0)),
                pl.BlockSpec((1, total_rows, VDIM), lambda h, b: (h, 0, 0)),
                pl.BlockSpec((block, 1), lambda h, b: (b[0], 0)),
                pl.BlockSpec((1, total_rows), lambda h, b: (0, 0)),
            ],
            out_specs=pl.BlockSpec((1, block, VDIM), lambda h, b: (h, 0, 0)),
            scratch_shapes=[pltpu.VMEM((block, window), jnp.float32)],
        ),
        out_shape=jax.ShapeDtypeStruct((heads, block, VDIM), jnp.bfloat16),
        cost_estimate=pl.CostEstimate(
            flops=flops,
            transcendentals=heads * block * window,
            bytes_accessed=2 * heads * (block * (NOPE + ROPE + VDIM) + window * (NOPE + VDIM)),
        ),
    )(
        jnp.reshape(index, (1,)).astype(jnp.int32),
        query,
        key_nope,
        key_rope,
        value,
        group_ids.reshape(total_rows, 1),
        group_ids.reshape(1, total_rows),
    )


def body(
    hidden_states,
    input_gain,
    query_down,
    memory_down,
    query_gain,
    memory_gain,
    query_up,
    key_up,
    value_up,
    segment_ids,
):
    tok_count = hidden_states.shape[0]
    seq_count = lax.axis_size("seq")
    tp_count = lax.axis_size("tp")
    seq_index = lax.axis_index("seq")
    tp_index = lax.axis_index("tp")
    width = hidden_states.shape[1] * tp_count
    total_rows = tok_count * seq_count
    doc_most = total_rows // 4
    qrank_piece = query_down.shape[1]
    memory_piece = memory_down.shape[1]
    qrank = qrank_piece * seq_count
    memory_cols = memory_piece * seq_count

    group_ids = lax.all_gather(segment_ids, "seq", axis=0, tiled=True)

    inputs = hidden_states.astype(jnp.float32)
    square_sums = lax.psum(jnp.sum(inputs * inputs, 1), "tp")
    normed = (inputs * lax.rsqrt(square_sums / width + epsilon)[:, None] * input_gain).astype(
        jnp.bfloat16
    )

    dp_index = lax.axis_index("dp")
    dp_count = lax.axis_size("dp")
    down_piece = jnp.concatenate([query_down, memory_down], 1)
    half_rows = down_piece.shape[0] // dp_count
    own_rows = lax.dynamic_slice_in_dim(down_piece, dp_index * half_rows, half_rows, 0)
    own_all = lax.all_gather(own_rows, "seq", axis=1, tiled=True)
    own_all, normed, group_ids = lax.optimization_barrier((own_all, normed, group_ids))
    partial = jnp.dot(
        lax.dynamic_slice_in_dim(normed, dp_index * half_rows, half_rows, 1),
        own_all,
        preferred_element_type=jnp.float32,
    )
    for shift in range(1, dp_count):
        peer = (dp_index + dp_count - shift) % dp_count
        peer_all = lax.ppermute(
            own_all, "dp", perm=[(i, (i + shift) % dp_count) for i in range(dp_count)]
        )
        partial = partial + jnp.dot(
            lax.dynamic_slice_in_dim(normed, peer * half_rows, half_rows, 1),
            peer_all,
            preferred_element_type=jnp.float32,
        )
    latent_rows = lax.psum_scatter(partial, "tp", scatter_dimension=0, tiled=True)

    token_index = jnp.arange(total_rows, dtype=jnp.int32)
    onehot = group_ids[:, None] == jnp.arange(DOCS, dtype=jnp.int32)[None, :]
    starts = jnp.min(jnp.where(onehot, token_index[:, None], total_rows), 0)
    position = token_index - jnp.sum(jnp.where(onehot, starts[None, :], 0), 1)
    chunk = latent_rows.shape[0]
    latent_rows = latent_rows.reshape(chunk, seq_count, qrank_piece + memory_piece)
    query_sums = latent_rows[:, :, :qrank_piece].reshape(chunk, qrank)
    memory_sums = latent_rows[:, :, qrank_piece:].reshape(chunk, memory_cols)
    chunk_position = lax.dynamic_slice(
        position, (seq_index * tok_count + tp_index * chunk,), (chunk,)
    )
    compressed_query = rms_scale(query_sums, query_gain).astype(jnp.bfloat16)
    compressed_memory = rms_scale(memory_sums[:, :KVRANK], memory_gain).astype(jnp.bfloat16)
    key_rope = rotate(memory_sums[:, KVRANK:], chunk_position).astype(jnp.bfloat16)
    packed = jnp.concatenate([compressed_query, compressed_memory, key_rope], 1)
    from_seq = [packed] + [
        lax.ppermute(packed, "seq", perm=[(i, (i + k) % seq_count) for i in range(seq_count)])
        for k in range(1, seq_count)
    ]
    packed = jnp.take(jnp.stack(from_seq), (seq_index - jnp.arange(seq_count)) % seq_count, axis=0)
    packed, query_up, key_up, value_up = lax.optimization_barrier(
        (packed, query_up, key_up, value_up)
    )
    packed = lax.all_gather(packed, "tp", axis=0, tiled=False)
    latent = jnp.transpose(packed, (1, 0, 2, 3)).reshape(total_rows, packed.shape[-1])
    cq_all = latent[:, :qrank]
    cm_all = latent[:, qrank : qrank + KVRANK]
    rope_all = latent[:, qrank + KVRANK :]

    local_heads = query_up.shape[1] // (NOPE + ROPE)
    heads = local_heads // seq_count

    def head_columns(weight, head_width):
        rows = weight.shape[0]
        cols = heads * head_width // dp_count
        own = lax.dynamic_slice_in_dim(
            weight.reshape(rows, seq_count, heads * head_width), dp_index * cols, cols, 2
        )
        own = lax.all_to_all(own, "seq", split_axis=1, concat_axis=0, tiled=True)
        own = own.reshape(rows * seq_count, cols)
        pieces = [own]
        for shift in range(1, dp_count):
            pieces.append(
                lax.ppermute(
                    own, "dp", perm=[(i, (i + shift) % dp_count) for i in range(dp_count)]
                )
            )
        ordered = []
        for core in range(dp_count):
            pick = pieces[0]
            for k in range(1, dp_count):
                pick = jnp.where((dp_index + dp_count - k) % dp_count == core, pieces[k], pick)
            ordered.append(pick)
        return jnp.concatenate(ordered, 1)

    query_w = head_columns(query_up, NOPE + ROPE)
    key_w = head_columns(key_up, NOPE)
    value_w = head_columns(value_up, VDIM)

    query_full = jnp.einsum(
        "td,dhe->hte",
        cq_all,
        query_w.reshape(qrank, heads, NOPE + ROPE),
        preferred_element_type=jnp.float32,
    )
    query = jnp.concatenate(
        [query_full[..., :NOPE], rotate(query_full[..., NOPE:], position[None, :])], -1
    ).astype(jnp.bfloat16)
    key_nope = jnp.einsum(
        "td,dhe->hte", cm_all, key_w.reshape(KVRANK, heads, NOPE), preferred_element_type=jnp.float32
    ).astype(jnp.bfloat16)
    value = jnp.einsum(
        "td,dhe->hte", cm_all, value_w.reshape(KVRANK, heads, VDIM), preferred_element_type=jnp.float32
    ).astype(jnp.bfloat16)
    score_scale = (NOPE + ROPE) ** (-0.5)
    received = [None] * seq_count
    for k in list(range(1, seq_count)) + [0]:
        rows = block_attention(
            query, key_nope, rope_all, value, group_ids, score_scale, doc_most, tok_count,
            (seq_index + k) % seq_count,
        )
        if k:
            rows = lax.ppermute(
                rows, "seq", perm=[(i, (i + k) % seq_count) for i in range(seq_count)]
            )
        received[k] = rows
    attended = jnp.take(
        jnp.stack(received), (seq_index - jnp.arange(seq_count)) % seq_count, axis=0
    )
    attended = jnp.transpose(attended, (2, 0, 1, 3))
    return attended.reshape(tok_count, local_heads * VDIM)


def solution(mesh):
    in_specs = (
        P(("dp", "seq"), "tp"),
        P("tp"),
        P("tp", "seq"),
        P("tp", "seq"),
        P(),
        P(),
        P("seq", "tp"),
        P("seq", "tp"),
        P("seq", "tp"),
        P(("dp", "seq")),
    )
    out_specs = P(("dp", "seq"), "tp")
    return jax.shard_map(body, mesh=mesh, in_specs=in_specs, out_specs=out_specs, check_vma=False)
```

```python
import functools

import jax
import jax.numpy as jnp
from jax import lax
from jax.experimental import pallas as pl
from jax.experimental.pallas import tpu as pltpu
from jax.sharding import PartitionSpec as P

KVRANK = 512
NOPE = 128
ROPE = 64
VDIM = 128
DOCS = 12


epsilon = 1e-06


def rms_scale(entries, gain_vector):
    return (
        entries * lax.rsqrt(jnp.mean(entries * entries, -1, keepdims=True) + epsilon) * gain_vector
    )


def rotate(entries, position):
    half_width = entries.shape[-1] // 2
    frequency = jnp.power(10000.0, -2.0 * jnp.arange(half_width, dtype=jnp.float32) / ROPE)
    angles = position.astype(jnp.float32)[..., None] * frequency
    cosine = jnp.cos(angles)
    sine_part = jnp.sin(angles)
    first_half = entries[..., :half_width]
    second_half = entries[..., half_width:]
    return jnp.concatenate(
        [
            first_half * cosine - second_half * sine_part,
            second_half * cosine + first_half * sine_part,
        ],
        -1,
    )


def heads_attention(query_all, key_all, value_all, group_ids, score_scale, doc_most):
    total_rows = query_all.shape[0]
    block_rows = min(512, total_rows)
    key_index = jnp.arange(total_rows, dtype=jnp.int32)
    results = []
    for block in range(total_rows // block_rows):
        lower = block * block_rows
        upper = lower + block_rows
        key_low = max(0, lower - doc_most)
        scores = (
            jnp.einsum(
                "qhd,khd->hqk",
                query_all[lower:upper],
                key_all[key_low:upper],
                preferred_element_type=jnp.float32,
            )
            * score_scale
        )
        allowed = (group_ids[lower:upper, None] == group_ids[None, key_low:upper]) & (
            key_index[lower:upper, None] >= key_index[None, key_low:upper]
        )
        scores = jnp.where(allowed[None], scores, -jnp.inf)
        row_max = jnp.max(scores, -1, keepdims=True)
        probs_full = jnp.exp(scores - row_max)
        denominator = jnp.sum(probs_full, -1)
        weights = probs_full.astype(jnp.bfloat16)
        weighted = jnp.einsum(
            "hqk,khd->qhd", weights, value_all[key_low:upper], preferred_element_type=jnp.float32
        )
        results.append((weighted / jnp.transpose(denominator)[:, :, None]).astype(jnp.bfloat16))
    return jnp.concatenate(results, 0)


def attention_kernel(
    block_ref, query_ref, key_ref, rope_ref, value_ref, ids_col_ref, ids_row_ref, out_ref, bias_ref, *, block, window, doc_most, scale
):
    lower = block_ref[0] * block
    start = pl.multiple_of(jnp.maximum(lower - doc_most, 0), block)

    @pl.when(pl.program_id(0) == 0)
    def _():
        query_index = lower + lax.broadcasted_iota(jnp.int32, (block, window), 0)
        key_index = start + lax.broadcasted_iota(jnp.int32, (block, window), 1)
        allowed = (ids_col_ref[...] == ids_row_ref[:, pl.ds(start, window)]) & (
            query_index >= key_index
        )
        bias_ref[...] = jnp.where(allowed, 0.0, -jnp.inf).astype(jnp.float32)

    query = query_ref[0]
    keys = key_ref[0, pl.ds(start, window), :]
    rope = rope_ref[pl.ds(start, window), :]
    values = value_ref[0, pl.ds(start, window), :]
    dims = (((1,), (1,)), ((), ()))
    scores = lax.dot_general(query[:, :NOPE], keys, dims, preferred_element_type=jnp.float32)
    scores = scores + lax.dot_general(
        query[:, NOPE:], rope, dims, preferred_element_type=jnp.float32
    )
    scores = scores * scale + bias_ref[...]
    row_max = jnp.max(scores, -1, keepdims=True)
    probs = jnp.exp(scores - row_max)
    denominator = jnp.sum(probs, -1, keepdims=True)
    weighted = jnp.dot(probs.astype(jnp.bfloat16), values, preferred_element_type=jnp.float32)
    out_ref[0] = (weighted / denominator).astype(out_ref.dtype)


def block_attention(query, key_nope, key_rope, value, group_ids, score_scale, doc_most, block, index):
    heads, total_rows, _ = query.shape
    window = min(total_rows, doc_most + block)
    kernel = functools.partial(
        attention_kernel, block=block, window=window, doc_most=doc_most, scale=score_scale
    )
    flops = 2 * heads * block * window * (NOPE + ROPE + VDIM)
    return pl.pallas_call(
        kernel,
        grid_spec=pltpu.PrefetchScalarGridSpec(
            num_scalar_prefetch=1,
            grid=(heads,),
            in_specs=[
                pl.BlockSpec((1, block, NOPE + ROPE), lambda h, b: (h, b[0], 0)),
                pl.BlockSpec((1, total_rows, NOPE), lambda h, b: (h, 0, 0)),
                pl.BlockSpec((total_rows, ROPE), lambda h, b: (0, 0)),
                pl.BlockSpec((1, total_rows, VDIM), lambda h, b: (h, 0, 0)),
                pl.BlockSpec((block, 1), lambda h, b: (b[0], 0)),
                pl.BlockSpec((1, total_rows), lambda h, b: (0, 0)),
            ],
            out_specs=pl.BlockSpec((1, block, VDIM), lambda h, b: (h, 0, 0)),
            scratch_shapes=[pltpu.VMEM((block, window), jnp.float32)],
        ),
        out_shape=jax.ShapeDtypeStruct((heads, block, VDIM), jnp.bfloat16),
        cost_estimate=pl.CostEstimate(
            flops=flops,
            transcendentals=heads * block * window,
            bytes_accessed=2 * heads * (block * (NOPE + ROPE + VDIM) + window * (NOPE + VDIM)),
        ),
    )(
        jnp.reshape(index, (1,)).astype(jnp.int32),
        query,
        key_nope,
        key_rope,
        value,
        group_ids.reshape(total_rows, 1),
        group_ids.reshape(1, total_rows),
    )


def body(
    hidden_states,
    input_gain,
    query_down,
    memory_down,
    query_gain,
    memory_gain,
    query_up,
    key_up,
    value_up,
    segment_ids,
):
    tok_count = hidden_states.shape[0]
    seq_count = lax.axis_size("seq")
    tp_count = lax.axis_size("tp")
    seq_index = lax.axis_index("seq")
    tp_index = lax.axis_index("tp")
    width = hidden_states.shape[1] * tp_count
    total_rows = tok_count * seq_count
    doc_most = total_rows // 4
    qrank_piece = query_down.shape[1]
    memory_piece = memory_down.shape[1]
    qrank = qrank_piece * seq_count
    memory_cols = memory_piece * seq_count

    group_ids = lax.all_gather(segment_ids, "seq", axis=0, tiled=True)

    inputs = hidden_states.astype(jnp.float32)
    square_sums = lax.psum(jnp.sum(inputs * inputs, 1), "tp")
    normed = (inputs * lax.rsqrt(square_sums / width + epsilon)[:, None] * input_gain).astype(
        jnp.bfloat16
    )

    dp_index = lax.axis_index("dp")
    dp_count = lax.axis_size("dp")
    down_piece = jnp.concatenate([query_down, memory_down], 1)
    half_rows = down_piece.shape[0] // dp_count
    own_rows = lax.dynamic_slice_in_dim(down_piece, dp_index * half_rows, half_rows, 0)
    own_all = lax.all_gather(own_rows, "seq", axis=1, tiled=True)
    own_all, normed, group_ids = lax.optimization_barrier((own_all, normed, group_ids))
    partial = jnp.dot(
        lax.dynamic_slice_in_dim(normed, dp_index * half_rows, half_rows, 1),
        own_all,
        preferred_element_type=jnp.float32,
    )
    for shift in range(1, dp_count):
        peer = (dp_index + dp_count - shift) % dp_count
        peer_all = lax.ppermute(
            own_all, "dp", perm=[(i, (i + shift) % dp_count) for i in range(dp_count)]
        )
        partial = partial + jnp.dot(
            lax.dynamic_slice_in_dim(normed, peer * half_rows, half_rows, 1),
            peer_all,
            preferred_element_type=jnp.float32,
        )
    latent_rows = lax.psum_scatter(partial, "tp", scatter_dimension=0, tiled=True)

    token_index = jnp.arange(total_rows, dtype=jnp.int32)
    onehot = group_ids[:, None] == jnp.arange(DOCS, dtype=jnp.int32)[None, :]
    starts = jnp.min(jnp.where(onehot, token_index[:, None], total_rows), 0)
    position = token_index - jnp.sum(jnp.where(onehot, starts[None, :], 0), 1)
    chunk = latent_rows.shape[0]
    latent_rows = latent_rows.reshape(chunk, seq_count, qrank_piece + memory_piece)
    query_sums = latent_rows[:, :, :qrank_piece].reshape(chunk, qrank)
    memory_sums = latent_rows[:, :, qrank_piece:].reshape(chunk, memory_cols)
    chunk_position = lax.dynamic_slice(
        position, (seq_index * tok_count + tp_index * chunk,), (chunk,)
    )
    compressed_query = rms_scale(query_sums, query_gain).astype(jnp.bfloat16)
    compressed_memory = rms_scale(memory_sums[:, :KVRANK], memory_gain).astype(jnp.bfloat16)
    key_rope = rotate(memory_sums[:, KVRANK:], chunk_position).astype(jnp.bfloat16)
    packed = jnp.concatenate([compressed_query, compressed_memory, key_rope], 1)
    from_seq = [packed] + [
        lax.ppermute(packed, "seq", perm=[(i, (i + k) % seq_count) for i in range(seq_count)])
        for k in range(1, seq_count)
    ]
    packed = jnp.take(jnp.stack(from_seq), (seq_index - jnp.arange(seq_count)) % seq_count, axis=0)
    packed, query_up, key_up, value_up = lax.optimization_barrier(
        (packed, query_up, key_up, value_up)
    )
    packed = lax.all_gather(packed, "tp", axis=0, tiled=False)
    latent = jnp.transpose(packed, (1, 0, 2, 3)).reshape(total_rows, packed.shape[-1])
    cq_all = latent[:, :qrank]
    cm_all = latent[:, qrank : qrank + KVRANK]
    rope_all = latent[:, qrank + KVRANK :]

    local_heads = query_up.shape[1] // (NOPE + ROPE)
    heads = local_heads // seq_count

    def head_columns(weight, head_width):
        rows = weight.shape[0]
        cols = heads * head_width // dp_count
        own = lax.dynamic_slice_in_dim(
            weight.reshape(rows, seq_count, heads * head_width), dp_index * cols, cols, 2
        )
        own = lax.all_to_all(own, "seq", split_axis=1, concat_axis=0, tiled=True)
        own = own.reshape(rows * seq_count, cols)
        pieces = [own]
        for shift in range(1, dp_count):
            pieces.append(
                lax.ppermute(
                    own, "dp", perm=[(i, (i + shift) % dp_count) for i in range(dp_count)]
                )
            )
        ordered = []
        for core in range(dp_count):
            pick = pieces[0]
            for k in range(1, dp_count):
                pick = jnp.where((dp_index + dp_count - k) % dp_count == core, pieces[k], pick)
            ordered.append(pick)
        return jnp.concatenate(ordered, 1)

    query_w = head_columns(query_up, NOPE + ROPE)
    key_w = head_columns(key_up, NOPE)
    value_w = head_columns(value_up, VDIM)

    query_full = jnp.einsum(
        "td,dhe->hte",
        cq_all,
        query_w.reshape(qrank, heads, NOPE + ROPE),
        preferred_element_type=jnp.float32,
    )
    query = jnp.concatenate(
        [query_full[..., :NOPE], rotate(query_full[..., NOPE:], position[None, :])], -1
    ).astype(jnp.bfloat16)
    key_nope = jnp.einsum(
        "td,dhe->hte", cm_all, key_w.reshape(KVRANK, heads, NOPE), preferred_element_type=jnp.float32
    ).astype(jnp.bfloat16)
    value = jnp.einsum(
        "td,dhe->hte", cm_all, value_w.reshape(KVRANK, heads, VDIM), preferred_element_type=jnp.float32
    ).astype(jnp.bfloat16)
    score_scale = (NOPE + ROPE) ** (-0.5)
    received = [None] * seq_count
    shifts = [k for k in range(seq_count - 1, 0, -1) if k % 2]
    shifts = shifts + [k for k in range(seq_count - 1, 0, -1) if k % 2 == 0] + [0]
    for k in shifts:
        rows = block_attention(
            query, key_nope, rope_all, value, group_ids, score_scale, doc_most, tok_count,
            (seq_index + k) % seq_count,
        )
        if k:
            rows = lax.ppermute(
                rows, "seq", perm=[(i, (i + k) % seq_count) for i in range(seq_count)]
            )
        received[k] = rows
    attended = jnp.take(
        jnp.stack(received), (seq_index - jnp.arange(seq_count)) % seq_count, axis=0
    )
    attended = jnp.transpose(attended, (2, 0, 1, 3))
    return attended.reshape(tok_count, local_heads * VDIM)


def solution(mesh):
    in_specs = (
        P(("dp", "seq"), "tp"),
        P("tp"),
        P("tp", "seq"),
        P("tp", "seq"),
        P(),
        P(),
        P("seq", "tp"),
        P("seq", "tp"),
        P("seq", "tp"),
        P(("dp", "seq")),
    )
    out_specs = P(("dp", "seq"), "tp")
    return jax.shard_map(body, mesh=mesh, in_specs=in_specs, out_specs=out_specs, check_vma=False)
```

```python
import functools

import jax
import jax.numpy as jnp
from jax import lax
from jax.experimental import pallas as pl
from jax.experimental.pallas import tpu as pltpu
from jax.sharding import PartitionSpec as P

KVRANK = 512
NOPE = 128
ROPE = 64
VDIM = 128
DOCS = 12


epsilon = 1e-06


def rms_scale(entries, gain_vector):
    return (
        entries * lax.rsqrt(jnp.mean(entries * entries, -1, keepdims=True) + epsilon) * gain_vector
    )


def rotate(entries, position):
    half_width = entries.shape[-1] // 2
    frequency = jnp.power(10000.0, -2.0 * jnp.arange(half_width, dtype=jnp.float32) / ROPE)
    angles = position.astype(jnp.float32)[..., None] * frequency
    cosine = jnp.cos(angles)
    sine_part = jnp.sin(angles)
    first_half = entries[..., :half_width]
    second_half = entries[..., half_width:]
    return jnp.concatenate(
        [
            first_half * cosine - second_half * sine_part,
            second_half * cosine + first_half * sine_part,
        ],
        -1,
    )


def heads_attention(query_all, key_all, value_all, group_ids, score_scale, doc_most):
    total_rows = query_all.shape[0]
    block_rows = min(512, total_rows)
    key_index = jnp.arange(total_rows, dtype=jnp.int32)
    results = []
    for block in range(total_rows // block_rows):
        lower = block * block_rows
        upper = lower + block_rows
        key_low = max(0, lower - doc_most)
        scores = (
            jnp.einsum(
                "qhd,khd->hqk",
                query_all[lower:upper],
                key_all[key_low:upper],
                preferred_element_type=jnp.float32,
            )
            * score_scale
        )
        allowed = (group_ids[lower:upper, None] == group_ids[None, key_low:upper]) & (
            key_index[lower:upper, None] >= key_index[None, key_low:upper]
        )
        scores = jnp.where(allowed[None], scores, -jnp.inf)
        row_max = jnp.max(scores, -1, keepdims=True)
        probs_full = jnp.exp(scores - row_max)
        denominator = jnp.sum(probs_full, -1)
        weights = probs_full.astype(jnp.bfloat16)
        weighted = jnp.einsum(
            "hqk,khd->qhd", weights, value_all[key_low:upper], preferred_element_type=jnp.float32
        )
        results.append((weighted / jnp.transpose(denominator)[:, :, None]).astype(jnp.bfloat16))
    return jnp.concatenate(results, 0)


def attention_kernel(
    block_ref, query_ref, key_ref, rope_ref, value_ref, ids_col_ref, ids_row_ref, out_ref, bias_ref, *, block, window, doc_most, scale
):
    lower = block_ref[0] * block
    start = pl.multiple_of(jnp.maximum(lower - doc_most, 0), block)

    @pl.when(pl.program_id(0) == 0)
    def _():
        query_index = lower + lax.broadcasted_iota(jnp.int32, (block, window), 0)
        key_index = start + lax.broadcasted_iota(jnp.int32, (block, window), 1)
        allowed = (ids_col_ref[...] == ids_row_ref[:, pl.ds(start, window)]) & (
            query_index >= key_index
        )
        bias_ref[...] = jnp.where(allowed, 0.0, -jnp.inf).astype(jnp.float32)

    query = query_ref[0]
    keys = key_ref[0, pl.ds(start, window), :]
    rope = rope_ref[pl.ds(start, window), :]
    values = value_ref[0, pl.ds(start, window), :]
    dims = (((1,), (1,)), ((), ()))
    scores = lax.dot_general(query[:, :NOPE], keys, dims, preferred_element_type=jnp.float32)
    scores = scores + lax.dot_general(
        query[:, NOPE:], rope, dims, preferred_element_type=jnp.float32
    )
    scores = scores * scale + bias_ref[...]
    row_max = jnp.max(scores, -1, keepdims=True)
    probs = jnp.exp(scores - row_max)
    denominator = jnp.sum(probs, -1, keepdims=True)
    weighted = jnp.dot(probs.astype(jnp.bfloat16), values, preferred_element_type=jnp.float32)
    out_ref[0] = (weighted / denominator).astype(out_ref.dtype)


def block_attention(query, key_nope, key_rope, value, group_ids, score_scale, doc_most, block, index):
    heads, total_rows, _ = query.shape
    window = min(total_rows, doc_most + block)
    kernel = functools.partial(
        attention_kernel, block=block, window=window, doc_most=doc_most, scale=score_scale
    )
    flops = 2 * heads * block * window * (NOPE + ROPE + VDIM)
    return pl.pallas_call(
        kernel,
        grid_spec=pltpu.PrefetchScalarGridSpec(
            num_scalar_prefetch=1,
            grid=(heads,),
            in_specs=[
                pl.BlockSpec((1, block, NOPE + ROPE), lambda h, b: (h, b[0], 0)),
                pl.BlockSpec((1, total_rows, NOPE), lambda h, b: (h, 0, 0)),
                pl.BlockSpec((total_rows, ROPE), lambda h, b: (0, 0)),
                pl.BlockSpec((1, total_rows, VDIM), lambda h, b: (h, 0, 0)),
                pl.BlockSpec((block, 1), lambda h, b: (b[0], 0)),
                pl.BlockSpec((1, total_rows), lambda h, b: (0, 0)),
            ],
            out_specs=pl.BlockSpec((1, block, VDIM), lambda h, b: (h, 0, 0)),
            scratch_shapes=[pltpu.VMEM((block, window), jnp.float32)],
        ),
        out_shape=jax.ShapeDtypeStruct((heads, block, VDIM), jnp.bfloat16),
        cost_estimate=pl.CostEstimate(
            flops=flops,
            transcendentals=heads * block * window,
            bytes_accessed=2 * heads * (block * (NOPE + ROPE + VDIM) + window * (NOPE + VDIM)),
        ),
    )(
        jnp.reshape(index, (1,)).astype(jnp.int32),
        query,
        key_nope,
        key_rope,
        value,
        group_ids.reshape(total_rows, 1),
        group_ids.reshape(1, total_rows),
    )


def body(
    hidden_states,
    input_gain,
    query_down,
    memory_down,
    query_gain,
    memory_gain,
    query_up,
    key_up,
    value_up,
    segment_ids,
):
    tok_count = hidden_states.shape[0]
    seq_count = lax.axis_size("seq")
    tp_count = lax.axis_size("tp")
    seq_index = lax.axis_index("seq")
    tp_index = lax.axis_index("tp")
    width = hidden_states.shape[1] * tp_count
    total_rows = tok_count * seq_count
    doc_most = total_rows // 4
    qrank_piece = query_down.shape[1]
    memory_piece = memory_down.shape[1]
    qrank = qrank_piece * seq_count
    memory_cols = memory_piece * seq_count

    group_ids = lax.all_gather(segment_ids, "seq", axis=0, tiled=True)

    inputs = hidden_states.astype(jnp.float32)
    square_sums = lax.psum(jnp.sum(inputs * inputs, 1), "tp")
    normed = (inputs * lax.rsqrt(square_sums / width + epsilon)[:, None] * input_gain).astype(
        jnp.bfloat16
    )

    dp_index = lax.axis_index("dp")
    dp_count = lax.axis_size("dp")
    down_piece = jnp.concatenate([query_down, memory_down], 1)
    half_rows = down_piece.shape[0] // dp_count
    own_rows = lax.dynamic_slice_in_dim(down_piece, dp_index * half_rows, half_rows, 0)
    own_all = lax.all_gather(own_rows, "seq", axis=1, tiled=True)
    own_all, normed, group_ids = lax.optimization_barrier((own_all, normed, group_ids))
    partial = jnp.dot(
        lax.dynamic_slice_in_dim(normed, dp_index * half_rows, half_rows, 1),
        own_all,
        preferred_element_type=jnp.float32,
    )
    for shift in range(1, dp_count):
        peer = (dp_index + dp_count - shift) % dp_count
        peer_all = lax.ppermute(
            own_all, "dp", perm=[(i, (i + shift) % dp_count) for i in range(dp_count)]
        )
        partial = partial + jnp.dot(
            lax.dynamic_slice_in_dim(normed, peer * half_rows, half_rows, 1),
            peer_all,
            preferred_element_type=jnp.float32,
        )
    latent_rows = lax.psum_scatter(partial, "tp", scatter_dimension=0, tiled=True)

    token_index = jnp.arange(total_rows, dtype=jnp.int32)
    onehot = group_ids[:, None] == jnp.arange(DOCS, dtype=jnp.int32)[None, :]
    starts = jnp.min(jnp.where(onehot, token_index[:, None], total_rows), 0)
    position = token_index - jnp.sum(jnp.where(onehot, starts[None, :], 0), 1)
    chunk = latent_rows.shape[0]
    latent_rows = latent_rows.reshape(chunk, seq_count, qrank_piece + memory_piece)
    query_sums = latent_rows[:, :, :qrank_piece].reshape(chunk, qrank)
    memory_sums = latent_rows[:, :, qrank_piece:].reshape(chunk, memory_cols)
    chunk_position = lax.dynamic_slice(
        position, (seq_index * tok_count + tp_index * chunk,), (chunk,)
    )
    compressed_query = rms_scale(query_sums, query_gain).astype(jnp.bfloat16)
    compressed_memory = rms_scale(memory_sums[:, :KVRANK], memory_gain).astype(jnp.bfloat16)
    key_rope = rotate(memory_sums[:, KVRANK:], chunk_position).astype(jnp.bfloat16)
    packed = jnp.concatenate([compressed_query, compressed_memory, key_rope], 1)
    from_seq = [packed] + [
        lax.ppermute(packed, "seq", perm=[(i, (i + k) % seq_count) for i in range(seq_count)])
        for k in range(1, seq_count)
    ]
    packed = jnp.take(jnp.stack(from_seq), (seq_index - jnp.arange(seq_count)) % seq_count, axis=0)
    packed, query_up, key_up, value_up = lax.optimization_barrier(
        (packed, query_up, key_up, value_up)
    )
    packed = lax.all_gather(packed, "tp", axis=0, tiled=False)
    latent = jnp.transpose(packed, (1, 0, 2, 3)).reshape(total_rows, packed.shape[-1])
    cq_all = latent[:, :qrank]
    cm_all = latent[:, qrank : qrank + KVRANK]
    rope_all = latent[:, qrank + KVRANK :]

    local_heads = query_up.shape[1] // (NOPE + ROPE)
    heads = local_heads // seq_count

    def own_columns(weight, head_width):
        rows = weight.shape[0]
        cols = heads * head_width // dp_count
        own = lax.dynamic_slice_in_dim(
            weight.reshape(rows, seq_count, heads * head_width), dp_index * cols, cols, 2
        )
        return jnp.transpose(own, (1, 0, 2)).reshape(seq_count, rows * cols), (rows, cols)

    packed_w = [
        own_columns(query_up, NOPE + ROPE),
        own_columns(key_up, NOPE),
        own_columns(value_up, VDIM),
    ]
    moved = lax.all_to_all(
        jnp.concatenate([p for p, _ in packed_w], 1), "seq", split_axis=0, concat_axis=0, tiled=True
    )

    def head_columns(offset, shape):
        rows, cols = shape
        own = moved[:, offset : offset + rows * cols].reshape(seq_count * rows, cols)
        pieces = [own]
        for shift in range(1, dp_count):
            pieces.append(
                lax.ppermute(
                    own, "dp", perm=[(i, (i + shift) % dp_count) for i in range(dp_count)]
                )
            )
        ordered = []
        for core in range(dp_count):
            pick = pieces[0]
            for k in range(1, dp_count):
                pick = jnp.where((dp_index + dp_count - k) % dp_count == core, pieces[k], pick)
            ordered.append(pick)
        return jnp.concatenate(ordered, 1)

    offsets = [0]
    for _, (rows, cols) in packed_w:
        offsets.append(offsets[-1] + rows * cols)
    query_w = head_columns(offsets[0], packed_w[0][1])
    key_w = head_columns(offsets[1], packed_w[1][1])
    value_w = head_columns(offsets[2], packed_w[2][1])

    query_full = jnp.einsum(
        "td,dhe->hte",
        cq_all,
        query_w.reshape(qrank, heads, NOPE + ROPE),
        preferred_element_type=jnp.float32,
    )
    query = jnp.concatenate(
        [query_full[..., :NOPE], rotate(query_full[..., NOPE:], position[None, :])], -1
    ).astype(jnp.bfloat16)
    key_nope = jnp.einsum(
        "td,dhe->hte", cm_all, key_w.reshape(KVRANK, heads, NOPE), preferred_element_type=jnp.float32
    ).astype(jnp.bfloat16)
    value = jnp.einsum(
        "td,dhe->hte", cm_all, value_w.reshape(KVRANK, heads, VDIM), preferred_element_type=jnp.float32
    ).astype(jnp.bfloat16)
    score_scale = (NOPE + ROPE) ** (-0.5)
    received = [None] * seq_count
    shifts = [k for k in range(seq_count - 1, 0, -1) if k % 2]
    shifts = shifts + [k for k in range(seq_count - 1, 0, -1) if k % 2 == 0] + [0]
    for k in shifts:
        rows = block_attention(
            query, key_nope, rope_all, value, group_ids, score_scale, doc_most, tok_count,
            (seq_index + k) % seq_count,
        )
        if k:
            rows = lax.ppermute(
                rows, "seq", perm=[(i, (i + k) % seq_count) for i in range(seq_count)]
            )
        received[k] = rows
    attended = jnp.take(
        jnp.stack(received), (seq_index - jnp.arange(seq_count)) % seq_count, axis=0
    )
    attended = jnp.transpose(attended, (2, 0, 1, 3))
    return attended.reshape(tok_count, local_heads * VDIM)


def solution(mesh):
    in_specs = (
        P(("dp", "seq"), "tp"),
        P("tp"),
        P("tp", "seq"),
        P("tp", "seq"),
        P(),
        P(),
        P("seq", "tp"),
        P("seq", "tp"),
        P("seq", "tp"),
        P(("dp", "seq")),
    )
    out_specs = P(("dp", "seq"), "tp")
    return jax.shard_map(body, mesh=mesh, in_specs=in_specs, out_specs=out_specs, check_vma=False)
```

```python
import functools

import jax
import jax.numpy as jnp
from jax import lax
from jax.experimental import pallas as pl
from jax.experimental.pallas import tpu as pltpu
from jax.sharding import PartitionSpec as P

KVRANK = 512
NOPE = 128
ROPE = 64
VDIM = 128
DOCS = 12


epsilon = 1e-06


def rms_scale(entries, gain_vector):
    return (
        entries * lax.rsqrt(jnp.mean(entries * entries, -1, keepdims=True) + epsilon) * gain_vector
    )


def rotate(entries, position):
    half_width = entries.shape[-1] // 2
    frequency = jnp.power(10000.0, -2.0 * jnp.arange(half_width, dtype=jnp.float32) / ROPE)
    angles = position.astype(jnp.float32)[..., None] * frequency
    cosine = jnp.cos(angles)
    sine_part = jnp.sin(angles)
    first_half = entries[..., :half_width]
    second_half = entries[..., half_width:]
    return jnp.concatenate(
        [
            first_half * cosine - second_half * sine_part,
            second_half * cosine + first_half * sine_part,
        ],
        -1,
    )


def heads_attention(query_all, key_all, value_all, group_ids, score_scale, doc_most):
    total_rows = query_all.shape[0]
    block_rows = min(512, total_rows)
    key_index = jnp.arange(total_rows, dtype=jnp.int32)
    results = []
    for block in range(total_rows // block_rows):
        lower = block * block_rows
        upper = lower + block_rows
        key_low = max(0, lower - doc_most)
        scores = (
            jnp.einsum(
                "qhd,khd->hqk",
                query_all[lower:upper],
                key_all[key_low:upper],
                preferred_element_type=jnp.float32,
            )
            * score_scale
        )
        allowed = (group_ids[lower:upper, None] == group_ids[None, key_low:upper]) & (
            key_index[lower:upper, None] >= key_index[None, key_low:upper]
        )
        scores = jnp.where(allowed[None], scores, -jnp.inf)
        row_max = jnp.max(scores, -1, keepdims=True)
        probs_full = jnp.exp(scores - row_max)
        denominator = jnp.sum(probs_full, -1)
        weights = probs_full.astype(jnp.bfloat16)
        weighted = jnp.einsum(
            "hqk,khd->qhd", weights, value_all[key_low:upper], preferred_element_type=jnp.float32
        )
        results.append((weighted / jnp.transpose(denominator)[:, :, None]).astype(jnp.bfloat16))
    return jnp.concatenate(results, 0)


def attention_kernel(
    block_ref, query_ref, key_ref, rope_ref, value_ref, ids_col_ref, ids_row_ref, out_ref, bias_ref, *, block, window, doc_most, scale
):
    lower = block_ref[0] * block
    start = pl.multiple_of(jnp.maximum(lower - doc_most, 0), block)

    @pl.when(pl.program_id(0) == 0)
    def _():
        query_index = lower + lax.broadcasted_iota(jnp.int32, (block, window), 0)
        key_index = start + lax.broadcasted_iota(jnp.int32, (block, window), 1)
        allowed = (ids_col_ref[...] == ids_row_ref[:, pl.ds(start, window)]) & (
            query_index >= key_index
        )
        bias_ref[...] = jnp.where(allowed, 0.0, -jnp.inf).astype(jnp.float32)

    query = query_ref[0]
    keys = key_ref[0, pl.ds(start, window), :]
    rope = rope_ref[pl.ds(start, window), :]
    values = value_ref[0, pl.ds(start, window), :]
    dims = (((1,), (1,)), ((), ()))
    scores = lax.dot_general(query[:, :NOPE], keys, dims, preferred_element_type=jnp.float32)
    scores = scores + lax.dot_general(
        query[:, NOPE:], rope, dims, preferred_element_type=jnp.float32
    )
    scores = scores * scale + bias_ref[...]
    row_max = jnp.max(scores, -1, keepdims=True)
    probs = jnp.exp(scores - row_max)
    denominator = jnp.sum(probs, -1, keepdims=True)
    weighted = jnp.dot(probs.astype(jnp.bfloat16), values, preferred_element_type=jnp.float32)
    out_ref[0] = (weighted / denominator).astype(out_ref.dtype)


def block_attention(query, key_nope, key_rope, value, group_ids, score_scale, doc_most, block, index):
    heads, total_rows, _ = query.shape
    window = min(total_rows, doc_most + block)
    kernel = functools.partial(
        attention_kernel, block=block, window=window, doc_most=doc_most, scale=score_scale
    )
    flops = 2 * heads * block * window * (NOPE + ROPE + VDIM)
    return pl.pallas_call(
        kernel,
        grid_spec=pltpu.PrefetchScalarGridSpec(
            num_scalar_prefetch=1,
            grid=(heads,),
            in_specs=[
                pl.BlockSpec((1, block, NOPE + ROPE), lambda h, b: (h, b[0], 0)),
                pl.BlockSpec((1, total_rows, NOPE), lambda h, b: (h, 0, 0)),
                pl.BlockSpec((total_rows, ROPE), lambda h, b: (0, 0)),
                pl.BlockSpec((1, total_rows, VDIM), lambda h, b: (h, 0, 0)),
                pl.BlockSpec((block, 1), lambda h, b: (b[0], 0)),
                pl.BlockSpec((1, total_rows), lambda h, b: (0, 0)),
            ],
            out_specs=pl.BlockSpec((1, block, VDIM), lambda h, b: (h, 0, 0)),
            scratch_shapes=[pltpu.VMEM((block, window), jnp.float32)],
        ),
        out_shape=jax.ShapeDtypeStruct((heads, block, VDIM), jnp.bfloat16),
        cost_estimate=pl.CostEstimate(
            flops=flops,
            transcendentals=heads * block * window,
            bytes_accessed=2 * heads * (block * (NOPE + ROPE + VDIM) + window * (NOPE + VDIM)),
        ),
    )(
        jnp.reshape(index, (1,)).astype(jnp.int32),
        query,
        key_nope,
        key_rope,
        value,
        group_ids.reshape(total_rows, 1),
        group_ids.reshape(1, total_rows),
    )


def body(
    hidden_states,
    input_gain,
    query_down,
    memory_down,
    query_gain,
    memory_gain,
    query_up,
    key_up,
    value_up,
    segment_ids,
):
    tok_count = hidden_states.shape[0]
    seq_count = lax.axis_size("seq")
    tp_count = lax.axis_size("tp")
    seq_index = lax.axis_index("seq")
    tp_index = lax.axis_index("tp")
    width = hidden_states.shape[1] * tp_count
    total_rows = tok_count * seq_count
    doc_most = total_rows // 4
    qrank_piece = query_down.shape[1]
    memory_piece = memory_down.shape[1]
    qrank = qrank_piece * seq_count
    memory_cols = memory_piece * seq_count

    group_ids = lax.all_gather(segment_ids, "seq", axis=0, tiled=True)

    inputs = hidden_states.astype(jnp.float32)
    square_sums = lax.psum(jnp.sum(inputs * inputs, 1), "tp")
    normed = (inputs * lax.rsqrt(square_sums / width + epsilon)[:, None] * input_gain).astype(
        jnp.bfloat16
    )

    dp_index = lax.axis_index("dp")
    dp_count = lax.axis_size("dp")
    down_piece = jnp.concatenate([query_down, memory_down], 1)
    half_rows = down_piece.shape[0] // dp_count
    own_rows = lax.dynamic_slice_in_dim(down_piece, dp_index * half_rows, half_rows, 0)
    own_all = lax.all_gather(own_rows, "seq", axis=1, tiled=True)
    own_all, normed, group_ids = lax.optimization_barrier((own_all, normed, group_ids))
    partial = jnp.dot(
        lax.dynamic_slice_in_dim(normed, dp_index * half_rows, half_rows, 1),
        own_all,
        preferred_element_type=jnp.float32,
    )
    for shift in range(1, dp_count):
        peer = (dp_index + dp_count - shift) % dp_count
        peer_all = lax.ppermute(
            own_all, "dp", perm=[(i, (i + shift) % dp_count) for i in range(dp_count)]
        )
        partial = partial + jnp.dot(
            lax.dynamic_slice_in_dim(normed, peer * half_rows, half_rows, 1),
            peer_all,
            preferred_element_type=jnp.float32,
        )
    pieces = partial.reshape(tp_count, partial.shape[0] // tp_count, partial.shape[1])
    latent_rows = lax.dynamic_index_in_dim(pieces, tp_index, 0, keepdims=False)
    for k in range(1, tp_count):
        sent = lax.dynamic_index_in_dim(pieces, (tp_index + k) % tp_count, 0, keepdims=False)
        latent_rows = latent_rows + lax.ppermute(
            sent, "tp", perm=[(i, (i + k) % tp_count) for i in range(tp_count)]
        )

    token_index = jnp.arange(total_rows, dtype=jnp.int32)
    onehot = group_ids[:, None] == jnp.arange(DOCS, dtype=jnp.int32)[None, :]
    starts = jnp.min(jnp.where(onehot, token_index[:, None], total_rows), 0)
    position = token_index - jnp.sum(jnp.where(onehot, starts[None, :], 0), 1)
    chunk = latent_rows.shape[0]
    latent_rows = latent_rows.reshape(chunk, seq_count, qrank_piece + memory_piece)
    query_sums = latent_rows[:, :, :qrank_piece].reshape(chunk, qrank)
    memory_sums = latent_rows[:, :, qrank_piece:].reshape(chunk, memory_cols)
    chunk_position = lax.dynamic_slice(
        position, (seq_index * tok_count + tp_index * chunk,), (chunk,)
    )
    compressed_query = rms_scale(query_sums, query_gain).astype(jnp.bfloat16)
    compressed_memory = rms_scale(memory_sums[:, :KVRANK], memory_gain).astype(jnp.bfloat16)
    key_rope = rotate(memory_sums[:, KVRANK:], chunk_position).astype(jnp.bfloat16)
    packed = jnp.concatenate([compressed_query, compressed_memory, key_rope], 1)
    from_seq = [packed] + [
        lax.ppermute(packed, "seq", perm=[(i, (i + k) % seq_count) for i in range(seq_count)])
        for k in range(1, seq_count)
    ]
    packed = jnp.take(jnp.stack(from_seq), (seq_index - jnp.arange(seq_count)) % seq_count, axis=0)
    packed, query_up, key_up, value_up = lax.optimization_barrier(
        (packed, query_up, key_up, value_up)
    )
    packed = lax.all_gather(packed, "tp", axis=0, tiled=False)
    latent = jnp.transpose(packed, (1, 0, 2, 3)).reshape(total_rows, packed.shape[-1])
    cq_all = latent[:, :qrank]
    cm_all = latent[:, qrank : qrank + KVRANK]
    rope_all = latent[:, qrank + KVRANK :]

    local_heads = query_up.shape[1] // (NOPE + ROPE)
    heads = local_heads // seq_count

    def head_columns(weight, head_width):
        rows = weight.shape[0]
        cols = heads * head_width // dp_count
        own = lax.dynamic_slice_in_dim(
            weight.reshape(rows, seq_count, heads * head_width), dp_index * cols, cols, 2
        )
        own = lax.all_to_all(own, "seq", split_axis=1, concat_axis=0, tiled=True)
        own = own.reshape(rows * seq_count, cols)
        pieces = [own]
        for shift in range(1, dp_count):
            pieces.append(
                lax.ppermute(
                    own, "dp", perm=[(i, (i + shift) % dp_count) for i in range(dp_count)]
                )
            )
        ordered = []
        for core in range(dp_count):
            pick = pieces[0]
            for k in range(1, dp_count):
                pick = jnp.where((dp_index + dp_count - k) % dp_count == core, pieces[k], pick)
            ordered.append(pick)
        return jnp.concatenate(ordered, 1)

    query_w = head_columns(query_up, NOPE + ROPE)
    key_w = head_columns(key_up, NOPE)
    value_w = head_columns(value_up, VDIM)

    query_full = jnp.einsum(
        "td,dhe->hte",
        cq_all,
        query_w.reshape(qrank, heads, NOPE + ROPE),
        preferred_element_type=jnp.float32,
    )
    query = jnp.concatenate(
        [query_full[..., :NOPE], rotate(query_full[..., NOPE:], position[None, :])], -1
    ).astype(jnp.bfloat16)
    key_nope = jnp.einsum(
        "td,dhe->hte", cm_all, key_w.reshape(KVRANK, heads, NOPE), preferred_element_type=jnp.float32
    ).astype(jnp.bfloat16)
    value = jnp.einsum(
        "td,dhe->hte", cm_all, value_w.reshape(KVRANK, heads, VDIM), preferred_element_type=jnp.float32
    ).astype(jnp.bfloat16)
    score_scale = (NOPE + ROPE) ** (-0.5)
    received = [None] * seq_count
    shifts = [k for k in range(seq_count - 1, 0, -1) if k % 2]
    shifts = shifts + [k for k in range(seq_count - 1, 0, -1) if k % 2 == 0] + [0]
    for k in shifts:
        rows = block_attention(
            query, key_nope, rope_all, value, group_ids, score_scale, doc_most, tok_count,
            (seq_index + k) % seq_count,
        )
        if k:
            rows = lax.ppermute(
                rows, "seq", perm=[(i, (i + k) % seq_count) for i in range(seq_count)]
            )
        received[k] = rows
    attended = jnp.take(
        jnp.stack(received), (seq_index - jnp.arange(seq_count)) % seq_count, axis=0
    )
    attended = jnp.transpose(attended, (2, 0, 1, 3))
    return attended.reshape(tok_count, local_heads * VDIM)


def solution(mesh):
    in_specs = (
        P(("dp", "seq"), "tp"),
        P("tp"),
        P("tp", "seq"),
        P("tp", "seq"),
        P(),
        P(),
        P("seq", "tp"),
        P("seq", "tp"),
        P("seq", "tp"),
        P(("dp", "seq")),
    )
    out_specs = P(("dp", "seq"), "tp")
    return jax.shard_map(body, mesh=mesh, in_specs=in_specs, out_specs=out_specs, check_vma=False)
```

```python
import functools

import jax
import jax.numpy as jnp
from jax import lax
from jax.experimental import pallas as pl
from jax.experimental.pallas import tpu as pltpu
from jax.sharding import PartitionSpec as P

KVRANK = 512
NOPE = 128
ROPE = 64
VDIM = 128
DOCS = 12


epsilon = 1e-06


def rms_scale(entries, gain_vector):
    return (
        entries * lax.rsqrt(jnp.mean(entries * entries, -1, keepdims=True) + epsilon) * gain_vector
    )


def rotate(entries, position):
    half_width = entries.shape[-1] // 2
    frequency = jnp.power(10000.0, -2.0 * jnp.arange(half_width, dtype=jnp.float32) / ROPE)
    angles = position.astype(jnp.float32)[..., None] * frequency
    cosine = jnp.cos(angles)
    sine_part = jnp.sin(angles)
    first_half = entries[..., :half_width]
    second_half = entries[..., half_width:]
    return jnp.concatenate(
        [
            first_half * cosine - second_half * sine_part,
            second_half * cosine + first_half * sine_part,
        ],
        -1,
    )


def heads_attention(query_all, key_all, value_all, group_ids, score_scale, doc_most):
    total_rows = query_all.shape[0]
    block_rows = min(512, total_rows)
    key_index = jnp.arange(total_rows, dtype=jnp.int32)
    results = []
    for block in range(total_rows // block_rows):
        lower = block * block_rows
        upper = lower + block_rows
        key_low = max(0, lower - doc_most)
        scores = (
            jnp.einsum(
                "qhd,khd->hqk",
                query_all[lower:upper],
                key_all[key_low:upper],
                preferred_element_type=jnp.float32,
            )
            * score_scale
        )
        allowed = (group_ids[lower:upper, None] == group_ids[None, key_low:upper]) & (
            key_index[lower:upper, None] >= key_index[None, key_low:upper]
        )
        scores = jnp.where(allowed[None], scores, -jnp.inf)
        row_max = jnp.max(scores, -1, keepdims=True)
        probs_full = jnp.exp(scores - row_max)
        denominator = jnp.sum(probs_full, -1)
        weights = probs_full.astype(jnp.bfloat16)
        weighted = jnp.einsum(
            "hqk,khd->qhd", weights, value_all[key_low:upper], preferred_element_type=jnp.float32
        )
        results.append((weighted / jnp.transpose(denominator)[:, :, None]).astype(jnp.bfloat16))
    return jnp.concatenate(results, 0)


def attention_kernel(
    block_ref, query_ref, key_ref, rope_ref, value_ref, ids_col_ref, ids_row_ref, out_ref, bias_ref, *, block, window, doc_most, scale
):
    lower = block_ref[0] * block
    start = pl.multiple_of(jnp.maximum(lower - doc_most, 0), block)

    @pl.when(pl.program_id(0) == 0)
    def _():
        query_index = lower + lax.broadcasted_iota(jnp.int32, (block, window), 0)
        key_index = start + lax.broadcasted_iota(jnp.int32, (block, window), 1)
        allowed = (ids_col_ref[...] == ids_row_ref[:, pl.ds(start, window)]) & (
            query_index >= key_index
        )
        bias_ref[...] = jnp.where(allowed, 0.0, -jnp.inf).astype(jnp.float32)

    query = query_ref[0]
    keys = key_ref[0, pl.ds(start, window), :]
    rope = rope_ref[pl.ds(start, window), :]
    values = value_ref[0, pl.ds(start, window), :]
    dims = (((1,), (1,)), ((), ()))
    scores = lax.dot_general(query[:, :NOPE], keys, dims, preferred_element_type=jnp.float32)
    scores = scores + lax.dot_general(
        query[:, NOPE:], rope, dims, preferred_element_type=jnp.float32
    )
    scores = scores * scale + bias_ref[...]
    row_max = jnp.max(scores, -1, keepdims=True)
    probs = jnp.exp(scores - row_max)
    denominator = jnp.sum(probs, -1, keepdims=True)
    weighted = jnp.dot(probs.astype(jnp.bfloat16), values, preferred_element_type=jnp.float32)
    out_ref[0] = (weighted / denominator).astype(out_ref.dtype)


def block_attention(query, key_nope, key_rope, value, group_ids, score_scale, doc_most, block, index):
    heads, total_rows, _ = query.shape
    window = min(total_rows, doc_most + block)
    kernel = functools.partial(
        attention_kernel, block=block, window=window, doc_most=doc_most, scale=score_scale
    )
    flops = 2 * heads * block * window * (NOPE + ROPE + VDIM)
    return pl.pallas_call(
        kernel,
        grid_spec=pltpu.PrefetchScalarGridSpec(
            num_scalar_prefetch=1,
            grid=(heads,),
            in_specs=[
                pl.BlockSpec((1, block, NOPE + ROPE), lambda h, b: (h, b[0], 0)),
                pl.BlockSpec((1, total_rows, NOPE), lambda h, b: (h, 0, 0)),
                pl.BlockSpec((total_rows, ROPE), lambda h, b: (0, 0)),
                pl.BlockSpec((1, total_rows, VDIM), lambda h, b: (h, 0, 0)),
                pl.BlockSpec((block, 1), lambda h, b: (b[0], 0)),
                pl.BlockSpec((1, total_rows), lambda h, b: (0, 0)),
            ],
            out_specs=pl.BlockSpec((1, block, VDIM), lambda h, b: (h, 0, 0)),
            scratch_shapes=[pltpu.VMEM((block, window), jnp.float32)],
        ),
        out_shape=jax.ShapeDtypeStruct((heads, block, VDIM), jnp.bfloat16),
        cost_estimate=pl.CostEstimate(
            flops=flops,
            transcendentals=heads * block * window,
            bytes_accessed=2 * heads * (block * (NOPE + ROPE + VDIM) + window * (NOPE + VDIM)),
        ),
    )(
        jnp.reshape(index, (1,)).astype(jnp.int32),
        query,
        key_nope,
        key_rope,
        value,
        group_ids.reshape(total_rows, 1),
        group_ids.reshape(1, total_rows),
    )


def body(
    hidden_states,
    input_gain,
    query_down,
    memory_down,
    query_gain,
    memory_gain,
    query_up,
    key_up,
    value_up,
    segment_ids,
):
    tok_count = hidden_states.shape[0]
    seq_count = lax.axis_size("seq")
    tp_count = lax.axis_size("tp")
    seq_index = lax.axis_index("seq")
    tp_index = lax.axis_index("tp")
    width = hidden_states.shape[1] * tp_count
    total_rows = tok_count * seq_count
    doc_most = total_rows // 4
    qrank_piece = query_down.shape[1]
    memory_piece = memory_down.shape[1]
    qrank = qrank_piece * seq_count
    memory_cols = memory_piece * seq_count

    group_ids = lax.all_gather(segment_ids, "seq", axis=0, tiled=True)

    inputs = hidden_states.astype(jnp.float32)
    square_sums = lax.psum(jnp.sum(inputs * inputs, 1), "tp")
    normed = (inputs * lax.rsqrt(square_sums / width + epsilon)[:, None] * input_gain).astype(
        jnp.bfloat16
    )

    dp_index = lax.axis_index("dp")
    dp_count = lax.axis_size("dp")
    down_piece = jnp.concatenate([query_down, memory_down], 1)
    half_rows = down_piece.shape[0] // dp_count
    own_rows = lax.dynamic_slice_in_dim(down_piece, dp_index * half_rows, half_rows, 0)
    own_all = lax.all_gather(own_rows, "seq", axis=1, tiled=True)
    own_all, normed, group_ids = lax.optimization_barrier((own_all, normed, group_ids))
    partial = jnp.dot(
        lax.dynamic_slice_in_dim(normed, dp_index * half_rows, half_rows, 1),
        own_all,
        preferred_element_type=jnp.float32,
    )
    for shift in range(1, dp_count):
        peer = (dp_index + dp_count - shift) % dp_count
        peer_all = lax.ppermute(
            own_all, "dp", perm=[(i, (i + shift) % dp_count) for i in range(dp_count)]
        )
        partial = partial + jnp.dot(
            lax.dynamic_slice_in_dim(normed, peer * half_rows, half_rows, 1),
            peer_all,
            preferred_element_type=jnp.float32,
        )
    pieces = partial.reshape(tp_count, partial.shape[0] // tp_count, partial.shape[1])
    latent_rows = lax.dynamic_index_in_dim(pieces, tp_index, 0, keepdims=False)
    for k in range(1, tp_count):
        sent = lax.dynamic_index_in_dim(pieces, (tp_index + k) % tp_count, 0, keepdims=False)
        latent_rows = latent_rows + lax.ppermute(
            sent, "tp", perm=[(i, (i + k) % tp_count) for i in range(tp_count)]
        )

    token_index = jnp.arange(total_rows, dtype=jnp.int32)
    onehot = group_ids[:, None] == jnp.arange(DOCS, dtype=jnp.int32)[None, :]
    starts = jnp.min(jnp.where(onehot, token_index[:, None], total_rows), 0)
    position = token_index - jnp.sum(jnp.where(onehot, starts[None, :], 0), 1)
    chunk = latent_rows.shape[0]
    latent_rows = latent_rows.reshape(chunk, seq_count, qrank_piece + memory_piece)
    query_sums = latent_rows[:, :, :qrank_piece].reshape(chunk, qrank)
    memory_sums = latent_rows[:, :, qrank_piece:].reshape(chunk, memory_cols)
    chunk_position = lax.dynamic_slice(
        position, (seq_index * tok_count + tp_index * chunk,), (chunk,)
    )
    compressed_query = rms_scale(query_sums, query_gain).astype(jnp.bfloat16)
    compressed_memory = rms_scale(memory_sums[:, :KVRANK], memory_gain).astype(jnp.bfloat16)
    key_rope = rotate(memory_sums[:, KVRANK:], chunk_position).astype(jnp.bfloat16)
    packed = jnp.concatenate([compressed_query, compressed_memory, key_rope], 1)
    from_seq = [packed] + [
        lax.ppermute(packed, "seq", perm=[(i, (i + k) % seq_count) for i in range(seq_count)])
        for k in range(1, seq_count)
    ]
    packed = jnp.take(jnp.stack(from_seq), (seq_index - jnp.arange(seq_count)) % seq_count, axis=0)
    packed, query_up, key_up, value_up = lax.optimization_barrier(
        (packed, query_up, key_up, value_up)
    )
    from_tp = [packed] + [
        lax.ppermute(packed, "tp", perm=[(i, (i + k) % tp_count) for i in range(tp_count)])
        for k in range(1, tp_count)
    ]
    packed = jnp.take(jnp.stack(from_tp), (tp_index - jnp.arange(tp_count)) % tp_count, axis=0)
    latent = jnp.transpose(packed, (1, 0, 2, 3)).reshape(total_rows, packed.shape[-1])
    cq_all = latent[:, :qrank]
    cm_all = latent[:, qrank : qrank + KVRANK]
    rope_all = latent[:, qrank + KVRANK :]

    local_heads = query_up.shape[1] // (NOPE + ROPE)
    heads = local_heads // seq_count

    def head_columns(weight, head_width):
        rows = weight.shape[0]
        cols = heads * head_width // dp_count
        own = lax.dynamic_slice_in_dim(
            weight.reshape(rows, seq_count, heads * head_width), dp_index * cols, cols, 2
        )
        own = lax.all_to_all(own, "seq", split_axis=1, concat_axis=0, tiled=True)
        own = own.reshape(rows * seq_count, cols)
        pieces = [own]
        for shift in range(1, dp_count):
            pieces.append(
                lax.ppermute(
                    own, "dp", perm=[(i, (i + shift) % dp_count) for i in range(dp_count)]
                )
            )
        ordered = []
        for core in range(dp_count):
            pick = pieces[0]
            for k in range(1, dp_count):
                pick = jnp.where((dp_index + dp_count - k) % dp_count == core, pieces[k], pick)
            ordered.append(pick)
        return jnp.concatenate(ordered, 1)

    query_w = head_columns(query_up, NOPE + ROPE)
    key_w = head_columns(key_up, NOPE)
    value_w = head_columns(value_up, VDIM)

    query_full = jnp.einsum(
        "td,dhe->hte",
        cq_all,
        query_w.reshape(qrank, heads, NOPE + ROPE),
        preferred_element_type=jnp.float32,
    )
    query = jnp.concatenate(
        [query_full[..., :NOPE], rotate(query_full[..., NOPE:], position[None, :])], -1
    ).astype(jnp.bfloat16)
    key_nope = jnp.einsum(
        "td,dhe->hte", cm_all, key_w.reshape(KVRANK, heads, NOPE), preferred_element_type=jnp.float32
    ).astype(jnp.bfloat16)
    value = jnp.einsum(
        "td,dhe->hte", cm_all, value_w.reshape(KVRANK, heads, VDIM), preferred_element_type=jnp.float32
    ).astype(jnp.bfloat16)
    score_scale = (NOPE + ROPE) ** (-0.5)
    received = [None] * seq_count
    shifts = [k for k in range(seq_count - 1, 0, -1) if k % 2]
    shifts = shifts + [k for k in range(seq_count - 1, 0, -1) if k % 2 == 0] + [0]
    for k in shifts:
        rows = block_attention(
            query, key_nope, rope_all, value, group_ids, score_scale, doc_most, tok_count,
            (seq_index + k) % seq_count,
        )
        if k:
            rows = lax.ppermute(
                rows, "seq", perm=[(i, (i + k) % seq_count) for i in range(seq_count)]
            )
        received[k] = rows
    attended = jnp.take(
        jnp.stack(received), (seq_index - jnp.arange(seq_count)) % seq_count, axis=0
    )
    attended = jnp.transpose(attended, (2, 0, 1, 3))
    return attended.reshape(tok_count, local_heads * VDIM)


def solution(mesh):
    in_specs = (
        P(("dp", "seq"), "tp"),
        P("tp"),
        P("tp", "seq"),
        P("tp", "seq"),
        P(),
        P(),
        P("seq", "tp"),
        P("seq", "tp"),
        P("seq", "tp"),
        P(("dp", "seq")),
    )
    out_specs = P(("dp", "seq"), "tp")
    return jax.shard_map(body, mesh=mesh, in_specs=in_specs, out_specs=out_specs, check_vma=False)
```

```python
import functools

import jax
import jax.numpy as jnp
from jax import lax
from jax.experimental import pallas as pl
from jax.experimental.pallas import tpu as pltpu
from jax.sharding import PartitionSpec as P

KVRANK = 512
NOPE = 128
ROPE = 64
VDIM = 128
DOCS = 12


epsilon = 1e-06


def rms_scale(entries, gain_vector):
    return (
        entries * lax.rsqrt(jnp.mean(entries * entries, -1, keepdims=True) + epsilon) * gain_vector
    )


def rotate(entries, position):
    half_width = entries.shape[-1] // 2
    frequency = jnp.power(10000.0, -2.0 * jnp.arange(half_width, dtype=jnp.float32) / ROPE)
    angles = position.astype(jnp.float32)[..., None] * frequency
    cosine = jnp.cos(angles)
    sine_part = jnp.sin(angles)
    first_half = entries[..., :half_width]
    second_half = entries[..., half_width:]
    return jnp.concatenate(
        [
            first_half * cosine - second_half * sine_part,
            second_half * cosine + first_half * sine_part,
        ],
        -1,
    )


def heads_attention(query_all, key_all, value_all, group_ids, score_scale, doc_most):
    total_rows = query_all.shape[0]
    block_rows = min(512, total_rows)
    key_index = jnp.arange(total_rows, dtype=jnp.int32)
    results = []
    for block in range(total_rows // block_rows):
        lower = block * block_rows
        upper = lower + block_rows
        key_low = max(0, lower - doc_most)
        scores = (
            jnp.einsum(
                "qhd,khd->hqk",
                query_all[lower:upper],
                key_all[key_low:upper],
                preferred_element_type=jnp.float32,
            )
            * score_scale
        )
        allowed = (group_ids[lower:upper, None] == group_ids[None, key_low:upper]) & (
            key_index[lower:upper, None] >= key_index[None, key_low:upper]
        )
        scores = jnp.where(allowed[None], scores, -jnp.inf)
        row_max = jnp.max(scores, -1, keepdims=True)
        probs_full = jnp.exp(scores - row_max)
        denominator = jnp.sum(probs_full, -1)
        weights = probs_full.astype(jnp.bfloat16)
        weighted = jnp.einsum(
            "hqk,khd->qhd", weights, value_all[key_low:upper], preferred_element_type=jnp.float32
        )
        results.append((weighted / jnp.transpose(denominator)[:, :, None]).astype(jnp.bfloat16))
    return jnp.concatenate(results, 0)


def attention_kernel(
    block_ref, query_ref, key_ref, rope_ref, value_ref, ids_col_ref, ids_row_ref, out_ref, bias_ref, *, block, window, doc_most, scale
):
    lower = block_ref[0] * block
    start = pl.multiple_of(jnp.maximum(lower - doc_most, 0), block)

    @pl.when(pl.program_id(0) == 0)
    def _():
        query_index = lower + lax.broadcasted_iota(jnp.int32, (block, window), 0)
        key_index = start + lax.broadcasted_iota(jnp.int32, (block, window), 1)
        allowed = (ids_col_ref[...] == ids_row_ref[:, pl.ds(start, window)]) & (
            query_index >= key_index
        )
        bias_ref[...] = jnp.where(allowed, 0.0, -jnp.inf).astype(jnp.float32)

    query = query_ref[0]
    keys = key_ref[0, pl.ds(start, window), :]
    rope = rope_ref[pl.ds(start, window), :]
    values = value_ref[0, pl.ds(start, window), :]
    dims = (((1,), (1,)), ((), ()))
    scores = lax.dot_general(query[:, :NOPE], keys, dims, preferred_element_type=jnp.float32)
    scores = scores + lax.dot_general(
        query[:, NOPE:], rope, dims, preferred_element_type=jnp.float32
    )
    scores = scores * scale + bias_ref[...]
    row_max = jnp.max(scores, -1, keepdims=True)
    probs = jnp.exp(scores - row_max)
    denominator = jnp.sum(probs, -1, keepdims=True)
    weighted = jnp.dot(probs.astype(jnp.bfloat16), values, preferred_element_type=jnp.float32)
    out_ref[0] = (weighted / denominator).astype(out_ref.dtype)


def block_attention(query, key_nope, key_rope, value, group_ids, score_scale, doc_most, block, index):
    heads, total_rows, _ = query.shape
    window = min(total_rows, doc_most + block)
    kernel = functools.partial(
        attention_kernel, block=block, window=window, doc_most=doc_most, scale=score_scale
    )
    flops = 2 * heads * block * window * (NOPE + ROPE + VDIM)
    return pl.pallas_call(
        kernel,
        grid_spec=pltpu.PrefetchScalarGridSpec(
            num_scalar_prefetch=1,
            grid=(heads,),
            in_specs=[
                pl.BlockSpec((1, block, NOPE + ROPE), lambda h, b: (h, b[0], 0)),
                pl.BlockSpec((1, total_rows, NOPE), lambda h, b: (h, 0, 0)),
                pl.BlockSpec((total_rows, ROPE), lambda h, b: (0, 0)),
                pl.BlockSpec((1, total_rows, VDIM), lambda h, b: (h, 0, 0)),
                pl.BlockSpec((block, 1), lambda h, b: (b[0], 0)),
                pl.BlockSpec((1, total_rows), lambda h, b: (0, 0)),
            ],
            out_specs=pl.BlockSpec((1, block, VDIM), lambda h, b: (h, 0, 0)),
            scratch_shapes=[pltpu.VMEM((block, window), jnp.float32)],
        ),
        out_shape=jax.ShapeDtypeStruct((heads, block, VDIM), jnp.bfloat16),
        cost_estimate=pl.CostEstimate(
            flops=flops,
            transcendentals=heads * block * window,
            bytes_accessed=2 * heads * (block * (NOPE + ROPE + VDIM) + window * (NOPE + VDIM)),
        ),
    )(
        jnp.reshape(index, (1,)).astype(jnp.int32),
        query,
        key_nope,
        key_rope,
        value,
        group_ids.reshape(total_rows, 1),
        group_ids.reshape(1, total_rows),
    )


def body(
    hidden_states,
    input_gain,
    query_down,
    memory_down,
    query_gain,
    memory_gain,
    query_up,
    key_up,
    value_up,
    segment_ids,
):
    tok_count = hidden_states.shape[0]
    seq_count = lax.axis_size("seq")
    tp_count = lax.axis_size("tp")
    seq_index = lax.axis_index("seq")
    tp_index = lax.axis_index("tp")
    width = hidden_states.shape[1] * tp_count
    total_rows = tok_count * seq_count
    doc_most = total_rows // 4
    qrank_piece = query_down.shape[1]
    memory_piece = memory_down.shape[1]
    qrank = qrank_piece * seq_count
    memory_cols = memory_piece * seq_count

    group_ids = lax.all_gather(segment_ids, "seq", axis=0, tiled=True)

    inputs = hidden_states.astype(jnp.float32)
    square_sums = lax.psum(jnp.sum(inputs * inputs, 1), "tp")
    normed = (inputs * lax.rsqrt(square_sums / width + epsilon)[:, None] * input_gain).astype(
        jnp.bfloat16
    )

    dp_index = lax.axis_index("dp")
    dp_count = lax.axis_size("dp")
    down_piece = jnp.concatenate([query_down, memory_down], 1)
    half_rows = down_piece.shape[0] // dp_count
    own_rows = lax.dynamic_slice_in_dim(down_piece, dp_index * half_rows, half_rows, 0)
    own_all = lax.all_gather(own_rows, "seq", axis=1, tiled=True)
    own_all, normed, group_ids = lax.optimization_barrier((own_all, normed, group_ids))
    partial = jnp.dot(
        lax.dynamic_slice_in_dim(normed, dp_index * half_rows, half_rows, 1),
        own_all,
        preferred_element_type=jnp.float32,
    )
    for shift in range(1, dp_count):
        peer = (dp_index + dp_count - shift) % dp_count
        peer_all = lax.ppermute(
            own_all, "dp", perm=[(i, (i + shift) % dp_count) for i in range(dp_count)]
        )
        partial = partial + jnp.dot(
            lax.dynamic_slice_in_dim(normed, peer * half_rows, half_rows, 1),
            peer_all,
            preferred_element_type=jnp.float32,
        )
    pieces = partial.reshape(tp_count, partial.shape[0] // tp_count, partial.shape[1])
    latent_rows = lax.dynamic_index_in_dim(pieces, tp_index, 0, keepdims=False)
    for k in range(1, tp_count):
        sent = lax.dynamic_index_in_dim(pieces, (tp_index + k) % tp_count, 0, keepdims=False)
        latent_rows = latent_rows + lax.ppermute(
            sent, "tp", perm=[(i, (i + k) % tp_count) for i in range(tp_count)]
        )
    latent_rows, query_up, key_up, value_up = lax.optimization_barrier(
        (latent_rows, query_up, key_up, value_up)
    )

    token_index = jnp.arange(total_rows, dtype=jnp.int32)
    onehot = group_ids[:, None] == jnp.arange(DOCS, dtype=jnp.int32)[None, :]
    starts = jnp.min(jnp.where(onehot, token_index[:, None], total_rows), 0)
    position = token_index - jnp.sum(jnp.where(onehot, starts[None, :], 0), 1)
    chunk = latent_rows.shape[0]
    latent_rows = latent_rows.reshape(chunk, seq_count, qrank_piece + memory_piece)
    query_sums = latent_rows[:, :, :qrank_piece].reshape(chunk, qrank)
    memory_sums = latent_rows[:, :, qrank_piece:].reshape(chunk, memory_cols)
    chunk_position = lax.dynamic_slice(
        position, (seq_index * tok_count + tp_index * chunk,), (chunk,)
    )
    compressed_query = rms_scale(query_sums, query_gain).astype(jnp.bfloat16)
    compressed_memory = rms_scale(memory_sums[:, :KVRANK], memory_gain).astype(jnp.bfloat16)
    key_rope = rotate(memory_sums[:, KVRANK:], chunk_position).astype(jnp.bfloat16)
    packed = jnp.concatenate([compressed_query, compressed_memory, key_rope], 1)
    from_seq = [packed] + [
        lax.ppermute(packed, "seq", perm=[(i, (i + k) % seq_count) for i in range(seq_count)])
        for k in range(1, seq_count)
    ]
    packed = jnp.take(jnp.stack(from_seq), (seq_index - jnp.arange(seq_count)) % seq_count, axis=0)
    packed = lax.all_gather(packed, "tp", axis=0, tiled=False)
    latent = jnp.transpose(packed, (1, 0, 2, 3)).reshape(total_rows, packed.shape[-1])
    cq_all = latent[:, :qrank]
    cm_all = latent[:, qrank : qrank + KVRANK]
    rope_all = latent[:, qrank + KVRANK :]

    local_heads = query_up.shape[1] // (NOPE + ROPE)
    heads = local_heads // seq_count

    def head_columns(weight, head_width):
        rows = weight.shape[0]
        cols = heads * head_width // dp_count
        own = lax.dynamic_slice_in_dim(
            weight.reshape(rows, seq_count, heads * head_width), dp_index * cols, cols, 2
        )
        own = lax.all_to_all(own, "seq", split_axis=1, concat_axis=0, tiled=True)
        own = own.reshape(rows * seq_count, cols)
        pieces = [own]
        for shift in range(1, dp_count):
            pieces.append(
                lax.ppermute(
                    own, "dp", perm=[(i, (i + shift) % dp_count) for i in range(dp_count)]
                )
            )
        ordered = []
        for core in range(dp_count):
            pick = pieces[0]
            for k in range(1, dp_count):
                pick = jnp.where((dp_index + dp_count - k) % dp_count == core, pieces[k], pick)
            ordered.append(pick)
        return jnp.concatenate(ordered, 1)

    query_w = head_columns(query_up, NOPE + ROPE)
    key_w = head_columns(key_up, NOPE)
    value_w = head_columns(value_up, VDIM)

    query_full = jnp.einsum(
        "td,dhe->hte",
        cq_all,
        query_w.reshape(qrank, heads, NOPE + ROPE),
        preferred_element_type=jnp.float32,
    )
    query = jnp.concatenate(
        [query_full[..., :NOPE], rotate(query_full[..., NOPE:], position[None, :])], -1
    ).astype(jnp.bfloat16)
    key_nope = jnp.einsum(
        "td,dhe->hte", cm_all, key_w.reshape(KVRANK, heads, NOPE), preferred_element_type=jnp.float32
    ).astype(jnp.bfloat16)
    value = jnp.einsum(
        "td,dhe->hte", cm_all, value_w.reshape(KVRANK, heads, VDIM), preferred_element_type=jnp.float32
    ).astype(jnp.bfloat16)
    score_scale = (NOPE + ROPE) ** (-0.5)
    received = [None] * seq_count
    shifts = [k for k in range(seq_count - 1, 0, -1) if k % 2]
    shifts = shifts + [k for k in range(seq_count - 1, 0, -1) if k % 2 == 0] + [0]
    for k in shifts:
        rows = block_attention(
            query, key_nope, rope_all, value, group_ids, score_scale, doc_most, tok_count,
            (seq_index + k) % seq_count,
        )
        if k:
            rows = lax.ppermute(
                rows, "seq", perm=[(i, (i + k) % seq_count) for i in range(seq_count)]
            )
        received[k] = rows
    attended = jnp.take(
        jnp.stack(received), (seq_index - jnp.arange(seq_count)) % seq_count, axis=0
    )
    attended = jnp.transpose(attended, (2, 0, 1, 3))
    return attended.reshape(tok_count, local_heads * VDIM)


def solution(mesh):
    in_specs = (
        P(("dp", "seq"), "tp"),
        P("tp"),
        P("tp", "seq"),
        P("tp", "seq"),
        P(),
        P(),
        P("seq", "tp"),
        P("seq", "tp"),
        P("seq", "tp"),
        P(("dp", "seq")),
    )
    out_specs = P(("dp", "seq"), "tp")
    return jax.shard_map(body, mesh=mesh, in_specs=in_specs, out_specs=out_specs, check_vma=False)
```

```python
import functools

import jax
import jax.numpy as jnp
from jax import lax
from jax.experimental import pallas as pl
from jax.experimental.pallas import tpu as pltpu
from jax.sharding import PartitionSpec as P

KVRANK = 512
NOPE = 128
ROPE = 64
VDIM = 128
DOCS = 12


epsilon = 1e-06


def rms_scale(entries, gain_vector):
    return (
        entries * lax.rsqrt(jnp.mean(entries * entries, -1, keepdims=True) + epsilon) * gain_vector
    )


def rotate(entries, position):
    half_width = entries.shape[-1] // 2
    frequency = jnp.power(10000.0, -2.0 * jnp.arange(half_width, dtype=jnp.float32) / ROPE)
    angles = position.astype(jnp.float32)[..., None] * frequency
    cosine = jnp.cos(angles)
    sine_part = jnp.sin(angles)
    first_half = entries[..., :half_width]
    second_half = entries[..., half_width:]
    return jnp.concatenate(
        [
            first_half * cosine - second_half * sine_part,
            second_half * cosine + first_half * sine_part,
        ],
        -1,
    )


def heads_attention(query_all, key_all, value_all, group_ids, score_scale, doc_most):
    total_rows = query_all.shape[0]
    block_rows = min(512, total_rows)
    key_index = jnp.arange(total_rows, dtype=jnp.int32)
    results = []
    for block in range(total_rows // block_rows):
        lower = block * block_rows
        upper = lower + block_rows
        key_low = max(0, lower - doc_most)
        scores = (
            jnp.einsum(
                "qhd,khd->hqk",
                query_all[lower:upper],
                key_all[key_low:upper],
                preferred_element_type=jnp.float32,
            )
            * score_scale
        )
        allowed = (group_ids[lower:upper, None] == group_ids[None, key_low:upper]) & (
            key_index[lower:upper, None] >= key_index[None, key_low:upper]
        )
        scores = jnp.where(allowed[None], scores, -jnp.inf)
        row_max = jnp.max(scores, -1, keepdims=True)
        probs_full = jnp.exp(scores - row_max)
        denominator = jnp.sum(probs_full, -1)
        weights = probs_full.astype(jnp.bfloat16)
        weighted = jnp.einsum(
            "hqk,khd->qhd", weights, value_all[key_low:upper], preferred_element_type=jnp.float32
        )
        results.append((weighted / jnp.transpose(denominator)[:, :, None]).astype(jnp.bfloat16))
    return jnp.concatenate(results, 0)


def attention_kernel(
    block_ref, query_ref, key_ref, rope_ref, value_ref, ids_col_ref, ids_row_ref, out_ref, bias_ref, *, block, window, doc_most, scale
):
    lower = block_ref[0] * block
    start = pl.multiple_of(jnp.maximum(lower - doc_most, 0), block)

    @pl.when(pl.program_id(0) == 0)
    def _():
        query_index = lower + lax.broadcasted_iota(jnp.int32, (block, window), 0)
        key_index = start + lax.broadcasted_iota(jnp.int32, (block, window), 1)
        allowed = (ids_col_ref[...] == ids_row_ref[:, pl.ds(start, window)]) & (
            query_index >= key_index
        )
        bias_ref[...] = jnp.where(allowed, 0.0, -jnp.inf).astype(jnp.float32)

    query = query_ref[0]
    keys = key_ref[0, pl.ds(start, window), :]
    rope = rope_ref[pl.ds(start, window), :]
    values = value_ref[0, pl.ds(start, window), :]
    dims = (((1,), (1,)), ((), ()))
    scores = lax.dot_general(query[:, :NOPE], keys, dims, preferred_element_type=jnp.float32)
    scores = scores + lax.dot_general(
        query[:, NOPE:], rope, dims, preferred_element_type=jnp.float32
    )
    scores = scores * scale + bias_ref[...]
    row_max = jnp.max(scores, -1, keepdims=True)
    probs = jnp.exp(scores - row_max)
    denominator = jnp.sum(probs, -1, keepdims=True)
    weighted = jnp.dot(probs.astype(jnp.bfloat16), values, preferred_element_type=jnp.float32)
    out_ref[0] = (weighted / denominator).astype(out_ref.dtype)


def block_attention(query, key_nope, key_rope, value, group_ids, score_scale, doc_most, block, index):
    heads, total_rows, _ = query.shape
    window = min(total_rows, doc_most + block)
    kernel = functools.partial(
        attention_kernel, block=block, window=window, doc_most=doc_most, scale=score_scale
    )
    flops = 2 * heads * block * window * (NOPE + ROPE + VDIM)
    return pl.pallas_call(
        kernel,
        grid_spec=pltpu.PrefetchScalarGridSpec(
            num_scalar_prefetch=1,
            grid=(heads,),
            in_specs=[
                pl.BlockSpec((1, block, NOPE + ROPE), lambda h, b: (h, b[0], 0)),
                pl.BlockSpec((1, total_rows, NOPE), lambda h, b: (h, 0, 0)),
                pl.BlockSpec((total_rows, ROPE), lambda h, b: (0, 0)),
                pl.BlockSpec((1, total_rows, VDIM), lambda h, b: (h, 0, 0)),
                pl.BlockSpec((block, 1), lambda h, b: (b[0], 0)),
                pl.BlockSpec((1, total_rows), lambda h, b: (0, 0)),
            ],
            out_specs=pl.BlockSpec((1, block, VDIM), lambda h, b: (h, 0, 0)),
            scratch_shapes=[pltpu.VMEM((block, window), jnp.float32)],
        ),
        out_shape=jax.ShapeDtypeStruct((heads, block, VDIM), jnp.bfloat16),
        cost_estimate=pl.CostEstimate(
            flops=flops,
            transcendentals=heads * block * window,
            bytes_accessed=2 * heads * (block * (NOPE + ROPE + VDIM) + window * (NOPE + VDIM)),
        ),
    )(
        jnp.reshape(index, (1,)).astype(jnp.int32),
        query,
        key_nope,
        key_rope,
        value,
        group_ids.reshape(total_rows, 1),
        group_ids.reshape(1, total_rows),
    )


def body(
    hidden_states,
    input_gain,
    query_down,
    memory_down,
    query_gain,
    memory_gain,
    query_up,
    key_up,
    value_up,
    segment_ids,
):
    tok_count = hidden_states.shape[0]
    seq_count = lax.axis_size("seq")
    tp_count = lax.axis_size("tp")
    seq_index = lax.axis_index("seq")
    tp_index = lax.axis_index("tp")
    width = hidden_states.shape[1] * tp_count
    total_rows = tok_count * seq_count
    doc_most = total_rows // 4
    qrank_piece = query_down.shape[1]
    memory_piece = memory_down.shape[1]
    qrank = qrank_piece * seq_count
    memory_cols = memory_piece * seq_count

    group_ids = lax.all_gather(segment_ids, "seq", axis=0, tiled=True)

    inputs = hidden_states.astype(jnp.float32)
    square_sums = lax.psum(jnp.sum(inputs * inputs, 1), "tp")
    normed = (inputs * lax.rsqrt(square_sums / width + epsilon)[:, None] * input_gain).astype(
        jnp.bfloat16
    )

    dp_index = lax.axis_index("dp")
    dp_count = lax.axis_size("dp")
    down_piece = jnp.concatenate([query_down, memory_down], 1)
    half_rows = down_piece.shape[0] // dp_count
    own_rows = lax.dynamic_slice_in_dim(down_piece, dp_index * half_rows, half_rows, 0)
    own_all = lax.all_gather(own_rows, "seq", axis=1, tiled=True)
    own_all, normed, group_ids = lax.optimization_barrier((own_all, normed, group_ids))
    partial = jnp.dot(
        lax.dynamic_slice_in_dim(normed, dp_index * half_rows, half_rows, 1),
        own_all,
        preferred_element_type=jnp.float32,
    )
    for shift in range(1, dp_count):
        peer = (dp_index + dp_count - shift) % dp_count
        peer_all = lax.ppermute(
            own_all, "dp", perm=[(i, (i + shift) % dp_count) for i in range(dp_count)]
        )
        partial = partial + jnp.dot(
            lax.dynamic_slice_in_dim(normed, peer * half_rows, half_rows, 1),
            peer_all,
            preferred_element_type=jnp.float32,
        )
    pieces = partial.reshape(tp_count, partial.shape[0] // tp_count, partial.shape[1])
    latent_rows = lax.dynamic_index_in_dim(pieces, tp_index, 0, keepdims=False)
    by_xor = tp_count & (tp_count - 1) == 0
    for k in range(1, tp_count):
        partner = [(i ^ k) if by_xor else (i + k) % tp_count for i in range(tp_count)]
        target = (tp_index ^ k) if by_xor else (tp_index + k) % tp_count
        sent = lax.dynamic_index_in_dim(pieces, target, 0, keepdims=False)
        latent_rows = latent_rows + lax.ppermute(
            sent, "tp", perm=[(i, partner[i]) for i in range(tp_count)]
        )

    token_index = jnp.arange(total_rows, dtype=jnp.int32)
    onehot = group_ids[:, None] == jnp.arange(DOCS, dtype=jnp.int32)[None, :]
    starts = jnp.min(jnp.where(onehot, token_index[:, None], total_rows), 0)
    position = token_index - jnp.sum(jnp.where(onehot, starts[None, :], 0), 1)
    chunk = latent_rows.shape[0]
    latent_rows = latent_rows.reshape(chunk, seq_count, qrank_piece + memory_piece)
    query_sums = latent_rows[:, :, :qrank_piece].reshape(chunk, qrank)
    memory_sums = latent_rows[:, :, qrank_piece:].reshape(chunk, memory_cols)
    chunk_position = lax.dynamic_slice(
        position, (seq_index * tok_count + tp_index * chunk,), (chunk,)
    )
    compressed_query = rms_scale(query_sums, query_gain).astype(jnp.bfloat16)
    compressed_memory = rms_scale(memory_sums[:, :KVRANK], memory_gain).astype(jnp.bfloat16)
    key_rope = rotate(memory_sums[:, KVRANK:], chunk_position).astype(jnp.bfloat16)
    packed = jnp.concatenate([compressed_query, compressed_memory, key_rope], 1)
    from_seq = [packed] + [
        lax.ppermute(packed, "seq", perm=[(i, (i + k) % seq_count) for i in range(seq_count)])
        for k in range(1, seq_count)
    ]
    packed = jnp.take(jnp.stack(from_seq), (seq_index - jnp.arange(seq_count)) % seq_count, axis=0)
    packed, query_up, key_up, value_up = lax.optimization_barrier(
        (packed, query_up, key_up, value_up)
    )
    packed = lax.all_gather(packed, "tp", axis=0, tiled=False)
    latent = jnp.transpose(packed, (1, 0, 2, 3)).reshape(total_rows, packed.shape[-1])
    cq_all = latent[:, :qrank]
    cm_all = latent[:, qrank : qrank + KVRANK]
    rope_all = latent[:, qrank + KVRANK :]

    local_heads = query_up.shape[1] // (NOPE + ROPE)
    heads = local_heads // seq_count

    def head_columns(weight, head_width):
        rows = weight.shape[0]
        cols = heads * head_width // dp_count
        own = lax.dynamic_slice_in_dim(
            weight.reshape(rows, seq_count, heads * head_width), dp_index * cols, cols, 2
        )
        own = lax.all_to_all(own, "seq", split_axis=1, concat_axis=0, tiled=True)
        own = own.reshape(rows * seq_count, cols)
        pieces = [own]
        for shift in range(1, dp_count):
            pieces.append(
                lax.ppermute(
                    own, "dp", perm=[(i, (i + shift) % dp_count) for i in range(dp_count)]
                )
            )
        ordered = []
        for core in range(dp_count):
            pick = pieces[0]
            for k in range(1, dp_count):
                pick = jnp.where((dp_index + dp_count - k) % dp_count == core, pieces[k], pick)
            ordered.append(pick)
        return jnp.concatenate(ordered, 1)

    query_w = head_columns(query_up, NOPE + ROPE)
    key_w = head_columns(key_up, NOPE)
    value_w = head_columns(value_up, VDIM)

    query_full = jnp.einsum(
        "td,dhe->hte",
        cq_all,
        query_w.reshape(qrank, heads, NOPE + ROPE),
        preferred_element_type=jnp.float32,
    )
    query = jnp.concatenate(
        [query_full[..., :NOPE], rotate(query_full[..., NOPE:], position[None, :])], -1
    ).astype(jnp.bfloat16)
    key_nope = jnp.einsum(
        "td,dhe->hte", cm_all, key_w.reshape(KVRANK, heads, NOPE), preferred_element_type=jnp.float32
    ).astype(jnp.bfloat16)
    value = jnp.einsum(
        "td,dhe->hte", cm_all, value_w.reshape(KVRANK, heads, VDIM), preferred_element_type=jnp.float32
    ).astype(jnp.bfloat16)
    score_scale = (NOPE + ROPE) ** (-0.5)
    received = [None] * seq_count
    shifts = [k for k in range(seq_count - 1, 0, -1) if k % 2]
    shifts = shifts + [k for k in range(seq_count - 1, 0, -1) if k % 2 == 0] + [0]
    for k in shifts:
        rows = block_attention(
            query, key_nope, rope_all, value, group_ids, score_scale, doc_most, tok_count,
            (seq_index + k) % seq_count,
        )
        if k:
            rows = lax.ppermute(
                rows, "seq", perm=[(i, (i + k) % seq_count) for i in range(seq_count)]
            )
        received[k] = rows
    attended = jnp.take(
        jnp.stack(received), (seq_index - jnp.arange(seq_count)) % seq_count, axis=0
    )
    attended = jnp.transpose(attended, (2, 0, 1, 3))
    return attended.reshape(tok_count, local_heads * VDIM)


def solution(mesh):
    in_specs = (
        P(("dp", "seq"), "tp"),
        P("tp"),
        P("tp", "seq"),
        P("tp", "seq"),
        P(),
        P(),
        P("seq", "tp"),
        P("seq", "tp"),
        P("seq", "tp"),
        P(("dp", "seq")),
    )
    out_specs = P(("dp", "seq"), "tp")
    return jax.shard_map(body, mesh=mesh, in_specs=in_specs, out_specs=out_specs, check_vma=False)
```

```python
import functools

import jax
import jax.numpy as jnp
from jax import lax
from jax.experimental import pallas as pl
from jax.experimental.pallas import tpu as pltpu
from jax.sharding import PartitionSpec as P

KVRANK = 512
NOPE = 128
ROPE = 64
VDIM = 128
DOCS = 12


epsilon = 1e-06


def rms_scale(entries, gain_vector):
    return (
        entries * lax.rsqrt(jnp.mean(entries * entries, -1, keepdims=True) + epsilon) * gain_vector
    )


def rotate(entries, position):
    half_width = entries.shape[-1] // 2
    frequency = jnp.power(10000.0, -2.0 * jnp.arange(half_width, dtype=jnp.float32) / ROPE)
    angles = position.astype(jnp.float32)[..., None] * frequency
    cosine = jnp.cos(angles)
    sine_part = jnp.sin(angles)
    first_half = entries[..., :half_width]
    second_half = entries[..., half_width:]
    return jnp.concatenate(
        [
            first_half * cosine - second_half * sine_part,
            second_half * cosine + first_half * sine_part,
        ],
        -1,
    )


def heads_attention(query_all, key_all, value_all, group_ids, score_scale, doc_most):
    total_rows = query_all.shape[0]
    block_rows = min(512, total_rows)
    key_index = jnp.arange(total_rows, dtype=jnp.int32)
    results = []
    for block in range(total_rows // block_rows):
        lower = block * block_rows
        upper = lower + block_rows
        key_low = max(0, lower - doc_most)
        scores = (
            jnp.einsum(
                "qhd,khd->hqk",
                query_all[lower:upper],
                key_all[key_low:upper],
                preferred_element_type=jnp.float32,
            )
            * score_scale
        )
        allowed = (group_ids[lower:upper, None] == group_ids[None, key_low:upper]) & (
            key_index[lower:upper, None] >= key_index[None, key_low:upper]
        )
        scores = jnp.where(allowed[None], scores, -jnp.inf)
        row_max = jnp.max(scores, -1, keepdims=True)
        probs_full = jnp.exp(scores - row_max)
        denominator = jnp.sum(probs_full, -1)
        weights = probs_full.astype(jnp.bfloat16)
        weighted = jnp.einsum(
            "hqk,khd->qhd", weights, value_all[key_low:upper], preferred_element_type=jnp.float32
        )
        results.append((weighted / jnp.transpose(denominator)[:, :, None]).astype(jnp.bfloat16))
    return jnp.concatenate(results, 0)


def attention_kernel(
    block_ref, query_ref, key_ref, rope_ref, value_ref, ids_col_ref, ids_row_ref, out_ref, bias_ref, *, block, window, doc_most, scale
):
    lower = block_ref[0] * block
    start = pl.multiple_of(jnp.maximum(lower - doc_most, 0), block)

    @pl.when(pl.program_id(0) == 0)
    def _():
        query_index = lower + lax.broadcasted_iota(jnp.int32, (block, window), 0)
        key_index = start + lax.broadcasted_iota(jnp.int32, (block, window), 1)
        allowed = (ids_col_ref[...] == ids_row_ref[:, pl.ds(start, window)]) & (
            query_index >= key_index
        )
        bias_ref[...] = jnp.where(allowed, 0.0, -jnp.inf).astype(jnp.float32)

    rope = rope_ref[pl.ds(start, window), :]
    dims = (((1,), (1,)), ((), ()))
    for head in range(query_ref.shape[0]):
        query = query_ref[head]
        keys = key_ref[head, pl.ds(start, window), :]
        values = value_ref[head, pl.ds(start, window), :]
        scores = lax.dot_general(query[:, :NOPE], keys, dims, preferred_element_type=jnp.float32)
        scores = scores + lax.dot_general(
            query[:, NOPE:], rope, dims, preferred_element_type=jnp.float32
        )
        scores = scores * scale + bias_ref[...]
        row_max = jnp.max(scores, -1, keepdims=True)
        probs = jnp.exp(scores - row_max)
        denominator = jnp.sum(probs, -1, keepdims=True)
        weighted = jnp.dot(probs.astype(jnp.bfloat16), values, preferred_element_type=jnp.float32)
        out_ref[head] = (weighted / denominator).astype(out_ref.dtype)


def block_attention(query, key_nope, key_rope, value, group_ids, score_scale, doc_most, block, index):
    heads, total_rows, _ = query.shape
    window = min(total_rows, doc_most + block)
    kernel = functools.partial(
        attention_kernel, block=block, window=window, doc_most=doc_most, scale=score_scale
    )
    flops = 2 * heads * block * window * (NOPE + ROPE + VDIM)
    step = 2 if heads % 2 == 0 else 1
    return pl.pallas_call(
        kernel,
        grid_spec=pltpu.PrefetchScalarGridSpec(
            num_scalar_prefetch=1,
            grid=(heads // step,),
            in_specs=[
                pl.BlockSpec((step, block, NOPE + ROPE), lambda h, b: (h, b[0], 0)),
                pl.BlockSpec((step, total_rows, NOPE), lambda h, b: (h, 0, 0)),
                pl.BlockSpec((total_rows, ROPE), lambda h, b: (0, 0)),
                pl.BlockSpec((step, total_rows, VDIM), lambda h, b: (h, 0, 0)),
                pl.BlockSpec((block, 1), lambda h, b: (b[0], 0)),
                pl.BlockSpec((1, total_rows), lambda h, b: (0, 0)),
            ],
            out_specs=pl.BlockSpec((step, block, VDIM), lambda h, b: (h, 0, 0)),
            scratch_shapes=[pltpu.VMEM((block, window), jnp.float32)],
        ),
        out_shape=jax.ShapeDtypeStruct((heads, block, VDIM), jnp.bfloat16),
        cost_estimate=pl.CostEstimate(
            flops=flops,
            transcendentals=heads * block * window,
            bytes_accessed=2 * heads * (block * (NOPE + ROPE + VDIM) + window * (NOPE + VDIM)),
        ),
    )(
        jnp.reshape(index, (1,)).astype(jnp.int32),
        query,
        key_nope,
        key_rope,
        value,
        group_ids.reshape(total_rows, 1),
        group_ids.reshape(1, total_rows),
    )


def body(
    hidden_states,
    input_gain,
    query_down,
    memory_down,
    query_gain,
    memory_gain,
    query_up,
    key_up,
    value_up,
    segment_ids,
):
    tok_count = hidden_states.shape[0]
    seq_count = lax.axis_size("seq")
    tp_count = lax.axis_size("tp")
    seq_index = lax.axis_index("seq")
    tp_index = lax.axis_index("tp")
    width = hidden_states.shape[1] * tp_count
    total_rows = tok_count * seq_count
    doc_most = total_rows // 4
    qrank_piece = query_down.shape[1]
    memory_piece = memory_down.shape[1]
    qrank = qrank_piece * seq_count
    memory_cols = memory_piece * seq_count

    group_ids = lax.all_gather(segment_ids, "seq", axis=0, tiled=True)

    inputs = hidden_states.astype(jnp.float32)
    square_sums = lax.psum(jnp.sum(inputs * inputs, 1), "tp")
    normed = (inputs * lax.rsqrt(square_sums / width + epsilon)[:, None] * input_gain).astype(
        jnp.bfloat16
    )

    dp_index = lax.axis_index("dp")
    dp_count = lax.axis_size("dp")
    down_piece = jnp.concatenate([query_down, memory_down], 1)
    half_rows = down_piece.shape[0] // dp_count
    own_rows = lax.dynamic_slice_in_dim(down_piece, dp_index * half_rows, half_rows, 0)
    own_all = lax.all_gather(own_rows, "seq", axis=1, tiled=True)
    own_all, normed, group_ids = lax.optimization_barrier((own_all, normed, group_ids))
    partial = jnp.dot(
        lax.dynamic_slice_in_dim(normed, dp_index * half_rows, half_rows, 1),
        own_all,
        preferred_element_type=jnp.float32,
    )
    for shift in range(1, dp_count):
        peer = (dp_index + dp_count - shift) % dp_count
        peer_all = lax.ppermute(
            own_all, "dp", perm=[(i, (i + shift) % dp_count) for i in range(dp_count)]
        )
        partial = partial + jnp.dot(
            lax.dynamic_slice_in_dim(normed, peer * half_rows, half_rows, 1),
            peer_all,
            preferred_element_type=jnp.float32,
        )
    pieces = partial.reshape(tp_count, partial.shape[0] // tp_count, partial.shape[1])
    latent_rows = lax.dynamic_index_in_dim(pieces, tp_index, 0, keepdims=False)
    for k in range(1, tp_count):
        sent = lax.dynamic_index_in_dim(pieces, (tp_index + k) % tp_count, 0, keepdims=False)
        latent_rows = latent_rows + lax.ppermute(
            sent, "tp", perm=[(i, (i + k) % tp_count) for i in range(tp_count)]
        )

    token_index = jnp.arange(total_rows, dtype=jnp.int32)
    onehot = group_ids[:, None] == jnp.arange(DOCS, dtype=jnp.int32)[None, :]
    starts = jnp.min(jnp.where(onehot, token_index[:, None], total_rows), 0)
    position = token_index - jnp.sum(jnp.where(onehot, starts[None, :], 0), 1)
    chunk = latent_rows.shape[0]
    latent_rows = latent_rows.reshape(chunk, seq_count, qrank_piece + memory_piece)
    query_sums = latent_rows[:, :, :qrank_piece].reshape(chunk, qrank)
    memory_sums = latent_rows[:, :, qrank_piece:].reshape(chunk, memory_cols)
    chunk_position = lax.dynamic_slice(
        position, (seq_index * tok_count + tp_index * chunk,), (chunk,)
    )
    compressed_query = rms_scale(query_sums, query_gain).astype(jnp.bfloat16)
    compressed_memory = rms_scale(memory_sums[:, :KVRANK], memory_gain).astype(jnp.bfloat16)
    key_rope = rotate(memory_sums[:, KVRANK:], chunk_position).astype(jnp.bfloat16)
    packed = jnp.concatenate([compressed_query, compressed_memory, key_rope], 1)
    from_seq = [packed] + [
        lax.ppermute(packed, "seq", perm=[(i, (i + k) % seq_count) for i in range(seq_count)])
        for k in range(1, seq_count)
    ]
    packed = jnp.take(jnp.stack(from_seq), (seq_index - jnp.arange(seq_count)) % seq_count, axis=0)
    packed, query_up, key_up, value_up = lax.optimization_barrier(
        (packed, query_up, key_up, value_up)
    )
    packed = lax.all_gather(packed, "tp", axis=0, tiled=False)
    latent = jnp.transpose(packed, (1, 0, 2, 3)).reshape(total_rows, packed.shape[-1])
    cq_all = latent[:, :qrank]
    cm_all = latent[:, qrank : qrank + KVRANK]
    rope_all = latent[:, qrank + KVRANK :]

    local_heads = query_up.shape[1] // (NOPE + ROPE)
    heads = local_heads // seq_count

    def head_columns(weight, head_width):
        rows = weight.shape[0]
        cols = heads * head_width // dp_count
        own = lax.dynamic_slice_in_dim(
            weight.reshape(rows, seq_count, heads * head_width), dp_index * cols, cols, 2
        )
        own = lax.all_to_all(own, "seq", split_axis=1, concat_axis=0, tiled=True)
        own = own.reshape(rows * seq_count, cols)
        pieces = [own]
        for shift in range(1, dp_count):
            pieces.append(
                lax.ppermute(
                    own, "dp", perm=[(i, (i + shift) % dp_count) for i in range(dp_count)]
                )
            )
        ordered = []
        for core in range(dp_count):
            pick = pieces[0]
            for k in range(1, dp_count):
                pick = jnp.where((dp_index + dp_count - k) % dp_count == core, pieces[k], pick)
            ordered.append(pick)
        return jnp.concatenate(ordered, 1)

    query_w = head_columns(query_up, NOPE + ROPE)
    key_w = head_columns(key_up, NOPE)
    value_w = head_columns(value_up, VDIM)

    query_full = jnp.einsum(
        "td,dhe->hte",
        cq_all,
        query_w.reshape(qrank, heads, NOPE + ROPE),
        preferred_element_type=jnp.float32,
    )
    query = jnp.concatenate(
        [query_full[..., :NOPE], rotate(query_full[..., NOPE:], position[None, :])], -1
    ).astype(jnp.bfloat16)
    key_nope = jnp.einsum(
        "td,dhe->hte", cm_all, key_w.reshape(KVRANK, heads, NOPE), preferred_element_type=jnp.float32
    ).astype(jnp.bfloat16)
    value = jnp.einsum(
        "td,dhe->hte", cm_all, value_w.reshape(KVRANK, heads, VDIM), preferred_element_type=jnp.float32
    ).astype(jnp.bfloat16)
    score_scale = (NOPE + ROPE) ** (-0.5)
    received = [None] * seq_count
    shifts = [k for k in range(seq_count - 1, 0, -1) if k % 2]
    shifts = shifts + [k for k in range(seq_count - 1, 0, -1) if k % 2 == 0] + [0]
    for k in shifts:
        rows = block_attention(
            query, key_nope, rope_all, value, group_ids, score_scale, doc_most, tok_count,
            (seq_index + k) % seq_count,
        )
        if k:
            rows = lax.ppermute(
                rows, "seq", perm=[(i, (i + k) % seq_count) for i in range(seq_count)]
            )
        received[k] = rows
    attended = jnp.take(
        jnp.stack(received), (seq_index - jnp.arange(seq_count)) % seq_count, axis=0
    )
    attended = jnp.transpose(attended, (2, 0, 1, 3))
    return attended.reshape(tok_count, local_heads * VDIM)


def solution(mesh):
    in_specs = (
        P(("dp", "seq"), "tp"),
        P("tp"),
        P("tp", "seq"),
        P("tp", "seq"),
        P(),
        P(),
        P("seq", "tp"),
        P("seq", "tp"),
        P("seq", "tp"),
        P(("dp", "seq")),
    )
    out_specs = P(("dp", "seq"), "tp")
    return jax.shard_map(body, mesh=mesh, in_specs=in_specs, out_specs=out_specs, check_vma=False)
```

```python
import functools

import jax
import jax.numpy as jnp
from jax import lax
from jax.experimental import pallas as pl
from jax.experimental.pallas import tpu as pltpu
from jax.sharding import PartitionSpec as P

KVRANK = 512
NOPE = 128
ROPE = 64
VDIM = 128
DOCS = 12


epsilon = 1e-06


def rms_scale(entries, gain_vector):
    return (
        entries * lax.rsqrt(jnp.mean(entries * entries, -1, keepdims=True) + epsilon) * gain_vector
    )


def rotate(entries, position):
    half_width = entries.shape[-1] // 2
    frequency = jnp.power(10000.0, -2.0 * jnp.arange(half_width, dtype=jnp.float32) / ROPE)
    angles = position.astype(jnp.float32)[..., None] * frequency
    cosine = jnp.cos(angles)
    sine_part = jnp.sin(angles)
    first_half = entries[..., :half_width]
    second_half = entries[..., half_width:]
    return jnp.concatenate(
        [
            first_half * cosine - second_half * sine_part,
            second_half * cosine + first_half * sine_part,
        ],
        -1,
    )


def heads_attention(query_all, key_all, value_all, group_ids, score_scale, doc_most):
    total_rows = query_all.shape[0]
    block_rows = min(512, total_rows)
    key_index = jnp.arange(total_rows, dtype=jnp.int32)
    results = []
    for block in range(total_rows // block_rows):
        lower = block * block_rows
        upper = lower + block_rows
        key_low = max(0, lower - doc_most)
        scores = (
            jnp.einsum(
                "qhd,khd->hqk",
                query_all[lower:upper],
                key_all[key_low:upper],
                preferred_element_type=jnp.float32,
            )
            * score_scale
        )
        allowed = (group_ids[lower:upper, None] == group_ids[None, key_low:upper]) & (
            key_index[lower:upper, None] >= key_index[None, key_low:upper]
        )
        scores = jnp.where(allowed[None], scores, -jnp.inf)
        row_max = jnp.max(scores, -1, keepdims=True)
        probs_full = jnp.exp(scores - row_max)
        denominator = jnp.sum(probs_full, -1)
        weights = probs_full.astype(jnp.bfloat16)
        weighted = jnp.einsum(
            "hqk,khd->qhd", weights, value_all[key_low:upper], preferred_element_type=jnp.float32
        )
        results.append((weighted / jnp.transpose(denominator)[:, :, None]).astype(jnp.bfloat16))
    return jnp.concatenate(results, 0)


def attention_kernel(
    block_ref, query_ref, key_ref, rope_ref, value_ref, ids_col_ref, ids_row_ref, out_ref, bias_ref, *, block, window, doc_most, scale
):
    lower = block_ref[0] * block
    start = pl.multiple_of(jnp.maximum(lower - doc_most, 0), block)

    @pl.when(pl.program_id(0) == 0)
    def _():
        query_index = lower + lax.broadcasted_iota(jnp.int32, (block, window), 0)
        key_index = start + lax.broadcasted_iota(jnp.int32, (block, window), 1)
        allowed = (ids_col_ref[...] == ids_row_ref[:, pl.ds(start, window)]) & (
            query_index >= key_index
        )
        bias_ref[...] = jnp.where(allowed, 0.0, -jnp.inf).astype(jnp.float32)

    rope = rope_ref[pl.ds(start, window), :]
    dims = (((1,), (1,)), ((), ()))
    for head in range(query_ref.shape[0]):
        query = query_ref[head]
        keys = key_ref[head, pl.ds(start, window), :]
        values = value_ref[head, pl.ds(start, window), :]
        scores = lax.dot_general(query[:, :NOPE], keys, dims, preferred_element_type=jnp.float32)
        scores = scores + lax.dot_general(
            query[:, NOPE:], rope, dims, preferred_element_type=jnp.float32
        )
        scores = scores * scale + bias_ref[...]
        row_max = jnp.max(scores, -1, keepdims=True)
        probs = jnp.exp(scores - row_max)
        denominator = jnp.sum(probs, -1, keepdims=True)
        weighted = jnp.dot(probs.astype(jnp.bfloat16), values, preferred_element_type=jnp.float32)
        out_ref[head] = (weighted / denominator).astype(out_ref.dtype)


def block_attention(query, key_nope, key_rope, value, group_ids, score_scale, doc_most, block, index):
    heads, total_rows, _ = query.shape
    window = min(total_rows, doc_most + block)
    kernel = functools.partial(
        attention_kernel, block=block, window=window, doc_most=doc_most, scale=score_scale
    )
    flops = 2 * heads * block * window * (NOPE + ROPE + VDIM)
    step = heads
    return pl.pallas_call(
        kernel,
        grid_spec=pltpu.PrefetchScalarGridSpec(
            num_scalar_prefetch=1,
            grid=(heads // step,),
            in_specs=[
                pl.BlockSpec((step, block, NOPE + ROPE), lambda h, b: (h, b[0], 0)),
                pl.BlockSpec((step, total_rows, NOPE), lambda h, b: (h, 0, 0)),
                pl.BlockSpec((total_rows, ROPE), lambda h, b: (0, 0)),
                pl.BlockSpec((step, total_rows, VDIM), lambda h, b: (h, 0, 0)),
                pl.BlockSpec((block, 1), lambda h, b: (b[0], 0)),
                pl.BlockSpec((1, total_rows), lambda h, b: (0, 0)),
            ],
            out_specs=pl.BlockSpec((step, block, VDIM), lambda h, b: (h, 0, 0)),
            scratch_shapes=[pltpu.VMEM((block, window), jnp.float32)],
        ),
        out_shape=jax.ShapeDtypeStruct((heads, block, VDIM), jnp.bfloat16),
        cost_estimate=pl.CostEstimate(
            flops=flops,
            transcendentals=heads * block * window,
            bytes_accessed=2 * heads * (block * (NOPE + ROPE + VDIM) + window * (NOPE + VDIM)),
        ),
    )(
        jnp.reshape(index, (1,)).astype(jnp.int32),
        query,
        key_nope,
        key_rope,
        value,
        group_ids.reshape(total_rows, 1),
        group_ids.reshape(1, total_rows),
    )


def body(
    hidden_states,
    input_gain,
    query_down,
    memory_down,
    query_gain,
    memory_gain,
    query_up,
    key_up,
    value_up,
    segment_ids,
):
    tok_count = hidden_states.shape[0]
    seq_count = lax.axis_size("seq")
    tp_count = lax.axis_size("tp")
    seq_index = lax.axis_index("seq")
    tp_index = lax.axis_index("tp")
    width = hidden_states.shape[1] * tp_count
    total_rows = tok_count * seq_count
    doc_most = total_rows // 4
    qrank_piece = query_down.shape[1]
    memory_piece = memory_down.shape[1]
    qrank = qrank_piece * seq_count
    memory_cols = memory_piece * seq_count

    group_ids = lax.all_gather(segment_ids, "seq", axis=0, tiled=True)

    inputs = hidden_states.astype(jnp.float32)
    square_sums = lax.psum(jnp.sum(inputs * inputs, 1), "tp")
    normed = (inputs * lax.rsqrt(square_sums / width + epsilon)[:, None] * input_gain).astype(
        jnp.bfloat16
    )

    dp_index = lax.axis_index("dp")
    dp_count = lax.axis_size("dp")
    down_piece = jnp.concatenate([query_down, memory_down], 1)
    half_rows = down_piece.shape[0] // dp_count
    own_rows = lax.dynamic_slice_in_dim(down_piece, dp_index * half_rows, half_rows, 0)
    own_all = lax.all_gather(own_rows, "seq", axis=1, tiled=True)
    own_all, normed, group_ids = lax.optimization_barrier((own_all, normed, group_ids))
    partial = jnp.dot(
        lax.dynamic_slice_in_dim(normed, dp_index * half_rows, half_rows, 1),
        own_all,
        preferred_element_type=jnp.float32,
    )
    for shift in range(1, dp_count):
        peer = (dp_index + dp_count - shift) % dp_count
        peer_all = lax.ppermute(
            own_all, "dp", perm=[(i, (i + shift) % dp_count) for i in range(dp_count)]
        )
        partial = partial + jnp.dot(
            lax.dynamic_slice_in_dim(normed, peer * half_rows, half_rows, 1),
            peer_all,
            preferred_element_type=jnp.float32,
        )
    pieces = partial.reshape(tp_count, partial.shape[0] // tp_count, partial.shape[1])
    latent_rows = lax.dynamic_index_in_dim(pieces, tp_index, 0, keepdims=False)
    for k in range(1, tp_count):
        sent = lax.dynamic_index_in_dim(pieces, (tp_index + k) % tp_count, 0, keepdims=False)
        latent_rows = latent_rows + lax.ppermute(
            sent, "tp", perm=[(i, (i + k) % tp_count) for i in range(tp_count)]
        )

    token_index = jnp.arange(total_rows, dtype=jnp.int32)
    onehot = group_ids[:, None] == jnp.arange(DOCS, dtype=jnp.int32)[None, :]
    starts = jnp.min(jnp.where(onehot, token_index[:, None], total_rows), 0)
    position = token_index - jnp.sum(jnp.where(onehot, starts[None, :], 0), 1)
    chunk = latent_rows.shape[0]
    latent_rows = latent_rows.reshape(chunk, seq_count, qrank_piece + memory_piece)
    query_sums = latent_rows[:, :, :qrank_piece].reshape(chunk, qrank)
    memory_sums = latent_rows[:, :, qrank_piece:].reshape(chunk, memory_cols)
    chunk_position = lax.dynamic_slice(
        position, (seq_index * tok_count + tp_index * chunk,), (chunk,)
    )
    compressed_query = rms_scale(query_sums, query_gain).astype(jnp.bfloat16)
    compressed_memory = rms_scale(memory_sums[:, :KVRANK], memory_gain).astype(jnp.bfloat16)
    key_rope = rotate(memory_sums[:, KVRANK:], chunk_position).astype(jnp.bfloat16)
    packed = jnp.concatenate([compressed_query, compressed_memory, key_rope], 1)
    from_seq = [packed] + [
        lax.ppermute(packed, "seq", perm=[(i, (i + k) % seq_count) for i in range(seq_count)])
        for k in range(1, seq_count)
    ]
    packed = jnp.take(jnp.stack(from_seq), (seq_index - jnp.arange(seq_count)) % seq_count, axis=0)
    packed, query_up, key_up, value_up = lax.optimization_barrier(
        (packed, query_up, key_up, value_up)
    )
    packed = lax.all_gather(packed, "tp", axis=0, tiled=False)
    latent = jnp.transpose(packed, (1, 0, 2, 3)).reshape(total_rows, packed.shape[-1])
    cq_all = latent[:, :qrank]
    cm_all = latent[:, qrank : qrank + KVRANK]
    rope_all = latent[:, qrank + KVRANK :]

    local_heads = query_up.shape[1] // (NOPE + ROPE)
    heads = local_heads // seq_count

    def head_columns(weight, head_width):
        rows = weight.shape[0]
        cols = heads * head_width // dp_count
        own = lax.dynamic_slice_in_dim(
            weight.reshape(rows, seq_count, heads * head_width), dp_index * cols, cols, 2
        )
        own = lax.all_to_all(own, "seq", split_axis=1, concat_axis=0, tiled=True)
        own = own.reshape(rows * seq_count, cols)
        pieces = [own]
        for shift in range(1, dp_count):
            pieces.append(
                lax.ppermute(
                    own, "dp", perm=[(i, (i + shift) % dp_count) for i in range(dp_count)]
                )
            )
        ordered = []
        for core in range(dp_count):
            pick = pieces[0]
            for k in range(1, dp_count):
                pick = jnp.where((dp_index + dp_count - k) % dp_count == core, pieces[k], pick)
            ordered.append(pick)
        return jnp.concatenate(ordered, 1)

    query_w = head_columns(query_up, NOPE + ROPE)
    key_w = head_columns(key_up, NOPE)
    value_w = head_columns(value_up, VDIM)

    query_full = jnp.einsum(
        "td,dhe->hte",
        cq_all,
        query_w.reshape(qrank, heads, NOPE + ROPE),
        preferred_element_type=jnp.float32,
    )
    query = jnp.concatenate(
        [query_full[..., :NOPE], rotate(query_full[..., NOPE:], position[None, :])], -1
    ).astype(jnp.bfloat16)
    key_nope = jnp.einsum(
        "td,dhe->hte", cm_all, key_w.reshape(KVRANK, heads, NOPE), preferred_element_type=jnp.float32
    ).astype(jnp.bfloat16)
    value = jnp.einsum(
        "td,dhe->hte", cm_all, value_w.reshape(KVRANK, heads, VDIM), preferred_element_type=jnp.float32
    ).astype(jnp.bfloat16)
    score_scale = (NOPE + ROPE) ** (-0.5)
    received = [None] * seq_count
    shifts = [k for k in range(seq_count - 1, 0, -1) if k % 2]
    shifts = shifts + [k for k in range(seq_count - 1, 0, -1) if k % 2 == 0] + [0]
    for k in shifts:
        rows = block_attention(
            query, key_nope, rope_all, value, group_ids, score_scale, doc_most, tok_count,
            (seq_index + k) % seq_count,
        )
        if k:
            rows = lax.ppermute(
                rows, "seq", perm=[(i, (i + k) % seq_count) for i in range(seq_count)]
            )
        received[k] = rows
    attended = jnp.take(
        jnp.stack(received), (seq_index - jnp.arange(seq_count)) % seq_count, axis=0
    )
    attended = jnp.transpose(attended, (2, 0, 1, 3))
    return attended.reshape(tok_count, local_heads * VDIM)


def solution(mesh):
    in_specs = (
        P(("dp", "seq"), "tp"),
        P("tp"),
        P("tp", "seq"),
        P("tp", "seq"),
        P(),
        P(),
        P("seq", "tp"),
        P("seq", "tp"),
        P("seq", "tp"),
        P(("dp", "seq")),
    )
    out_specs = P(("dp", "seq"), "tp")
    return jax.shard_map(body, mesh=mesh, in_specs=in_specs, out_specs=out_specs, check_vma=False)
```
